512 devices in a mesh: gx: 32 (over y, x_hi, core), gy: 8 (over z), gz: 2 (over x_lo).
Axes of the slice: x: 4 (x_hi: 2, x_lo: 2; x = x_hi * 2 + x_lo), y: 8, z: 8, core: 2. Of those that a mesh axis runs over, the one named last changes fastest.
Arguments:
- velocity: float32 [3, 4, 256, 3072], P(None, 'gz', 'gx', 'gy'), may hold values from -6 to 6
- adjoint: float32 [3, 4, 256, 3072], P(None, 'gz', 'gx', 'gy'), may hold values from -0.3 to 0.3
- viscosity: float32 [4, 256, 3072], P('gz', 'gx', 'gy'), may hold values from 0.5 to 5
- hang_flags: int32 [256, 1024], P('gx', 'gy'), may hold values 0 or 1
- hang_index: int32 [256, 1024], P('gx', 'gy'), may hold values from 0 to 7
- block_table: float32 [8, 3, 3], replicated, may hold values from -0.5 to 1
- friction: float32 [256, 3072], P('gx', ('gy', 'gz')), may hold values from -3 to 3
- basal_mask: int32 [256, 3072], P('gx', ('gy', 'gz')), may hold values 0 or 1
- direction: float32 [256, 3072], P('gx', ('gy', 'gz')), may hold values from -6 to 6
Outputs:
- stokes_image: float32 [3, 4, 256, 3072], P(None, 'gz', 'gx', 'gy')
- hessian_dir: float32 [256, 3072], P('gx', ('gy', 'gz'))
The draws below stay inside these ranges and needn't reach their ends.
All inputs are finite; a program needn't handle non-finite values. No bound on the sum of `hang_flags` or of `basal_mask` on one device may be relied on, other than what follows from the above.
Results may differ from the reference program's by a relative error of at most 0.00025.
Values sent between devices are 32-bit elements; how exact they have to be, the bound alone decides.
No kernel may reach another device: no remote copies, remote signals or barrier semaphores. Data moves between devices by JAX's collectives and lax.ppermute only.
A program may use at most 64 MiB of HBM per device.

```python
import math
import jax
import jax.numpy as jnp
from jax import lax

CY = 384
NB = 8
NX = 256
NY = 3072
NZ = 4
N_GY = 8


def set_ends(drawn, own_key, low, largest):
    shape = drawn.shape
    spot = [jax.random.randint(jax.random.fold_in(own_key, axis), (), 0, shape[axis]) for axis in range(len(shape))]
    drawn = drawn.at[tuple(spot)].set(low)
    longest = shape.index(max(shape))
    spot[longest] = (spot[longest] + 1) % shape[longest]
    return drawn.at[tuple(spot)].set(largest)


def level_of(key, shape, cuts, least, largest):
    factor_of, own = 1.0, jax.random.fold_in(key, 6)
    for axis_at, shards_of in cuts:
        draws = jnp.exp(jax.random.uniform(jax.random.fold_in(own, axis_at), (shards_of,), jnp.float32, least / len(cuts), largest / len(cuts)))
        factor_of = factor_of * jnp.repeat(draws, shape[axis_at] // shards_of).reshape([-1 if axis == axis_at else 1 for axis in range(len(shape))])
    return factor_of


def gaussian(stream_key, extent, spread, most, pieces=(), kind=jnp.bfloat16):
    values = spread * jax.random.normal(stream_key, extent, jnp.float32)
    if pieces:
        values = values * level_of(stream_key, extent, pieces, -0.22, 0.18)
    return jnp.clip(values, -most, most).astype(kind)


def setup_inputs(seed: int = 0) -> dict:
    keys = jax.random.split(jax.random.key(seed), 10)
    return {
        "velocity": gaussian(keys[0], (3, NZ, NX, NY), 1.0, 6.0, ((1, 2), (2, 32), (3, 8)), jnp.float32),
        "adjoint": gaussian(keys[1], (3, NZ, NX, NY), 0.05, 0.3, ((1, 2), (2, 32), (3, 8)), jnp.float32),
        "viscosity": jnp.clip(jnp.exp(math.log(5.0) - 2.3025851 * jax.random.uniform(keys[2], (NZ, NX, NY), jnp.float32) ** level_of(keys[2], (NZ, NX, NY), ((0, 2), (1, 32), (2, 8)), -0.2, 0.2)), 0.5, 5.0),
        "hang_flags": set_ends((jax.random.randint(keys[3], (NX, NY // 3), 0, 4) < 1).astype(jnp.int32), jax.random.fold_in(keys[3], 1), 0, 1),
        "hang_index": set_ends(jax.random.randint(keys[4], (NX, NY // 3), 0, NB), jax.random.fold_in(keys[4], 1), 0, NB - 1).astype(jnp.int32),
        "block_table": jnp.clip(jax.random.uniform(keys[5], (NB, 3, 3), jnp.float32, -0.5, 1.0), -0.5, 1.0),
        "friction": gaussian(keys[6], (NX, NY), 0.5, 3.0, ((0, 32), (1, 16)), jnp.float32),
        "basal_mask": set_ends((jax.random.randint(keys[7], (NX, NY), 0, 4) < 3).astype(jnp.int32), jax.random.fold_in(keys[7], 1), 0, 1),
        "direction": gaussian(keys[8], (NX, NY), 1.0, 6.0, ((0, 32), (1, 16)), jnp.float32),
    }


reg_weight = 0.05


def block_matrices(hang_flags, hang_index, block_table):
    groups = CY // 3
    one_hot = (hang_index.reshape(NX, N_GY, groups)[..., None] == jnp.arange(NB, dtype=jnp.int32)).astype(jnp.float32)
    blocks = jnp.einsum('xhgn,nmk->mkxhg', one_hot, block_table.astype(jnp.float32), precision=lax.Precision.HIGHEST)
    hanging = hang_flags.reshape(NX, N_GY, groups).astype(jnp.float32)
    identity = jnp.eye(3, dtype=jnp.float32)[:, :, None, None, None]
    return hanging * blocks + (1.0 - hanging) * identity


def apply_blocks(local_blocks, field, transpose):
    groups = CY // 3
    levels = field.shape[1]
    shaped = field.reshape(3, levels, NX, N_GY, 3, groups)
    if transpose:
        mixed = jnp.einsum('mkxhg,czxhmg->czxhkg', local_blocks, shaped, precision=lax.Precision.HIGHEST)
    else:
        mixed = jnp.einsum('mkxhg,czxhkg->czxhmg', local_blocks, shaped, precision=lax.Precision.HIGHEST)
    return mixed.reshape(field.shape)


def shifted(padded, spatial, offset):
    lead = padded.ndim - 3
    index = [slice(None)] * lead + [slice(1, -1)] * 3
    if offset == 1:
        index[lead + spatial] = slice(2, None)
    elif offset == -1:
        index[lead + spatial] = slice(None, -2)
    return padded[tuple(index)]


def stencil(padded_vel, padded_visc):
    centre_vel = shifted(padded_vel, 0, 0)
    centre_visc = shifted(padded_visc, 0, 0)
    total = jnp.zeros(centre_vel.shape, jnp.float32)
    for spatial in range(3):
        for offset in (1, -1):
            face = 0.5 * (centre_visc + shifted(padded_visc, spatial, offset))
            total = total + face[None] * (centre_vel - shifted(padded_vel, spatial, offset))
    return total


def laplace(padded):
    return 4.0 * padded[1:-1, 1:-1] - padded[2:, 1:-1] - padded[:-2, 1:-1] - padded[1:-1, 2:] - padded[1:-1, :-2]


def reference(velocity, adjoint, viscosity, hang_flags, hang_index, block_table, friction, basal_mask, direction):
    local_blocks = block_matrices(hang_flags, hang_index, block_table)
    constrained = apply_blocks(local_blocks, velocity, False)
    padded_vel = jnp.pad(constrained, ((0, 0), (1, 1), (1, 1), (1, 1)))
    padded_visc = jnp.pad(viscosity, 1)
    applied = stencil(padded_vel, padded_visc)
    stokes_image = apply_blocks(local_blocks, applied, True)
    column_sums = jnp.sum(stokes_image * adjoint, axis=(0, 1))
    bilaplace = laplace(jnp.pad(laplace(jnp.pad(direction, 1)), 1))
    hessian_dir = reg_weight * bilaplace + basal_mask.astype(jnp.float32) * (jnp.exp(friction) * column_sums)
    return stokes_image, hessian_dir
```

```python
import jax
import jax.numpy as jnp
from jax import lax
from jax.sharding import PartitionSpec as P

NB = 8


reg_weight = 0.05


def shift_pairs(count, step):
    if step > 0:
        return [(i, i + 1) for i in range(count - 1)]
    return [(i + 1, i) for i in range(count - 1)]


def block_matrices(hang_flags, hang_index, block_table):
    hanging = hang_flags != 0
    rows = []
    for m in range(3):
        row = []
        for k in range(3):
            entry = jnp.full(hang_index.shape, block_table[0, m, k], jnp.float32)
            for number in range(1, NB):
                entry = jnp.where(hang_index == number, block_table[number, m, k], entry)
            row.append(jnp.where(hanging, entry, 1.0 if m == k else 0.0))
        rows.append(row)
    return rows


def apply_blocks(blocks, field, transpose):
    groups = field.shape[-1] // 3
    slots = [field[..., k * groups:(k + 1) * groups] for k in range(3)]
    mixed = []
    for m in range(3):
        total = None
        for k in range(3):
            weight = blocks[k][m] if transpose else blocks[m][k]
            term = weight * slots[k]
            total = term if total is None else total + term
        mixed.append(total)
    return jnp.concatenate(mixed, axis=-1)


def shifted(padded, spatial, offset):
    lead = padded.ndim - 3
    index = [slice(None)] * lead + [slice(1, -1)] * 3
    if offset == 1:
        index[lead + spatial] = slice(2, None)
    elif offset == -1:
        index[lead + spatial] = slice(None, -2)
    return padded[tuple(index)]


def stencil(padded_vel, padded_visc):
    centre_vel = shifted(padded_vel, 0, 0)
    centre_visc = shifted(padded_visc, 0, 0)
    total = jnp.zeros(centre_vel.shape, jnp.float32)
    for spatial in range(3):
        for offset in (1, -1):
            face = 0.5 * (centre_visc + shifted(padded_visc, spatial, offset))
            total = total + face[None] * (centre_vel - shifted(padded_vel, spatial, offset))
    return total


def laplace(padded):
    return (
        4.0 * padded[1:-1, 1:-1]
        - padded[2:, 1:-1]
        - padded[:-2, 1:-1]
        - padded[1:-1, 2:]
        - padded[1:-1, :-2]
    )


def local(
    velocity,
    adjoint,
    viscosity,
    hang_flags,
    hang_index,
    block_table,
    friction,
    basal_mask,
    direction,
):
    n_x = lax.axis_size("gx")
    n_y = lax.axis_size("gy")
    n_z = lax.axis_size("gz")
    i_x = lax.axis_index("gx")
    i_z = lax.axis_index("gz")
    n_col = n_y * n_z
    i_col = lax.axis_index("gy") * n_z + i_z

    blocks = block_matrices(hang_flags, hang_index, block_table)
    constrained = apply_blocks(blocks, velocity, False)
    stacked = jnp.concatenate([constrained, viscosity[None]], axis=0)
    fields, levels, rows, cols = stacked.shape
    d_rows, d_cols = direction.shape

    def x_packet(stack_row, dir_rows):
        return jnp.concatenate(
            [stack_row.reshape(fields * levels, cols), dir_rows.reshape(1, cols)], axis=0
        )

    from_left = lax.ppermute(
        x_packet(stacked[:, :, rows - 1], direction[d_rows - 2:]), "gx", shift_pairs(n_x, 1)
    )
    from_right = lax.ppermute(
        x_packet(stacked[:, :, 0], direction[:2]), "gx", shift_pairs(n_x, -1)
    )
    y_left = lax.ppermute(stacked[:, :, :, cols - 1:], "gy", shift_pairs(n_y, 1))
    y_right = lax.ppermute(stacked[:, :, :, :1], "gy", shift_pairs(n_y, -1))
    if n_z == 2:
        sent = lax.dynamic_slice_in_dim(stacked, (1 - i_z) * (levels - 1), 1, axis=1)
        got = lax.ppermute(sent, "gz", [(0, 1), (1, 0)])
        zero = jnp.zeros_like(got)
        z_low = jnp.where(i_z == 1, got, zero)
        z_high = jnp.where(i_z == 0, got, zero)
    else:
        z_low = lax.ppermute(stacked[:, levels - 1:], "gz", shift_pairs(n_z, 1))
        z_high = lax.ppermute(stacked[:, :1], "gz", shift_pairs(n_z, -1))

    x_low = from_left[: fields * levels].reshape(fields, levels, 1, cols)
    x_high = from_right[: fields * levels].reshape(fields, levels, 1, cols)
    d_low = from_left[fields * levels:].reshape(2, d_cols)
    d_high = from_right[fields * levels:].reshape(2, d_cols)

    d_ext = jnp.concatenate([d_low, direction, d_high], axis=0)
    d_left = lax.ppermute(d_ext[:, d_cols - 2:], ("gy", "gz"), shift_pairs(n_col, 1))
    d_right = lax.ppermute(d_ext[:, :2], ("gy", "gz"), shift_pairs(n_col, -1))

    padded = jnp.concatenate([y_left, stacked, y_right], axis=3)
    pad_y = ((0, 0), (0, 0), (0, 0), (1, 1))
    padded = jnp.concatenate(
        [jnp.pad(x_low, pad_y), padded, jnp.pad(x_high, pad_y)], axis=2
    )
    pad_xy = ((0, 0), (0, 0), (1, 1), (1, 1))
    padded = jnp.concatenate(
        [jnp.pad(z_low, pad_xy), padded, jnp.pad(z_high, pad_xy)], axis=1
    )
    applied = stencil(padded[:3], padded[3])
    stokes_image = apply_blocks(blocks, applied, True)
    partial_value = jnp.sum(stokes_image * adjoint, axis=(0, 1))

    own_width = cols // n_z
    if n_z == 2:
        sent = lax.dynamic_slice_in_dim(partial_value, (1 - i_z) * own_width, own_width, axis=1)
        mine = lax.dynamic_slice_in_dim(partial_value, i_z * own_width, own_width, axis=1)
        column = mine + lax.ppermute(sent, "gz", [(0, 1), (1, 0)])
    else:
        column = lax.psum_scatter(partial_value, "gz", scatter_dimension=1, tiled=True)

    d_full = jnp.concatenate([d_left, d_ext, d_right], axis=1)
    inner = laplace(d_full)
    row_ids = lax.broadcasted_iota(jnp.int32, inner.shape, 0)
    col_ids = lax.broadcasted_iota(jnp.int32, inner.shape, 1)
    outside = (
        ((row_ids == 0) & (i_x == 0))
        | ((row_ids == inner.shape[0] - 1) & (i_x == n_x - 1))
        | ((col_ids == 0) & (i_col == 0))
        | ((col_ids == inner.shape[1] - 1) & (i_col == n_col - 1))
    )
    inner = jnp.where(outside, 0.0, inner)
    bilaplace = laplace(inner)
    hessian_dir = reg_weight * bilaplace + basal_mask.astype(jnp.float32) * (
        jnp.exp(friction) * column
    )
    return (stokes_image, hessian_dir)


def solution(mesh):
    return jax.shard_map(
        local,
        mesh=mesh,
        in_specs=(
            P(None, "gz", "gx", "gy"),
            P(None, "gz", "gx", "gy"),
            P("gz", "gx", "gy"),
            P("gx", "gy"),
            P("gx", "gy"),
            P(),
            P("gx", ("gy", "gz")),
            P("gx", ("gy", "gz")),
            P("gx", ("gy", "gz")),
        ),
        out_specs=(P(None, "gz", "gx", "gy"), P("gx", ("gy", "gz"))),
        check_vma=False,
    )
```

```python
import jax
import jax.numpy as jnp
from jax import lax
from jax.sharding import PartitionSpec as P


reg_weight = 0.05


def shift_pairs(count, step):
    if step > 0:
        return [(i, i + 1) for i in range(count - 1)]
    return [(i + 1, i) for i in range(count - 1)]


def block_matrices(hang_flags, hang_index, block_table):
    count = block_table.shape[0]
    numbers = lax.broadcasted_iota(jnp.int32, (count,) + hang_index.shape, 0)
    one_hot = (hang_index[None] == numbers).astype(jnp.float32)
    table = block_table.astype(jnp.float32).reshape(count, 9)
    chosen = lax.dot_general(
        table, one_hot, (((0,), (0,)), ((), ())), precision=lax.Precision.HIGHEST
    )
    identity = jnp.eye(3, dtype=jnp.float32).reshape(9)[:, None, None]
    blocks = jnp.where(hang_flags[None] != 0, chosen, identity)
    return [[blocks[m * 3 + k] for k in range(3)] for m in range(3)]


def apply_blocks(blocks, field, transpose):
    groups = field.shape[-1] // 3
    slots = [field[..., k * groups:(k + 1) * groups] for k in range(3)]
    mixed = []
    for m in range(3):
        total = None
        for k in range(3):
            weight = blocks[k][m] if transpose else blocks[m][k]
            term = weight * slots[k]
            total = term if total is None else total + term
        mixed.append(total)
    return jnp.concatenate(mixed, axis=-1)


def shifted(padded, spatial, offset):
    lead = padded.ndim - 3
    index = [slice(None)] * lead + [slice(1, -1)] * 3
    if offset == 1:
        index[lead + spatial] = slice(2, None)
    elif offset == -1:
        index[lead + spatial] = slice(None, -2)
    return padded[tuple(index)]


def stencil(padded_vel, padded_visc):
    centre_vel = shifted(padded_vel, 0, 0)
    centre_visc = shifted(padded_visc, 0, 0)
    total = jnp.zeros(centre_vel.shape, jnp.float32)
    for spatial in range(3):
        for offset in (1, -1):
            face = 0.5 * (centre_visc + shifted(padded_visc, spatial, offset))
            total = total + face[None] * (centre_vel - shifted(padded_vel, spatial, offset))
    return total


def laplace(padded):
    return (
        4.0 * padded[1:-1, 1:-1]
        - padded[2:, 1:-1]
        - padded[:-2, 1:-1]
        - padded[1:-1, 2:]
        - padded[1:-1, :-2]
    )


def local(
    velocity,
    adjoint,
    viscosity,
    hang_flags,
    hang_index,
    block_table,
    friction,
    basal_mask,
    direction,
):
    n_x = lax.axis_size("gx")
    n_y = lax.axis_size("gy")
    n_z = lax.axis_size("gz")
    i_x = lax.axis_index("gx")
    i_z = lax.axis_index("gz")
    n_col = n_y * n_z
    i_col = lax.axis_index("gy") * n_z + i_z

    blocks = block_matrices(hang_flags, hang_index, block_table)
    constrained = apply_blocks(blocks, velocity, False)
    stacked = jnp.concatenate([constrained, viscosity[None]], axis=0)
    fields, levels, rows, cols = stacked.shape
    d_rows, d_cols = direction.shape

    def x_packet(stack_row, dir_rows):
        return jnp.concatenate(
            [stack_row.reshape(fields * levels, cols), dir_rows.reshape(1, cols)], axis=0
        )

    from_left = lax.ppermute(
        x_packet(stacked[:, :, rows - 1], direction[d_rows - 2:]), "gx", shift_pairs(n_x, 1)
    )
    from_right = lax.ppermute(
        x_packet(stacked[:, :, 0], direction[:2]), "gx", shift_pairs(n_x, -1)
    )
    y_left = lax.ppermute(stacked[:, :, :, cols - 1:], "gy", shift_pairs(n_y, 1))
    y_right = lax.ppermute(stacked[:, :, :, :1], "gy", shift_pairs(n_y, -1))
    if n_z == 2:
        sent = lax.dynamic_slice_in_dim(stacked, (1 - i_z) * (levels - 1), 1, axis=1)
        got = lax.ppermute(sent, "gz", [(0, 1), (1, 0)])
        zero = jnp.zeros_like(got)
        z_low = jnp.where(i_z == 1, got, zero)
        z_high = jnp.where(i_z == 0, got, zero)
    else:
        z_low = lax.ppermute(stacked[:, levels - 1:], "gz", shift_pairs(n_z, 1))
        z_high = lax.ppermute(stacked[:, :1], "gz", shift_pairs(n_z, -1))

    x_low = from_left[: fields * levels].reshape(fields, levels, 1, cols)
    x_high = from_right[: fields * levels].reshape(fields, levels, 1, cols)
    d_low = from_left[fields * levels:].reshape(2, d_cols)
    d_high = from_right[fields * levels:].reshape(2, d_cols)

    d_ext = jnp.concatenate([d_low, direction, d_high], axis=0)
    d_left = lax.ppermute(d_ext[:, d_cols - 2:], ("gy", "gz"), shift_pairs(n_col, 1))
    d_right = lax.ppermute(d_ext[:, :2], ("gy", "gz"), shift_pairs(n_col, -1))

    padded = jnp.concatenate([y_left, stacked, y_right], axis=3)
    pad_y = ((0, 0), (0, 0), (0, 0), (1, 1))
    padded = jnp.concatenate(
        [jnp.pad(x_low, pad_y), padded, jnp.pad(x_high, pad_y)], axis=2
    )
    pad_xy = ((0, 0), (0, 0), (1, 1), (1, 1))
    padded = jnp.concatenate(
        [jnp.pad(z_low, pad_xy), padded, jnp.pad(z_high, pad_xy)], axis=1
    )
    applied = stencil(padded[:3], padded[3])
    stokes_image = apply_blocks(blocks, applied, True)
    partial_value = jnp.sum(stokes_image * adjoint, axis=(0, 1))

    own_width = cols // n_z
    if n_z == 2:
        sent = lax.dynamic_slice_in_dim(partial_value, (1 - i_z) * own_width, own_width, axis=1)
        mine = lax.dynamic_slice_in_dim(partial_value, i_z * own_width, own_width, axis=1)
        column = mine + lax.ppermute(sent, "gz", [(0, 1), (1, 0)])
    else:
        column = lax.psum_scatter(partial_value, "gz", scatter_dimension=1, tiled=True)

    d_full = jnp.concatenate([d_left, d_ext, d_right], axis=1)
    inner = laplace(d_full)
    row_ids = lax.broadcasted_iota(jnp.int32, inner.shape, 0)
    col_ids = lax.broadcasted_iota(jnp.int32, inner.shape, 1)
    outside = (
        ((row_ids == 0) & (i_x == 0))
        | ((row_ids == inner.shape[0] - 1) & (i_x == n_x - 1))
        | ((col_ids == 0) & (i_col == 0))
        | ((col_ids == inner.shape[1] - 1) & (i_col == n_col - 1))
    )
    inner = jnp.where(outside, 0.0, inner)
    bilaplace = laplace(inner)
    hessian_dir = reg_weight * bilaplace + basal_mask.astype(jnp.float32) * (
        jnp.exp(friction) * column
    )
    return (stokes_image, hessian_dir)


def solution(mesh):
    return jax.shard_map(
        local,
        mesh=mesh,
        in_specs=(
            P(None, "gz", "gx", "gy"),
            P(None, "gz", "gx", "gy"),
            P("gz", "gx", "gy"),
            P("gx", "gy"),
            P("gx", "gy"),
            P(),
            P("gx", ("gy", "gz")),
            P("gx", ("gy", "gz")),
            P("gx", ("gy", "gz")),
        ),
        out_specs=(P(None, "gz", "gx", "gy"), P("gx", ("gy", "gz"))),
        check_vma=False,
    )
```

```python
import jax
import jax.numpy as jnp
from jax import lax
from jax.sharding import PartitionSpec as P


reg_weight = 0.05


def shift_pairs(count, step):
    if step > 0:
        return [(i, i + 1) for i in range(count - 1)]
    return [(i + 1, i) for i in range(count - 1)]


def block_matrices(hang_flags, hang_index, block_table):
    count = block_table.shape[0]
    numbers = lax.broadcasted_iota(jnp.int32, (count,) + hang_index.shape, 0)
    one_hot = (hang_index[None] == numbers).astype(jnp.float32)
    table = block_table.astype(jnp.float32).reshape(count, 9)
    chosen = lax.dot_general(
        table, one_hot, (((0,), (0,)), ((), ())), precision=lax.Precision.HIGHEST
    )
    identity = jnp.eye(3, dtype=jnp.float32).reshape(9)[:, None, None]
    blocks = jnp.where(hang_flags[None] != 0, chosen, identity)
    return [[blocks[m * 3 + k] for k in range(3)] for m in range(3)]


def apply_blocks(blocks, field, transpose):
    groups = field.shape[-1] // 3
    slots = [field[..., k * groups:(k + 1) * groups] for k in range(3)]
    mixed = []
    for m in range(3):
        total = None
        for k in range(3):
            weight = blocks[k][m] if transpose else blocks[m][k]
            term = weight * slots[k]
            total = term if total is None else total + term
        mixed.append(total)
    return jnp.concatenate(mixed, axis=-1)


def shifted(padded, spatial, offset):
    lead = padded.ndim - 3
    index = [slice(None)] * lead + [slice(1, -1)] * 3
    if offset == 1:
        index[lead + spatial] = slice(2, None)
    elif offset == -1:
        index[lead + spatial] = slice(None, -2)
    return padded[tuple(index)]


def stencil(padded_vel, padded_visc):
    centre_vel = shifted(padded_vel, 0, 0)
    centre_visc = shifted(padded_visc, 0, 0)
    total = jnp.zeros(centre_vel.shape, jnp.float32)
    for spatial in range(3):
        for offset in (1, -1):
            face = 0.5 * (centre_visc + shifted(padded_visc, spatial, offset))
            total = total + face[None] * (centre_vel - shifted(padded_vel, spatial, offset))
    return total


def laplace(padded):
    return (
        4.0 * padded[1:-1, 1:-1]
        - padded[2:, 1:-1]
        - padded[:-2, 1:-1]
        - padded[1:-1, 2:]
        - padded[1:-1, :-2]
    )


def local(
    velocity,
    adjoint,
    viscosity,
    hang_flags,
    hang_index,
    block_table,
    friction,
    basal_mask,
    direction,
):
    n_x = lax.axis_size("gx")
    n_y = lax.axis_size("gy")
    n_z = lax.axis_size("gz")
    i_x = lax.axis_index("gx")
    i_z = lax.axis_index("gz")
    n_col = n_y * n_z
    i_col = lax.axis_index("gy") * n_z + i_z

    blocks = block_matrices(hang_flags, hang_index, block_table)
    constrained = apply_blocks(blocks, velocity, False)
    stacked = jnp.concatenate([constrained, viscosity[None]], axis=0)
    fields, levels, rows, cols = stacked.shape
    d_rows, d_cols = direction.shape

    def x_packet(stack_row, dir_rows):
        return jnp.concatenate(
            [stack_row.reshape(fields * levels, cols), dir_rows.reshape(1, cols)], axis=0
        )

    from_left = lax.ppermute(
        x_packet(stacked[:, :, rows - 1], direction[d_rows - 2:]), "gx", shift_pairs(n_x, 1)
    )
    from_right = lax.ppermute(
        x_packet(stacked[:, :, 0], direction[:2]), "gx", shift_pairs(n_x, -1)
    )
    y_left = lax.ppermute(stacked[:, :, :, cols - 1:], "gy", shift_pairs(n_y, 1))
    y_right = lax.ppermute(stacked[:, :, :, :1], "gy", shift_pairs(n_y, -1))
    if n_z == 2:
        sent = lax.dynamic_slice_in_dim(stacked, (1 - i_z) * (levels - 1), 1, axis=1)
        got = lax.ppermute(sent, "gz", [(0, 1), (1, 0)])
        zero = jnp.zeros_like(got)
        z_low = jnp.where(i_z == 1, got, zero)
        z_high = jnp.where(i_z == 0, got, zero)
    else:
        z_low = lax.ppermute(stacked[:, levels - 1:], "gz", shift_pairs(n_z, 1))
        z_high = lax.ppermute(stacked[:, :1], "gz", shift_pairs(n_z, -1))

    x_low = from_left[: fields * levels].reshape(fields, levels, 1, cols)
    x_high = from_right[: fields * levels].reshape(fields, levels, 1, cols)
    d_low = from_left[fields * levels:].reshape(2, d_cols)
    d_high = from_right[fields * levels:].reshape(2, d_cols)

    d_ext = jnp.concatenate([d_low, direction, d_high], axis=0)
    padded = jnp.concatenate([y_left, stacked, y_right], axis=3)
    pad_y = ((0, 0), (0, 0), (0, 0), (1, 1))
    padded = jnp.concatenate(
        [jnp.pad(x_low, pad_y), padded, jnp.pad(x_high, pad_y)], axis=2
    )
    pad_xy = ((0, 0), (0, 0), (1, 1), (1, 1))
    padded = jnp.concatenate(
        [jnp.pad(z_low, pad_xy), padded, jnp.pad(z_high, pad_xy)], axis=1
    )
    applied = stencil(padded[:3], padded[3])
    stokes_image = apply_blocks(blocks, applied, True)
    partial_value = jnp.sum(stokes_image * adjoint, axis=(0, 1))

    own_width = cols // n_z
    if n_z == 2:
        sent = lax.dynamic_slice_in_dim(partial_value, (1 - i_z) * own_width, own_width, axis=1)
        mine = lax.dynamic_slice_in_dim(partial_value, i_z * own_width, own_width, axis=1)
        d_partner = lax.dynamic_slice_in_dim(d_ext, (1 - i_z) * (d_cols - 2), 2, axis=1)
        d_across = lax.dynamic_slice_in_dim(d_ext, i_z * (d_cols - 2), 2, axis=1)
        flat = d_partner.reshape(1, -1)
        packet = jnp.concatenate(
            [sent, jnp.pad(flat, ((0, 0), (0, own_width - flat.shape[1])))], axis=0
        )
        packet, d_across = lax.optimization_barrier((packet, d_across))
        got = lax.ppermute(packet, "gz", [(0, 1), (1, 0)])
        across_pairs = []
        for block in range(n_y - 1):
            across_pairs += [(2 * block + 1, 2 * block + 2), (2 * block + 2, 2 * block + 1)]
        got_across = lax.ppermute(d_across, ("gy", "gz"), across_pairs)
        column = mine + got[: sent.shape[0]]
        got_partner = got[sent.shape[0], : flat.shape[1]].reshape(d_partner.shape)
        d_left = jnp.where(i_z == 0, got_across, got_partner)
        d_right = jnp.where(i_z == 0, got_partner, got_across)
    else:
        column = lax.psum_scatter(partial_value, "gz", scatter_dimension=1, tiled=True)
        d_left = lax.ppermute(d_ext[:, d_cols - 2:], ("gy", "gz"), shift_pairs(n_col, 1))
        d_right = lax.ppermute(d_ext[:, :2], ("gy", "gz"), shift_pairs(n_col, -1))

    d_full = jnp.concatenate([d_left, d_ext, d_right], axis=1)
    inner = laplace(d_full)
    row_ids = lax.broadcasted_iota(jnp.int32, inner.shape, 0)
    col_ids = lax.broadcasted_iota(jnp.int32, inner.shape, 1)
    outside = (
        ((row_ids == 0) & (i_x == 0))
        | ((row_ids == inner.shape[0] - 1) & (i_x == n_x - 1))
        | ((col_ids == 0) & (i_col == 0))
        | ((col_ids == inner.shape[1] - 1) & (i_col == n_col - 1))
    )
    inner = jnp.where(outside, 0.0, inner)
    bilaplace = laplace(inner)
    hessian_dir = reg_weight * bilaplace + basal_mask.astype(jnp.float32) * (
        jnp.exp(friction) * column
    )
    return (stokes_image, hessian_dir)


def solution(mesh):
    return jax.shard_map(
        local,
        mesh=mesh,
        in_specs=(
            P(None, "gz", "gx", "gy"),
            P(None, "gz", "gx", "gy"),
            P("gz", "gx", "gy"),
            P("gx", "gy"),
            P("gx", "gy"),
            P(),
            P("gx", ("gy", "gz")),
            P("gx", ("gy", "gz")),
            P("gx", ("gy", "gz")),
        ),
        out_specs=(P(None, "gz", "gx", "gy"), P("gx", ("gy", "gz"))),
        check_vma=False,
    )
```

```python
import jax
import jax.numpy as jnp
from jax import lax
from jax.sharding import PartitionSpec as P


reg_weight = 0.05


def shift_pairs(count, step):
    if step > 0:
        return [(i, i + 1) for i in range(count - 1)]
    return [(i + 1, i) for i in range(count - 1)]


def neighbour_swaps(low_edge, high_edge, axis, index, count):
    even = index % 2 == 0
    pairs_a = [(i, i ^ 1) for i in range(count - count % 2)]
    pairs_b = []
    for k in range(1, count - 1, 2):
        pairs_b += [(k, k + 1), (k + 1, k)]
    got_a = lax.ppermute(jnp.where(even, high_edge, low_edge), axis, pairs_a)
    got_b = lax.ppermute(jnp.where(even, low_edge, high_edge), axis, pairs_b)
    from_below = jnp.where(even, got_b, got_a)
    from_above = jnp.where(even, got_a, got_b)
    return from_below, from_above


def block_matrices(hang_flags, hang_index, block_table):
    count = block_table.shape[0]
    numbers = lax.broadcasted_iota(jnp.int32, (count,) + hang_index.shape, 0)
    one_hot = (hang_index[None] == numbers).astype(jnp.float32)
    table = block_table.astype(jnp.float32).reshape(count, 9)
    chosen = lax.dot_general(
        table, one_hot, (((0,), (0,)), ((), ())), precision=lax.Precision.HIGHEST
    )
    identity = jnp.eye(3, dtype=jnp.float32).reshape(9)[:, None, None]
    blocks = jnp.where(hang_flags[None] != 0, chosen, identity)
    return [[blocks[m * 3 + k] for k in range(3)] for m in range(3)]


def apply_blocks(blocks, field, transpose):
    groups = field.shape[-1] // 3
    slots = [field[..., k * groups:(k + 1) * groups] for k in range(3)]
    mixed = []
    for m in range(3):
        total = None
        for k in range(3):
            weight = blocks[k][m] if transpose else blocks[m][k]
            term = weight * slots[k]
            total = term if total is None else total + term
        mixed.append(total)
    return jnp.concatenate(mixed, axis=-1)


def shifted(padded, spatial, offset):
    lead = padded.ndim - 3
    index = [slice(None)] * lead + [slice(1, -1)] * 3
    if offset == 1:
        index[lead + spatial] = slice(2, None)
    elif offset == -1:
        index[lead + spatial] = slice(None, -2)
    return padded[tuple(index)]


def stencil(padded_vel, padded_visc):
    centre_vel = shifted(padded_vel, 0, 0)
    centre_visc = shifted(padded_visc, 0, 0)
    total = jnp.zeros(centre_vel.shape, jnp.float32)
    for spatial in range(3):
        for offset in (1, -1):
            face = 0.5 * (centre_visc + shifted(padded_visc, spatial, offset))
            total = total + face[None] * (centre_vel - shifted(padded_vel, spatial, offset))
    return total


def laplace(padded):
    return (
        4.0 * padded[1:-1, 1:-1]
        - padded[2:, 1:-1]
        - padded[:-2, 1:-1]
        - padded[1:-1, 2:]
        - padded[1:-1, :-2]
    )


def local(
    velocity,
    adjoint,
    viscosity,
    hang_flags,
    hang_index,
    block_table,
    friction,
    basal_mask,
    direction,
):
    n_x = lax.axis_size("gx")
    n_y = lax.axis_size("gy")
    n_z = lax.axis_size("gz")
    i_x = lax.axis_index("gx")
    i_z = lax.axis_index("gz")
    n_col = n_y * n_z
    i_col = lax.axis_index("gy") * n_z + i_z

    blocks = block_matrices(hang_flags, hang_index, block_table)
    constrained = apply_blocks(blocks, velocity, False)
    stacked = jnp.concatenate([constrained, viscosity[None]], axis=0)
    fields, levels, rows, cols = stacked.shape
    d_rows, d_cols = direction.shape

    def x_packet(stack_row, dir_rows):
        return jnp.concatenate(
            [stack_row.reshape(fields * levels, cols), dir_rows.reshape(1, cols)], axis=0
        )

    from_left, from_right = neighbour_swaps(
        x_packet(stacked[:, :, 0], direction[:2]),
        x_packet(stacked[:, :, rows - 1], direction[d_rows - 2:]),
        "gx", i_x, n_x,
    )
    y_left, y_right = neighbour_swaps(
        stacked[:, :, :, :1], stacked[:, :, :, cols - 1:], "gy", lax.axis_index("gy"), n_y
    )
    if n_z == 2:
        sent = lax.dynamic_slice_in_dim(stacked, (1 - i_z) * (levels - 1), 1, axis=1)
        got = lax.ppermute(sent, "gz", [(0, 1), (1, 0)])
        zero = jnp.zeros_like(got)
        z_low = jnp.where(i_z == 1, got, zero)
        z_high = jnp.where(i_z == 0, got, zero)
    else:
        z_low = lax.ppermute(stacked[:, levels - 1:], "gz", shift_pairs(n_z, 1))
        z_high = lax.ppermute(stacked[:, :1], "gz", shift_pairs(n_z, -1))

    x_low = from_left[: fields * levels].reshape(fields, levels, 1, cols)
    x_high = from_right[: fields * levels].reshape(fields, levels, 1, cols)
    d_low = from_left[fields * levels:].reshape(2, d_cols)
    d_high = from_right[fields * levels:].reshape(2, d_cols)

    d_ext = jnp.concatenate([d_low, direction, d_high], axis=0)
    padded = jnp.concatenate([y_left, stacked, y_right], axis=3)
    pad_y = ((0, 0), (0, 0), (0, 0), (1, 1))
    padded = jnp.concatenate(
        [jnp.pad(x_low, pad_y), padded, jnp.pad(x_high, pad_y)], axis=2
    )
    pad_xy = ((0, 0), (0, 0), (1, 1), (1, 1))
    padded = jnp.concatenate(
        [jnp.pad(z_low, pad_xy), padded, jnp.pad(z_high, pad_xy)], axis=1
    )
    applied = stencil(padded[:3], padded[3])
    stokes_image = apply_blocks(blocks, applied, True)
    partial_value = jnp.sum(stokes_image * adjoint, axis=(0, 1))

    own_width = cols // n_z
    if n_z == 2:
        sent = lax.dynamic_slice_in_dim(partial_value, (1 - i_z) * own_width, own_width, axis=1)
        mine = lax.dynamic_slice_in_dim(partial_value, i_z * own_width, own_width, axis=1)
        d_partner = lax.dynamic_slice_in_dim(d_ext, (1 - i_z) * (d_cols - 2), 2, axis=1)
        d_across = lax.dynamic_slice_in_dim(d_ext, i_z * (d_cols - 2), 2, axis=1)
        flat = d_partner.reshape(1, -1)
        packet = jnp.concatenate(
            [sent, jnp.pad(flat, ((0, 0), (0, own_width - flat.shape[1])))], axis=0
        )
        packet, d_across = lax.optimization_barrier((packet, d_across))
        got = lax.ppermute(packet, "gz", [(0, 1), (1, 0)])
        across_pairs = []
        for block in range(n_y - 1):
            across_pairs += [(2 * block + 1, 2 * block + 2), (2 * block + 2, 2 * block + 1)]
        got_across = lax.ppermute(d_across, ("gy", "gz"), across_pairs)
        column = mine + got[: sent.shape[0]]
        got_partner = got[sent.shape[0], : flat.shape[1]].reshape(d_partner.shape)
        d_left = jnp.where(i_z == 0, got_across, got_partner)
        d_right = jnp.where(i_z == 0, got_partner, got_across)
    else:
        column = lax.psum_scatter(partial_value, "gz", scatter_dimension=1, tiled=True)
        d_left = lax.ppermute(d_ext[:, d_cols - 2:], ("gy", "gz"), shift_pairs(n_col, 1))
        d_right = lax.ppermute(d_ext[:, :2], ("gy", "gz"), shift_pairs(n_col, -1))

    d_full = jnp.concatenate([d_left, d_ext, d_right], axis=1)
    inner = laplace(d_full)
    row_ids = lax.broadcasted_iota(jnp.int32, inner.shape, 0)
    col_ids = lax.broadcasted_iota(jnp.int32, inner.shape, 1)
    outside = (
        ((row_ids == 0) & (i_x == 0))
        | ((row_ids == inner.shape[0] - 1) & (i_x == n_x - 1))
        | ((col_ids == 0) & (i_col == 0))
        | ((col_ids == inner.shape[1] - 1) & (i_col == n_col - 1))
    )
    inner = jnp.where(outside, 0.0, inner)
    bilaplace = laplace(inner)
    hessian_dir = reg_weight * bilaplace + basal_mask.astype(jnp.float32) * (
        jnp.exp(friction) * column
    )
    return (stokes_image, hessian_dir)


def solution(mesh):
    return jax.shard_map(
        local,
        mesh=mesh,
        in_specs=(
            P(None, "gz", "gx", "gy"),
            P(None, "gz", "gx", "gy"),
            P("gz", "gx", "gy"),
            P("gx", "gy"),
            P("gx", "gy"),
            P(),
            P("gx", ("gy", "gz")),
            P("gx", ("gy", "gz")),
            P("gx", ("gy", "gz")),
        ),
        out_specs=(P(None, "gz", "gx", "gy"), P("gx", ("gy", "gz"))),
        check_vma=False,
    )
```

```python
import jax
import jax.numpy as jnp
from jax import lax
from jax.sharding import PartitionSpec as P
from jax.experimental import pallas as pl
from jax.experimental.pallas import tpu as pltpu


reg_weight = 0.05


def shift_pairs(count, step):
    if step > 0:
        return [(i, i + 1) for i in range(count - 1)]
    return [(i + 1, i) for i in range(count - 1)]


def prologue_kernel(
    vel_hbm, visc_hbm, flags_hbm, index_hbm, table_hbm, dir_hbm,
    stacked_ref, blocks_ref, low_ref, high_ref,
    vel_v, visc_v, flags_v, index_v, table_s, dir_v, sems,
):
    pairs = [
        (vel_hbm, vel_v), (visc_hbm, visc_v), (flags_hbm, flags_v),
        (index_hbm, index_v), (table_hbm, table_s), (dir_hbm, dir_v),
    ]
    copies = [pltpu.make_async_copy(s, d, sems.at[i]) for i, (s, d) in enumerate(pairs)]
    for copy in copies:
        copy.start()
    for copy in copies:
        copy.wait()
    index = index_v[...]
    hanging = flags_v[...] != 0
    count = table_s.shape[0] // 9
    blocks = []
    for j in range(9):
        entry = jnp.full(index.shape, table_s[j], jnp.float32)
        for number in range(1, count):
            entry = jnp.where(index == number, table_s[number * 9 + j], entry)
        entry = jnp.where(hanging, entry, 1.0 if j % 4 == 0 else 0.0)
        blocks_ref[j] = entry
        blocks.append(entry)
    groups = index.shape[1]
    fields, levels, rows, cols = stacked_ref.shape
    for c in range(fields - 1):
        for z in range(levels):
            slots = [vel_v[c, z, :, k * groups:(k + 1) * groups] for k in range(3)]
            for m in range(3):
                total = blocks[m * 3] * slots[0]
                total = total + blocks[m * 3 + 1] * slots[1]
                total = total + blocks[m * 3 + 2] * slots[2]
                stacked_ref[c, z, :, m * groups:(m + 1) * groups] = total
    stacked_ref[fields - 1] = visc_v[...]
    for f in range(fields):
        for z in range(levels):
            row = f * levels + z
            low_ref[row:row + 1, :] = stacked_ref[f, z, 0:1, :]
            high_ref[row:row + 1, :] = stacked_ref[f, z, rows - 1:rows, :]
    d_rows, d_cols = dir_v.shape
    edge = fields * levels
    low_ref[edge:, :] = jnp.zeros((2, cols), jnp.float32)
    high_ref[edge:, :] = jnp.zeros((2, cols), jnp.float32)
    low_ref[edge:, 0:d_cols] = dir_v[0:2, :]
    high_ref[edge:, 0:d_cols] = dir_v[d_rows - 2:, :]


def prologue(velocity, viscosity, hang_flags, hang_index, block_table, direction):
    fields = velocity.shape[0] + 1
    stack_shape = (fields,) + viscosity.shape
    packet = (fields * viscosity.shape[0] + 2, viscosity.shape[2])
    table = block_table.astype(jnp.float32).reshape(-1)
    f32 = jnp.float32
    anywhere = pl.BlockSpec(memory_space=pl.ANY)
    in_vmem = pl.BlockSpec(memory_space=pltpu.VMEM)
    return pl.pallas_call(
        prologue_kernel,
        out_shape=(
            jax.ShapeDtypeStruct(stack_shape, f32),
            jax.ShapeDtypeStruct((9,) + hang_index.shape, f32),
            jax.ShapeDtypeStruct(packet, f32),
            jax.ShapeDtypeStruct(packet, f32),
        ),
        in_specs=[anywhere] * 6,
        out_specs=(in_vmem,) * 4,
        scratch_shapes=[
            pltpu.VMEM(velocity.shape, f32),
            pltpu.VMEM(viscosity.shape, f32),
            pltpu.VMEM(hang_flags.shape, jnp.int32),
            pltpu.VMEM(hang_index.shape, jnp.int32),
            pltpu.SMEM(table.shape, f32),
            pltpu.VMEM(direction.shape, f32),
            pltpu.SemaphoreType.DMA((6,)),
        ],
        cost_estimate=pl.CostEstimate(
            flops=200000, transcendentals=0, bytes_accessed=300000
        ),
    )(velocity, viscosity, hang_flags, hang_index, table, direction)


def block_matrices(hang_flags, hang_index, block_table):
    count = block_table.shape[0]
    numbers = lax.broadcasted_iota(jnp.int32, (count,) + hang_index.shape, 0)
    one_hot = (hang_index[None] == numbers).astype(jnp.float32)
    table = block_table.astype(jnp.float32).reshape(count, 9)
    chosen = lax.dot_general(
        table, one_hot, (((0,), (0,)), ((), ())), precision=lax.Precision.HIGHEST
    )
    identity = jnp.eye(3, dtype=jnp.float32).reshape(9)[:, None, None]
    blocks = jnp.where(hang_flags[None] != 0, chosen, identity)
    return [[blocks[m * 3 + k] for k in range(3)] for m in range(3)]


def apply_blocks(blocks, field, transpose):
    groups = field.shape[-1] // 3
    slots = [field[..., k * groups:(k + 1) * groups] for k in range(3)]
    mixed = []
    for m in range(3):
        total = None
        for k in range(3):
            weight = blocks[k][m] if transpose else blocks[m][k]
            term = weight * slots[k]
            total = term if total is None else total + term
        mixed.append(total)
    return jnp.concatenate(mixed, axis=-1)


def shifted(padded, spatial, offset):
    lead = padded.ndim - 3
    index = [slice(None)] * lead + [slice(1, -1)] * 3
    if offset == 1:
        index[lead + spatial] = slice(2, None)
    elif offset == -1:
        index[lead + spatial] = slice(None, -2)
    return padded[tuple(index)]


def stencil(padded_vel, padded_visc):
    centre_vel = shifted(padded_vel, 0, 0)
    centre_visc = shifted(padded_visc, 0, 0)
    total = jnp.zeros(centre_vel.shape, jnp.float32)
    for spatial in range(3):
        for offset in (1, -1):
            face = 0.5 * (centre_visc + shifted(padded_visc, spatial, offset))
            total = total + face[None] * (centre_vel - shifted(padded_vel, spatial, offset))
    return total


def laplace(padded):
    return (
        4.0 * padded[1:-1, 1:-1]
        - padded[2:, 1:-1]
        - padded[:-2, 1:-1]
        - padded[1:-1, 2:]
        - padded[1:-1, :-2]
    )


def local(
    velocity,
    adjoint,
    viscosity,
    hang_flags,
    hang_index,
    block_table,
    friction,
    basal_mask,
    direction,
):
    n_x = lax.axis_size("gx")
    n_y = lax.axis_size("gy")
    n_z = lax.axis_size("gz")
    i_x = lax.axis_index("gx")
    i_z = lax.axis_index("gz")
    n_col = n_y * n_z
    i_col = lax.axis_index("gy") * n_z + i_z

    stacked, table9, low_packet, high_packet = prologue(
        velocity, viscosity, hang_flags, hang_index, block_table, direction
    )
    blocks = [[table9[m * 3 + k] for k in range(3)] for m in range(3)]
    fields, levels, rows, cols = stacked.shape
    d_rows, d_cols = direction.shape

    from_left = lax.ppermute(high_packet, "gx", shift_pairs(n_x, 1))
    from_right = lax.ppermute(low_packet, "gx", shift_pairs(n_x, -1))
    y_left = lax.ppermute(stacked[:, :, :, cols - 1:], "gy", shift_pairs(n_y, 1))
    y_right = lax.ppermute(stacked[:, :, :, :1], "gy", shift_pairs(n_y, -1))
    if n_z == 2:
        sent = lax.dynamic_slice_in_dim(stacked, (1 - i_z) * (levels - 1), 1, axis=1)
        got = lax.ppermute(sent, "gz", [(0, 1), (1, 0)])
        zero = jnp.zeros_like(got)
        z_low = jnp.where(i_z == 1, got, zero)
        z_high = jnp.where(i_z == 0, got, zero)
    else:
        z_low = lax.ppermute(stacked[:, levels - 1:], "gz", shift_pairs(n_z, 1))
        z_high = lax.ppermute(stacked[:, :1], "gz", shift_pairs(n_z, -1))

    x_low = from_left[: fields * levels].reshape(fields, levels, 1, cols)
    x_high = from_right[: fields * levels].reshape(fields, levels, 1, cols)
    d_low = from_left[fields * levels:, :d_cols]
    d_high = from_right[fields * levels:, :d_cols]

    d_ext = jnp.concatenate([d_low, direction, d_high], axis=0)
    padded = jnp.concatenate([y_left, stacked, y_right], axis=3)
    pad_y = ((0, 0), (0, 0), (0, 0), (1, 1))
    padded = jnp.concatenate(
        [jnp.pad(x_low, pad_y), padded, jnp.pad(x_high, pad_y)], axis=2
    )
    pad_xy = ((0, 0), (0, 0), (1, 1), (1, 1))
    padded = jnp.concatenate(
        [jnp.pad(z_low, pad_xy), padded, jnp.pad(z_high, pad_xy)], axis=1
    )
    applied = stencil(padded[:3], padded[3])
    stokes_image = apply_blocks(blocks, applied, True)
    partial_value = jnp.sum(stokes_image * adjoint, axis=(0, 1))

    own_width = cols // n_z
    if n_z == 2:
        sent = lax.dynamic_slice_in_dim(partial_value, (1 - i_z) * own_width, own_width, axis=1)
        mine = lax.dynamic_slice_in_dim(partial_value, i_z * own_width, own_width, axis=1)
        d_partner = lax.dynamic_slice_in_dim(d_ext, (1 - i_z) * (d_cols - 2), 2, axis=1)
        d_across = lax.dynamic_slice_in_dim(d_ext, i_z * (d_cols - 2), 2, axis=1)
        flat = d_partner.reshape(1, -1)
        packet = jnp.concatenate(
            [sent, jnp.pad(flat, ((0, 0), (0, own_width - flat.shape[1])))], axis=0
        )
        packet, d_across = lax.optimization_barrier((packet, d_across))
        got = lax.ppermute(packet, "gz", [(0, 1), (1, 0)])
        across_pairs = []
        for block in range(n_y - 1):
            across_pairs += [(2 * block + 1, 2 * block + 2), (2 * block + 2, 2 * block + 1)]
        got_across = lax.ppermute(d_across, ("gy", "gz"), across_pairs)
        column = mine + got[: sent.shape[0]]
        got_partner = got[sent.shape[0], : flat.shape[1]].reshape(d_partner.shape)
        d_left = jnp.where(i_z == 0, got_across, got_partner)
        d_right = jnp.where(i_z == 0, got_partner, got_across)
    else:
        column = lax.psum_scatter(partial_value, "gz", scatter_dimension=1, tiled=True)
        d_left = lax.ppermute(d_ext[:, d_cols - 2:], ("gy", "gz"), shift_pairs(n_col, 1))
        d_right = lax.ppermute(d_ext[:, :2], ("gy", "gz"), shift_pairs(n_col, -1))

    d_full = jnp.concatenate([d_left, d_ext, d_right], axis=1)
    inner = laplace(d_full)
    row_ids = lax.broadcasted_iota(jnp.int32, inner.shape, 0)
    col_ids = lax.broadcasted_iota(jnp.int32, inner.shape, 1)
    outside = (
        ((row_ids == 0) & (i_x == 0))
        | ((row_ids == inner.shape[0] - 1) & (i_x == n_x - 1))
        | ((col_ids == 0) & (i_col == 0))
        | ((col_ids == inner.shape[1] - 1) & (i_col == n_col - 1))
    )
    inner = jnp.where(outside, 0.0, inner)
    bilaplace = laplace(inner)
    hessian_dir = reg_weight * bilaplace + basal_mask.astype(jnp.float32) * (
        jnp.exp(friction) * column
    )
    return (stokes_image, hessian_dir)


def solution(mesh):
    return jax.shard_map(
        local,
        mesh=mesh,
        in_specs=(
            P(None, "gz", "gx", "gy"),
            P(None, "gz", "gx", "gy"),
            P("gz", "gx", "gy"),
            P("gx", "gy"),
            P("gx", "gy"),
            P(),
            P("gx", ("gy", "gz")),
            P("gx", ("gy", "gz")),
            P("gx", ("gy", "gz")),
        ),
        out_specs=(P(None, "gz", "gx", "gy"), P("gx", ("gy", "gz"))),
        check_vma=False,
    )
```

```python
import jax
import jax.numpy as jnp
from jax import lax
from jax.sharding import PartitionSpec as P
from jax.experimental import pallas as pl
from jax.experimental.pallas import tpu as pltpu


reg_weight = 0.05


def shift_pairs(count, step):
    if step > 0:
        return [(i, i + 1) for i in range(count - 1)]
    return [(i + 1, i) for i in range(count - 1)]


def prologue_kernel(
    vel_hbm, visc_hbm, flags_hbm, index_hbm, table_s, dir_hbm,
    stacked_ref, blocks_ref, low_ref, high_ref, level_ref,
    vel_v, visc_v, flags_v, index_v, dir_v, sems,
):
    pairs = [
        (vel_hbm, vel_v), (visc_hbm, visc_v), (flags_hbm, flags_v),
        (index_hbm, index_v), (dir_hbm, dir_v),
    ]
    copies = [pltpu.make_async_copy(s, d, sems.at[i]) for i, (s, d) in enumerate(pairs)]
    for copy in copies:
        copy.start()
    for copy in copies:
        copy.wait()
    index = index_v[...]
    hanging = flags_v[...] != 0
    count = table_s.shape[0]
    blocks = []
    for j in range(9):
        entry = jnp.full(index.shape, table_s[0, j // 3, j % 3], jnp.float32)
        for number in range(1, count):
            entry = jnp.where(index == number, table_s[number, j // 3, j % 3], entry)
        entry = jnp.where(hanging, entry, 1.0 if j % 4 == 0 else 0.0)
        blocks_ref[j] = entry
        blocks.append(entry)
    groups = index.shape[1]
    fields, levels, rows, cols = stacked_ref.shape
    for c in range(fields - 1):
        for z in range(levels):
            slots = [vel_v[c, z, :, k * groups:(k + 1) * groups] for k in range(3)]
            for m in range(3):
                total = blocks[m * 3] * slots[0]
                total = total + blocks[m * 3 + 1] * slots[1]
                total = total + blocks[m * 3 + 2] * slots[2]
                stacked_ref[c, z, :, m * groups:(m + 1) * groups] = total
    stacked_ref[fields - 1] = visc_v[...]
    for f in range(fields):
        for z in range(levels):
            row = f * levels + z
            low_ref[row:row + 1, :] = stacked_ref[f, z, 0:1, :]
            high_ref[row:row + 1, :] = stacked_ref[f, z, rows - 1:rows, :]
    if lax.axis_size("gz") == 2:
        level = (1 - lax.axis_index("gz")) * (levels - 1)
        level_ref[...] = stacked_ref[:, pl.ds(level, 1)]
    else:
        level_ref[...] = stacked_ref[:, 0:1]
    d_rows, d_cols = dir_v.shape
    edge = fields * levels
    low_ref[edge:, :] = jnp.zeros((2, cols), jnp.float32)
    high_ref[edge:, :] = jnp.zeros((2, cols), jnp.float32)
    low_ref[edge:, 0:d_cols] = dir_v[0:2, :]
    high_ref[edge:, 0:d_cols] = dir_v[d_rows - 2:, :]


def prologue(velocity, viscosity, hang_flags, hang_index, block_table, direction):
    fields = velocity.shape[0] + 1
    stack_shape = (fields,) + viscosity.shape
    packet = (fields * viscosity.shape[0] + 2, viscosity.shape[2])
    f32 = jnp.float32
    anywhere = pl.BlockSpec(memory_space=pl.ANY)
    in_vmem = pl.BlockSpec(memory_space=pltpu.VMEM)
    return pl.pallas_call(
        prologue_kernel,
        out_shape=(
            jax.ShapeDtypeStruct(stack_shape, f32),
            jax.ShapeDtypeStruct((9,) + hang_index.shape, f32),
            jax.ShapeDtypeStruct(packet, f32),
            jax.ShapeDtypeStruct(packet, f32),
            jax.ShapeDtypeStruct((fields, 1) + viscosity.shape[1:], f32),
        ),
        in_specs=[anywhere] * 4 + [pl.BlockSpec(memory_space=pltpu.SMEM), anywhere],
        out_specs=(in_vmem,) * 5,
        scratch_shapes=[
            pltpu.VMEM(velocity.shape, f32),
            pltpu.VMEM(viscosity.shape, f32),
            pltpu.VMEM(hang_flags.shape, jnp.int32),
            pltpu.VMEM(hang_index.shape, jnp.int32),
            pltpu.VMEM(direction.shape, f32),
            pltpu.SemaphoreType.DMA((5,)),
        ],
        cost_estimate=pl.CostEstimate(
            flops=200000, transcendentals=0, bytes_accessed=300000
        ),
    )(velocity, viscosity, hang_flags, hang_index, block_table.astype(f32), direction)


def block_matrices(hang_flags, hang_index, block_table):
    count = block_table.shape[0]
    numbers = lax.broadcasted_iota(jnp.int32, (count,) + hang_index.shape, 0)
    one_hot = (hang_index[None] == numbers).astype(jnp.float32)
    table = block_table.astype(jnp.float32).reshape(count, 9)
    chosen = lax.dot_general(
        table, one_hot, (((0,), (0,)), ((), ())), precision=lax.Precision.HIGHEST
    )
    identity = jnp.eye(3, dtype=jnp.float32).reshape(9)[:, None, None]
    blocks = jnp.where(hang_flags[None] != 0, chosen, identity)
    return [[blocks[m * 3 + k] for k in range(3)] for m in range(3)]


def apply_blocks(blocks, field, transpose):
    groups = field.shape[-1] // 3
    slots = [field[..., k * groups:(k + 1) * groups] for k in range(3)]
    mixed = []
    for m in range(3):
        total = None
        for k in range(3):
            weight = blocks[k][m] if transpose else blocks[m][k]
            term = weight * slots[k]
            total = term if total is None else total + term
        mixed.append(total)
    return jnp.concatenate(mixed, axis=-1)


def shifted(padded, spatial, offset):
    lead = padded.ndim - 3
    index = [slice(None)] * lead + [slice(1, -1)] * 3
    if offset == 1:
        index[lead + spatial] = slice(2, None)
    elif offset == -1:
        index[lead + spatial] = slice(None, -2)
    return padded[tuple(index)]


def stencil(padded_vel, padded_visc):
    centre_vel = shifted(padded_vel, 0, 0)
    centre_visc = shifted(padded_visc, 0, 0)
    total = jnp.zeros(centre_vel.shape, jnp.float32)
    for spatial in range(3):
        for offset in (1, -1):
            face = 0.5 * (centre_visc + shifted(padded_visc, spatial, offset))
            total = total + face[None] * (centre_vel - shifted(padded_vel, spatial, offset))
    return total


def laplace(padded):
    return (
        4.0 * padded[1:-1, 1:-1]
        - padded[2:, 1:-1]
        - padded[:-2, 1:-1]
        - padded[1:-1, 2:]
        - padded[1:-1, :-2]
    )


def local(
    velocity,
    adjoint,
    viscosity,
    hang_flags,
    hang_index,
    block_table,
    friction,
    basal_mask,
    direction,
):
    n_x = lax.axis_size("gx")
    n_y = lax.axis_size("gy")
    n_z = lax.axis_size("gz")
    i_x = lax.axis_index("gx")
    i_z = lax.axis_index("gz")
    n_col = n_y * n_z
    i_col = lax.axis_index("gy") * n_z + i_z

    stacked, table9, low_packet, high_packet, z_sent = prologue(
        velocity, viscosity, hang_flags, hang_index, block_table, direction
    )
    blocks = [[table9[m * 3 + k] for k in range(3)] for m in range(3)]
    fields, levels, rows, cols = stacked.shape
    d_rows, d_cols = direction.shape

    from_left = lax.ppermute(high_packet, "gx", shift_pairs(n_x, 1))
    from_right = lax.ppermute(low_packet, "gx", shift_pairs(n_x, -1))
    y_left = lax.ppermute(stacked[:, :, :, cols - 1:], "gy", shift_pairs(n_y, 1))
    y_right = lax.ppermute(stacked[:, :, :, :1], "gy", shift_pairs(n_y, -1))
    if n_z == 2:
        got = lax.ppermute(z_sent, "gz", [(0, 1), (1, 0)])
        zero = jnp.zeros_like(got)
        z_low = jnp.where(i_z == 1, got, zero)
        z_high = jnp.where(i_z == 0, got, zero)
    else:
        z_low = lax.ppermute(stacked[:, levels - 1:], "gz", shift_pairs(n_z, 1))
        z_high = lax.ppermute(stacked[:, :1], "gz", shift_pairs(n_z, -1))

    x_low = from_left[: fields * levels].reshape(fields, levels, 1, cols)
    x_high = from_right[: fields * levels].reshape(fields, levels, 1, cols)
    d_low = from_left[fields * levels:, :d_cols]
    d_high = from_right[fields * levels:, :d_cols]

    d_ext = jnp.concatenate([d_low, direction, d_high], axis=0)
    padded = jnp.concatenate([y_left, stacked, y_right], axis=3)
    pad_y = ((0, 0), (0, 0), (0, 0), (1, 1))
    padded = jnp.concatenate(
        [jnp.pad(x_low, pad_y), padded, jnp.pad(x_high, pad_y)], axis=2
    )
    pad_xy = ((0, 0), (0, 0), (1, 1), (1, 1))
    padded = jnp.concatenate(
        [jnp.pad(z_low, pad_xy), padded, jnp.pad(z_high, pad_xy)], axis=1
    )
    applied = stencil(padded[:3], padded[3])
    stokes_image = apply_blocks(blocks, applied, True)
    partial_value = jnp.sum(stokes_image * adjoint, axis=(0, 1))

    own_width = cols // n_z
    if n_z == 2:
        sent = lax.dynamic_slice_in_dim(partial_value, (1 - i_z) * own_width, own_width, axis=1)
        mine = lax.dynamic_slice_in_dim(partial_value, i_z * own_width, own_width, axis=1)
        d_partner = lax.dynamic_slice_in_dim(d_ext, (1 - i_z) * (d_cols - 2), 2, axis=1)
        d_across = lax.dynamic_slice_in_dim(d_ext, i_z * (d_cols - 2), 2, axis=1)
        flat = d_partner.reshape(1, -1)
        packet = jnp.concatenate(
            [sent, jnp.pad(flat, ((0, 0), (0, own_width - flat.shape[1])))], axis=0
        )
        packet, d_across = lax.optimization_barrier((packet, d_across))
        got = lax.ppermute(packet, "gz", [(0, 1), (1, 0)])
        across_pairs = []
        for block in range(n_y - 1):
            across_pairs += [(2 * block + 1, 2 * block + 2), (2 * block + 2, 2 * block + 1)]
        got_across = lax.ppermute(d_across, ("gy", "gz"), across_pairs)
        column = mine + got[: sent.shape[0]]
        got_partner = got[sent.shape[0], : flat.shape[1]].reshape(d_partner.shape)
        d_left = jnp.where(i_z == 0, got_across, got_partner)
        d_right = jnp.where(i_z == 0, got_partner, got_across)
    else:
        column = lax.psum_scatter(partial_value, "gz", scatter_dimension=1, tiled=True)
        d_left = lax.ppermute(d_ext[:, d_cols - 2:], ("gy", "gz"), shift_pairs(n_col, 1))
        d_right = lax.ppermute(d_ext[:, :2], ("gy", "gz"), shift_pairs(n_col, -1))

    d_full = jnp.concatenate([d_left, d_ext, d_right], axis=1)
    inner = laplace(d_full)
    row_ids = lax.broadcasted_iota(jnp.int32, inner.shape, 0)
    col_ids = lax.broadcasted_iota(jnp.int32, inner.shape, 1)
    outside = (
        ((row_ids == 0) & (i_x == 0))
        | ((row_ids == inner.shape[0] - 1) & (i_x == n_x - 1))
        | ((col_ids == 0) & (i_col == 0))
        | ((col_ids == inner.shape[1] - 1) & (i_col == n_col - 1))
    )
    inner = jnp.where(outside, 0.0, inner)
    bilaplace = laplace(inner)
    hessian_dir = reg_weight * bilaplace + basal_mask.astype(jnp.float32) * (
        jnp.exp(friction) * column
    )
    return (stokes_image, hessian_dir)


def solution(mesh):
    return jax.shard_map(
        local,
        mesh=mesh,
        in_specs=(
            P(None, "gz", "gx", "gy"),
            P(None, "gz", "gx", "gy"),
            P("gz", "gx", "gy"),
            P("gx", "gy"),
            P("gx", "gy"),
            P(),
            P("gx", ("gy", "gz")),
            P("gx", ("gy", "gz")),
            P("gx", ("gy", "gz")),
        ),
        out_specs=(P(None, "gz", "gx", "gy"), P("gx", ("gy", "gz"))),
        check_vma=False,
    )
```

```python
import functools

import jax
import jax.numpy as jnp
from jax import lax
from jax.sharding import PartitionSpec as P
from jax.experimental import pallas as pl
from jax.experimental.pallas import tpu as pltpu


reg_weight = 0.05


def shift_pairs(count, step):
    if step > 0:
        return [(i, i + 1) for i in range(count - 1)]
    return [(i + 1, i) for i in range(count - 1)]


def prologue_kernel(
    vel_hbm, visc_hbm, flags_hbm, index_hbm, table_hbm, dir_hbm,
    stacked_ref, blocks_ref, low_ref, high_ref,
    vel_v, visc_v, flags_v, index_v, table_s, dir_v, sems,
):
    pairs = [
        (vel_hbm, vel_v), (visc_hbm, visc_v), (flags_hbm, flags_v),
        (index_hbm, index_v), (table_hbm, table_s), (dir_hbm, dir_v),
    ]
    copies = [pltpu.make_async_copy(s, d, sems.at[i]) for i, (s, d) in enumerate(pairs)]
    for copy in copies:
        copy.start()
    for copy in copies:
        copy.wait()
    index = index_v[...]
    hanging = flags_v[...] != 0
    count = table_s.shape[0] // 9
    blocks = []
    for j in range(9):
        entry = jnp.full(index.shape, table_s[j], jnp.float32)
        for number in range(1, count):
            entry = jnp.where(index == number, table_s[number * 9 + j], entry)
        entry = jnp.where(hanging, entry, 1.0 if j % 4 == 0 else 0.0)
        blocks_ref[j] = entry
        blocks.append(entry)
    groups = index.shape[1]
    fields, levels, rows, cols = stacked_ref.shape
    for c in range(fields - 1):
        for z in range(levels):
            slots = [vel_v[c, z, :, k * groups:(k + 1) * groups] for k in range(3)]
            for m in range(3):
                total = blocks[m * 3] * slots[0]
                total = total + blocks[m * 3 + 1] * slots[1]
                total = total + blocks[m * 3 + 2] * slots[2]
                stacked_ref[c, z, :, m * groups:(m + 1) * groups] = total
    stacked_ref[fields - 1] = visc_v[...]
    for f in range(fields):
        for z in range(levels):
            row = f * levels + z
            low_ref[row:row + 1, :] = stacked_ref[f, z, 0:1, :]
            high_ref[row:row + 1, :] = stacked_ref[f, z, rows - 1:rows, :]
    d_rows, d_cols = dir_v.shape
    edge = fields * levels
    low_ref[edge:, :] = jnp.zeros((2, cols), jnp.float32)
    high_ref[edge:, :] = jnp.zeros((2, cols), jnp.float32)
    low_ref[edge:, 0:d_cols] = dir_v[0:2, :]
    high_ref[edge:, 0:d_cols] = dir_v[d_rows - 2:, :]


def prologue(velocity, viscosity, hang_flags, hang_index, block_table, direction):
    fields = velocity.shape[0] + 1
    stack_shape = (fields,) + viscosity.shape
    packet = (fields * viscosity.shape[0] + 2, viscosity.shape[2])
    table = block_table.astype(jnp.float32).reshape(-1)
    f32 = jnp.float32
    anywhere = pl.BlockSpec(memory_space=pl.ANY)
    in_vmem = pl.BlockSpec(memory_space=pltpu.VMEM)
    return pl.pallas_call(
        prologue_kernel,
        out_shape=(
            jax.ShapeDtypeStruct(stack_shape, f32),
            jax.ShapeDtypeStruct((9,) + hang_index.shape, f32),
            jax.ShapeDtypeStruct(packet, f32),
            jax.ShapeDtypeStruct(packet, f32),
        ),
        in_specs=[anywhere] * 6,
        out_specs=(in_vmem,) * 4,
        scratch_shapes=[
            pltpu.VMEM(velocity.shape, f32),
            pltpu.VMEM(viscosity.shape, f32),
            pltpu.VMEM(hang_flags.shape, jnp.int32),
            pltpu.VMEM(hang_index.shape, jnp.int32),
            pltpu.SMEM(table.shape, f32),
            pltpu.VMEM(direction.shape, f32),
            pltpu.SemaphoreType.DMA((6,)),
        ],
        cost_estimate=pl.CostEstimate(
            flops=200000, transcendentals=0, bytes_accessed=300000
        ),
    )(velocity, viscosity, hang_flags, hang_index, table, direction)


def stencil_kernel(
    swap, stacked_hbm, blocks_hbm, adjoint_hbm, from_left_ref, from_right_ref,
    y_left_ref, y_right_ref, z_low_ref, z_high_ref,
    stokes_ref, partial_ref, stack_v, blocks_v, adjoint_v, sems,
):
    pairs = [(stacked_hbm, stack_v), (blocks_hbm, blocks_v), (adjoint_hbm, adjoint_v)]
    copies = [pltpu.make_async_copy(s, d, sems.at[i]) for i, (s, d) in enumerate(pairs)]
    for copy in copies:
        copy.start()
    for copy in copies:
        copy.wait()
    fields, levels, rows, cols = stack_v.shape
    shape = (rows, cols)
    groups = cols // 3
    row_ids = lax.broadcasted_iota(jnp.int32, shape, 0)
    col_ids = lax.broadcasted_iota(jnp.int32, shape, 1)
    if swap:
        i_z = lax.axis_index("gz")
        low_on = i_z == 1
        high_on = i_z == 0

    def neighbours(f, z):
        centre = stack_v[f, z]
        r = f * levels + z
        if z > 0:
            z_minus = stack_v[f, z - 1]
        else:
            z_minus = z_low_ref[f, 0]
            if swap:
                z_minus = jnp.where(low_on, z_minus, 0.0)
        if z < levels - 1:
            z_plus = stack_v[f, z + 1]
        else:
            z_plus = z_high_ref[f, 0]
            if swap:
                z_plus = jnp.where(high_on, z_plus, 0.0)
        x_minus = jnp.where(
            row_ids == 0, jnp.broadcast_to(from_left_ref[r:r + 1, :], shape),
            pltpu.roll(centre, 1, 0),
        )
        x_plus = jnp.where(
            row_ids == rows - 1, jnp.broadcast_to(from_right_ref[r:r + 1, :], shape),
            pltpu.roll(centre, rows - 1, 0),
        )
        y_minus = jnp.where(
            col_ids == 0, jnp.broadcast_to(y_left_ref[f, z], shape), pltpu.roll(centre, 1, 1)
        )
        y_plus = jnp.where(
            col_ids == cols - 1, jnp.broadcast_to(y_right_ref[f, z], shape),
            pltpu.roll(centre, cols - 1, 1),
        )
        return centre, [z_plus, z_minus, x_plus, x_minus, y_plus, y_minus]

    part = jnp.zeros(shape, jnp.float32)
    for z in range(levels):
        mu, mu_next = neighbours(fields - 1, z)
        faces = [0.5 * (mu + other) for other in mu_next]
        for c in range(fields - 1):
            centre, others = neighbours(c, z)
            total = jnp.zeros(shape, jnp.float32)
            for face, other in zip(faces, others):
                total = total + face * (centre - other)
            for k in range(3):
                image = blocks_v[k] * total[:, 0:groups]
                image = image + blocks_v[3 + k] * total[:, groups:2 * groups]
                image = image + blocks_v[6 + k] * total[:, 2 * groups:]
                stokes_ref[c, z, :, k * groups:(k + 1) * groups] = image
    for c in range(fields - 1):
        for z in range(levels):
            part = part + stokes_ref[c, z] * adjoint_v[c, z]
    partial_ref[...] = part


def stencil_apply(stacked, blocks, adjoint, from_left, from_right, y_left, y_right, z_low, z_high, swap):
    f32 = jnp.float32
    anywhere = pl.BlockSpec(memory_space=pl.ANY)
    in_vmem = pl.BlockSpec(memory_space=pltpu.VMEM)
    return pl.pallas_call(
        functools.partial(stencil_kernel, swap),
        out_shape=(
            jax.ShapeDtypeStruct(adjoint.shape, f32),
            jax.ShapeDtypeStruct(adjoint.shape[2:], f32),
        ),
        in_specs=[anywhere] * 3 + [in_vmem] * 6,
        out_specs=(in_vmem, in_vmem),
        scratch_shapes=[
            pltpu.VMEM(stacked.shape, f32),
            pltpu.VMEM(blocks.shape, f32),
            pltpu.VMEM(adjoint.shape, f32),
            pltpu.SemaphoreType.DMA((3,)),
        ],
        cost_estimate=pl.CostEstimate(
            flops=400000, transcendentals=0, bytes_accessed=300000
        ),
    )(stacked, blocks, adjoint, from_left, from_right, y_left, y_right, z_low, z_high)


def block_matrices(hang_flags, hang_index, block_table):
    count = block_table.shape[0]
    numbers = lax.broadcasted_iota(jnp.int32, (count,) + hang_index.shape, 0)
    one_hot = (hang_index[None] == numbers).astype(jnp.float32)
    table = block_table.astype(jnp.float32).reshape(count, 9)
    chosen = lax.dot_general(
        table, one_hot, (((0,), (0,)), ((), ())), precision=lax.Precision.HIGHEST
    )
    identity = jnp.eye(3, dtype=jnp.float32).reshape(9)[:, None, None]
    blocks = jnp.where(hang_flags[None] != 0, chosen, identity)
    return [[blocks[m * 3 + k] for k in range(3)] for m in range(3)]


def apply_blocks(blocks, field, transpose):
    groups = field.shape[-1] // 3
    slots = [field[..., k * groups:(k + 1) * groups] for k in range(3)]
    mixed = []
    for m in range(3):
        total = None
        for k in range(3):
            weight = blocks[k][m] if transpose else blocks[m][k]
            term = weight * slots[k]
            total = term if total is None else total + term
        mixed.append(total)
    return jnp.concatenate(mixed, axis=-1)


def shifted(padded, spatial, offset):
    lead = padded.ndim - 3
    index = [slice(None)] * lead + [slice(1, -1)] * 3
    if offset == 1:
        index[lead + spatial] = slice(2, None)
    elif offset == -1:
        index[lead + spatial] = slice(None, -2)
    return padded[tuple(index)]


def stencil(padded_vel, padded_visc):
    centre_vel = shifted(padded_vel, 0, 0)
    centre_visc = shifted(padded_visc, 0, 0)
    total = jnp.zeros(centre_vel.shape, jnp.float32)
    for spatial in range(3):
        for offset in (1, -1):
            face = 0.5 * (centre_visc + shifted(padded_visc, spatial, offset))
            total = total + face[None] * (centre_vel - shifted(padded_vel, spatial, offset))
    return total


def laplace(padded):
    return (
        4.0 * padded[1:-1, 1:-1]
        - padded[2:, 1:-1]
        - padded[:-2, 1:-1]
        - padded[1:-1, 2:]
        - padded[1:-1, :-2]
    )


def local(
    velocity,
    adjoint,
    viscosity,
    hang_flags,
    hang_index,
    block_table,
    friction,
    basal_mask,
    direction,
):
    n_x = lax.axis_size("gx")
    n_y = lax.axis_size("gy")
    n_z = lax.axis_size("gz")
    i_x = lax.axis_index("gx")
    i_z = lax.axis_index("gz")
    n_col = n_y * n_z
    i_col = lax.axis_index("gy") * n_z + i_z

    stacked, table9, low_packet, high_packet = prologue(
        velocity, viscosity, hang_flags, hang_index, block_table, direction
    )
    blocks = [[table9[m * 3 + k] for k in range(3)] for m in range(3)]
    fields, levels, rows, cols = stacked.shape
    d_rows, d_cols = direction.shape

    from_left = lax.ppermute(high_packet, "gx", shift_pairs(n_x, 1))
    from_right = lax.ppermute(low_packet, "gx", shift_pairs(n_x, -1))
    y_left = lax.ppermute(stacked[:, :, :, cols - 1:], "gy", shift_pairs(n_y, 1))
    y_right = lax.ppermute(stacked[:, :, :, :1], "gy", shift_pairs(n_y, -1))
    if n_z == 2:
        sent = lax.dynamic_slice_in_dim(stacked, (1 - i_z) * (levels - 1), 1, axis=1)
        got = lax.ppermute(sent, "gz", [(0, 1), (1, 0)])
        z_low = z_high = got
    else:
        z_low = lax.ppermute(stacked[:, levels - 1:], "gz", shift_pairs(n_z, 1))
        z_high = lax.ppermute(stacked[:, :1], "gz", shift_pairs(n_z, -1))

    d_low = from_left[fields * levels:, :d_cols]
    d_high = from_right[fields * levels:, :d_cols]

    d_ext = jnp.concatenate([d_low, direction, d_high], axis=0)
    stokes_image, partial_value = stencil_apply(
        stacked, table9, adjoint, from_left, from_right, y_left, y_right, z_low, z_high, n_z == 2
    )

    own_width = cols // n_z
    if n_z == 2:
        sent = lax.dynamic_slice_in_dim(partial_value, (1 - i_z) * own_width, own_width, axis=1)
        mine = lax.dynamic_slice_in_dim(partial_value, i_z * own_width, own_width, axis=1)
        d_partner = lax.dynamic_slice_in_dim(d_ext, (1 - i_z) * (d_cols - 2), 2, axis=1)
        d_across = lax.dynamic_slice_in_dim(d_ext, i_z * (d_cols - 2), 2, axis=1)
        flat = d_partner.reshape(1, -1)
        packet = jnp.concatenate(
            [sent, jnp.pad(flat, ((0, 0), (0, own_width - flat.shape[1])))], axis=0
        )
        packet, d_across = lax.optimization_barrier((packet, d_across))
        got = lax.ppermute(packet, "gz", [(0, 1), (1, 0)])
        across_pairs = []
        for block in range(n_y - 1):
            across_pairs += [(2 * block + 1, 2 * block + 2), (2 * block + 2, 2 * block + 1)]
        got_across = lax.ppermute(d_across, ("gy", "gz"), across_pairs)
        column = mine + got[: sent.shape[0]]
        got_partner = got[sent.shape[0], : flat.shape[1]].reshape(d_partner.shape)
        d_left = jnp.where(i_z == 0, got_across, got_partner)
        d_right = jnp.where(i_z == 0, got_partner, got_across)
    else:
        column = lax.psum_scatter(partial_value, "gz", scatter_dimension=1, tiled=True)
        d_left = lax.ppermute(d_ext[:, d_cols - 2:], ("gy", "gz"), shift_pairs(n_col, 1))
        d_right = lax.ppermute(d_ext[:, :2], ("gy", "gz"), shift_pairs(n_col, -1))

    d_full = jnp.concatenate([d_left, d_ext, d_right], axis=1)
    inner = laplace(d_full)
    row_ids = lax.broadcasted_iota(jnp.int32, inner.shape, 0)
    col_ids = lax.broadcasted_iota(jnp.int32, inner.shape, 1)
    outside = (
        ((row_ids == 0) & (i_x == 0))
        | ((row_ids == inner.shape[0] - 1) & (i_x == n_x - 1))
        | ((col_ids == 0) & (i_col == 0))
        | ((col_ids == inner.shape[1] - 1) & (i_col == n_col - 1))
    )
    inner = jnp.where(outside, 0.0, inner)
    bilaplace = laplace(inner)
    hessian_dir = reg_weight * bilaplace + basal_mask.astype(jnp.float32) * (
        jnp.exp(friction) * column
    )
    return (stokes_image, hessian_dir)


def solution(mesh):
    return jax.shard_map(
        local,
        mesh=mesh,
        in_specs=(
            P(None, "gz", "gx", "gy"),
            P(None, "gz", "gx", "gy"),
            P("gz", "gx", "gy"),
            P("gx", "gy"),
            P("gx", "gy"),
            P(),
            P("gx", ("gy", "gz")),
            P("gx", ("gy", "gz")),
            P("gx", ("gy", "gz")),
        ),
        out_specs=(P(None, "gz", "gx", "gy"), P("gx", ("gy", "gz"))),
        check_vma=False,
    )
```

```python
import jax
import jax.numpy as jnp
from jax import lax
from jax.sharding import PartitionSpec as P
from jax.experimental import pallas as pl
from jax.experimental.pallas import tpu as pltpu


reg_weight = 0.05


def shift_pairs(count, step):
    if step > 0:
        return [(i, i + 1) for i in range(count - 1)]
    return [(i + 1, i) for i in range(count - 1)]


def prologue_kernel(
    vel_hbm, visc_hbm, flags_hbm, index_hbm, table_hbm, dir_hbm,
    stacked_ref, blocks_ref, low_ref, high_ref, level_ref,
    vel_v, visc_v, flags_v, index_v, table_s, dir_v, sems,
):
    pairs = [
        (vel_hbm, vel_v), (visc_hbm, visc_v), (flags_hbm, flags_v),
        (index_hbm, index_v), (table_hbm, table_s), (dir_hbm, dir_v),
    ]
    copies = [pltpu.make_async_copy(s, d, sems.at[i]) for i, (s, d) in enumerate(pairs)]
    for copy in copies:
        copy.start()
    for copy in copies:
        copy.wait()
    index = index_v[...]
    hanging = flags_v[...] != 0
    count = table_s.shape[0] // 9
    blocks = []
    for j in range(9):
        entry = jnp.full(index.shape, table_s[j], jnp.float32)
        for number in range(1, count):
            entry = jnp.where(index == number, table_s[number * 9 + j], entry)
        entry = jnp.where(hanging, entry, 1.0 if j % 4 == 0 else 0.0)
        blocks_ref[j] = entry
        blocks.append(entry)
    groups = index.shape[1]
    fields, levels, rows, cols = stacked_ref.shape
    for c in range(fields - 1):
        for z in range(levels):
            slots = [vel_v[c, z, :, k * groups:(k + 1) * groups] for k in range(3)]
            for m in range(3):
                total = blocks[m * 3] * slots[0]
                total = total + blocks[m * 3 + 1] * slots[1]
                total = total + blocks[m * 3 + 2] * slots[2]
                stacked_ref[c, z, :, m * groups:(m + 1) * groups] = total
    stacked_ref[fields - 1] = visc_v[...]
    for f in range(fields):
        for z in range(levels):
            row = f * levels + z
            low_ref[row:row + 1, :] = stacked_ref[f, z, 0:1, :]
            high_ref[row:row + 1, :] = stacked_ref[f, z, rows - 1:rows, :]
    if lax.axis_size("gz") == 2:
        level = (1 - lax.axis_index("gz")) * (levels - 1)
        level_ref[...] = stacked_ref[:, pl.ds(level, 1)]
    else:
        level_ref[...] = stacked_ref[:, 0:1]
    d_rows, d_cols = dir_v.shape
    edge = fields * levels
    low_ref[edge:, :] = jnp.zeros((2, cols), jnp.float32)
    high_ref[edge:, :] = jnp.zeros((2, cols), jnp.float32)
    low_ref[edge:, 0:d_cols] = dir_v[0:2, :]
    high_ref[edge:, 0:d_cols] = dir_v[d_rows - 2:, :]


def prologue(velocity, viscosity, hang_flags, hang_index, block_table, direction):
    fields = velocity.shape[0] + 1
    stack_shape = (fields,) + viscosity.shape
    packet = (fields * viscosity.shape[0] + 2, viscosity.shape[2])
    table = block_table.astype(jnp.float32).reshape(-1)
    f32 = jnp.float32
    anywhere = pl.BlockSpec(memory_space=pl.ANY)
    in_vmem = pl.BlockSpec(memory_space=pltpu.VMEM)
    return pl.pallas_call(
        prologue_kernel,
        out_shape=(
            jax.ShapeDtypeStruct(stack_shape, f32),
            jax.ShapeDtypeStruct((9,) + hang_index.shape, f32),
            jax.ShapeDtypeStruct(packet, f32),
            jax.ShapeDtypeStruct(packet, f32),
            jax.ShapeDtypeStruct((fields, 1) + viscosity.shape[1:], f32),
        ),
        in_specs=[anywhere] * 6,
        out_specs=(in_vmem,) * 5,
        scratch_shapes=[
            pltpu.VMEM(velocity.shape, f32),
            pltpu.VMEM(viscosity.shape, f32),
            pltpu.VMEM(hang_flags.shape, jnp.int32),
            pltpu.VMEM(hang_index.shape, jnp.int32),
            pltpu.SMEM(table.shape, f32),
            pltpu.VMEM(direction.shape, f32),
            pltpu.SemaphoreType.DMA((6,)),
        ],
        cost_estimate=pl.CostEstimate(
            flops=200000, transcendentals=0, bytes_accessed=300000
        ),
    )(velocity, viscosity, hang_flags, hang_index, table, direction)


def block_matrices(hang_flags, hang_index, block_table):
    count = block_table.shape[0]
    numbers = lax.broadcasted_iota(jnp.int32, (count,) + hang_index.shape, 0)
    one_hot = (hang_index[None] == numbers).astype(jnp.float32)
    table = block_table.astype(jnp.float32).reshape(count, 9)
    chosen = lax.dot_general(
        table, one_hot, (((0,), (0,)), ((), ())), precision=lax.Precision.HIGHEST
    )
    identity = jnp.eye(3, dtype=jnp.float32).reshape(9)[:, None, None]
    blocks = jnp.where(hang_flags[None] != 0, chosen, identity)
    return [[blocks[m * 3 + k] for k in range(3)] for m in range(3)]


def apply_blocks(blocks, field, transpose):
    groups = field.shape[-1] // 3
    slots = [field[..., k * groups:(k + 1) * groups] for k in range(3)]
    mixed = []
    for m in range(3):
        total = None
        for k in range(3):
            weight = blocks[k][m] if transpose else blocks[m][k]
            term = weight * slots[k]
            total = term if total is None else total + term
        mixed.append(total)
    return jnp.concatenate(mixed, axis=-1)


def shifted(padded, spatial, offset):
    lead = padded.ndim - 3
    index = [slice(None)] * lead + [slice(1, -1)] * 3
    if offset == 1:
        index[lead + spatial] = slice(2, None)
    elif offset == -1:
        index[lead + spatial] = slice(None, -2)
    return padded[tuple(index)]


def stencil(padded_vel, padded_visc):
    centre_vel = shifted(padded_vel, 0, 0)
    centre_visc = shifted(padded_visc, 0, 0)
    total = jnp.zeros(centre_vel.shape, jnp.float32)
    for spatial in range(3):
        for offset in (1, -1):
            face = 0.5 * (centre_visc + shifted(padded_visc, spatial, offset))
            total = total + face[None] * (centre_vel - shifted(padded_vel, spatial, offset))
    return total


def laplace(padded):
    return (
        4.0 * padded[1:-1, 1:-1]
        - padded[2:, 1:-1]
        - padded[:-2, 1:-1]
        - padded[1:-1, 2:]
        - padded[1:-1, :-2]
    )


def local(
    velocity,
    adjoint,
    viscosity,
    hang_flags,
    hang_index,
    block_table,
    friction,
    basal_mask,
    direction,
):
    n_x = lax.axis_size("gx")
    n_y = lax.axis_size("gy")
    n_z = lax.axis_size("gz")
    i_x = lax.axis_index("gx")
    i_z = lax.axis_index("gz")
    n_col = n_y * n_z
    i_col = lax.axis_index("gy") * n_z + i_z

    stacked, table9, low_packet, high_packet, z_sent = prologue(
        velocity, viscosity, hang_flags, hang_index, block_table, direction
    )
    blocks = [[table9[m * 3 + k] for k in range(3)] for m in range(3)]
    fields, levels, rows, cols = stacked.shape
    d_rows, d_cols = direction.shape

    from_left = lax.ppermute(high_packet, "gx", shift_pairs(n_x, 1))
    from_right = lax.ppermute(low_packet, "gx", shift_pairs(n_x, -1))
    y_left = lax.ppermute(stacked[:, :, :, cols - 1:], "gy", shift_pairs(n_y, 1))
    y_right = lax.ppermute(stacked[:, :, :, :1], "gy", shift_pairs(n_y, -1))
    if n_z == 2:
        got = lax.ppermute(z_sent, "gz", [(0, 1), (1, 0)])
        zero = jnp.zeros_like(got)
        z_low = jnp.where(i_z == 1, got, zero)
        z_high = jnp.where(i_z == 0, got, zero)
    else:
        z_low = lax.ppermute(stacked[:, levels - 1:], "gz", shift_pairs(n_z, 1))
        z_high = lax.ppermute(stacked[:, :1], "gz", shift_pairs(n_z, -1))

    x_low = from_left[: fields * levels].reshape(fields, levels, 1, cols)
    x_high = from_right[: fields * levels].reshape(fields, levels, 1, cols)
    d_low = from_left[fields * levels:, :d_cols]
    d_high = from_right[fields * levels:, :d_cols]

    d_ext = jnp.concatenate([d_low, direction, d_high], axis=0)
    padded = jnp.concatenate([y_left, stacked, y_right], axis=3)
    pad_y = ((0, 0), (0, 0), (0, 0), (1, 1))
    padded = jnp.concatenate(
        [jnp.pad(x_low, pad_y), padded, jnp.pad(x_high, pad_y)], axis=2
    )
    pad_xy = ((0, 0), (0, 0), (1, 1), (1, 1))
    padded = jnp.concatenate(
        [jnp.pad(z_low, pad_xy), padded, jnp.pad(z_high, pad_xy)], axis=1
    )
    applied = stencil(padded[:3], padded[3])
    stokes_image = apply_blocks(blocks, applied, True)
    partial_value = jnp.sum(stokes_image * adjoint, axis=(0, 1))

    own_width = cols // n_z
    if n_z == 2:
        sent = lax.dynamic_slice_in_dim(partial_value, (1 - i_z) * own_width, own_width, axis=1)
        mine = lax.dynamic_slice_in_dim(partial_value, i_z * own_width, own_width, axis=1)
        d_partner = lax.dynamic_slice_in_dim(d_ext, (1 - i_z) * (d_cols - 2), 2, axis=1)
        d_across = lax.dynamic_slice_in_dim(d_ext, i_z * (d_cols - 2), 2, axis=1)
        flat = d_partner.reshape(1, -1)
        packet = jnp.concatenate(
            [sent, jnp.pad(flat, ((0, 0), (0, own_width - flat.shape[1])))], axis=0
        )
        packet, d_across = lax.optimization_barrier((packet, d_across))
        got = lax.ppermute(packet, "gz", [(0, 1), (1, 0)])
        across_pairs = []
        for block in range(n_y - 1):
            across_pairs += [(2 * block + 1, 2 * block + 2), (2 * block + 2, 2 * block + 1)]
        got_across = lax.ppermute(d_across, ("gy", "gz"), across_pairs)
        column = mine + got[: sent.shape[0]]
        got_partner = got[sent.shape[0], : flat.shape[1]].reshape(d_partner.shape)
        d_left = jnp.where(i_z == 0, got_across, got_partner)
        d_right = jnp.where(i_z == 0, got_partner, got_across)
    else:
        column = lax.psum_scatter(partial_value, "gz", scatter_dimension=1, tiled=True)
        d_left = lax.ppermute(d_ext[:, d_cols - 2:], ("gy", "gz"), shift_pairs(n_col, 1))
        d_right = lax.ppermute(d_ext[:, :2], ("gy", "gz"), shift_pairs(n_col, -1))

    d_full = jnp.concatenate([d_left, d_ext, d_right], axis=1)
    inner = laplace(d_full)
    row_ids = lax.broadcasted_iota(jnp.int32, inner.shape, 0)
    col_ids = lax.broadcasted_iota(jnp.int32, inner.shape, 1)
    outside = (
        ((row_ids == 0) & (i_x == 0))
        | ((row_ids == inner.shape[0] - 1) & (i_x == n_x - 1))
        | ((col_ids == 0) & (i_col == 0))
        | ((col_ids == inner.shape[1] - 1) & (i_col == n_col - 1))
    )
    inner = jnp.where(outside, 0.0, inner)
    bilaplace = laplace(inner)
    hessian_dir = reg_weight * bilaplace + basal_mask.astype(jnp.float32) * (
        jnp.exp(friction) * column
    )
    return (stokes_image, hessian_dir)


def solution(mesh):
    return jax.shard_map(
        local,
        mesh=mesh,
        in_specs=(
            P(None, "gz", "gx", "gy"),
            P(None, "gz", "gx", "gy"),
            P("gz", "gx", "gy"),
            P("gx", "gy"),
            P("gx", "gy"),
            P(),
            P("gx", ("gy", "gz")),
            P("gx", ("gy", "gz")),
            P("gx", ("gy", "gz")),
        ),
        out_specs=(P(None, "gz", "gx", "gy"), P("gx", ("gy", "gz"))),
        check_vma=False,
    )
```

```python
import jax
import jax.numpy as jnp
from jax import lax
from jax.sharding import PartitionSpec as P
from jax.experimental import pallas as pl
from jax.experimental.pallas import tpu as pltpu


reg_weight = 0.05


def shift_pairs(count, step):
    if step > 0:
        return [(i, i + 1) for i in range(count - 1)]
    return [(i + 1, i) for i in range(count - 1)]


def prologue_kernel(
    vel_hbm, visc_hbm, flags_hbm, index_hbm, table_hbm, dir_hbm,
    stacked_ref, blocks_ref, low_ref, high_ref, level_ref, y_low_ref, y_high_ref,
    vel_v, visc_v, flags_v, index_v, table_s, dir_v, sems,
):
    pairs = [
        (vel_hbm, vel_v), (visc_hbm, visc_v), (flags_hbm, flags_v),
        (index_hbm, index_v), (table_hbm, table_s), (dir_hbm, dir_v),
    ]
    copies = [pltpu.make_async_copy(s, d, sems.at[i]) for i, (s, d) in enumerate(pairs)]
    for copy in copies:
        copy.start()
    for copy in copies:
        copy.wait()
    index = index_v[...]
    hanging = flags_v[...] != 0
    count = table_s.shape[0] // 9
    blocks = []
    for j in range(9):
        base = (j // 3) * 3 * count + (j % 3) * count
        entry = jnp.full(index.shape, table_s[base], jnp.float32)
        for number in range(1, count):
            entry = jnp.where(index == number, table_s[base + number], entry)
        entry = jnp.where(hanging, entry, 1.0 if j % 4 == 0 else 0.0)
        blocks_ref[j] = entry
        blocks.append(entry)
    groups = index.shape[1]
    fields, levels, rows, cols = stacked_ref.shape
    for c in range(fields - 1):
        for z in range(levels):
            slots = [vel_v[c, z, :, k * groups:(k + 1) * groups] for k in range(3)]
            for m in range(3):
                total = blocks[m * 3] * slots[0]
                total = total + blocks[m * 3 + 1] * slots[1]
                total = total + blocks[m * 3 + 2] * slots[2]
                stacked_ref[c, z, :, m * groups:(m + 1) * groups] = total
    stacked_ref[fields - 1] = visc_v[...]
    for f in range(fields):
        for z in range(levels):
            row = f * levels + z
            low_ref[row:row + 1, :] = stacked_ref[f, z, 0:1, :]
            high_ref[row:row + 1, :] = stacked_ref[f, z, rows - 1:rows, :]
    for f in range(fields):
        for z in range(levels):
            y_low_ref[f, z] = stacked_ref[f, z, :, 0:1]
            y_high_ref[f, z] = stacked_ref[f, z, :, cols - 1:cols]
    if lax.axis_size("gz") == 2:
        level = (1 - lax.axis_index("gz")) * (levels - 1)
        level_ref[...] = stacked_ref[:, pl.ds(level, 1)]
    else:
        level_ref[...] = stacked_ref[:, 0:1]
    d_rows, d_cols = dir_v.shape
    edge = fields * levels
    low_ref[edge:, :] = jnp.zeros((2, cols), jnp.float32)
    high_ref[edge:, :] = jnp.zeros((2, cols), jnp.float32)
    low_ref[edge:, 0:d_cols] = dir_v[0:2, :]
    high_ref[edge:, 0:d_cols] = dir_v[d_rows - 2:, :]


def prologue(velocity, viscosity, hang_flags, hang_index, block_table, direction):
    fields = velocity.shape[0] + 1
    stack_shape = (fields,) + viscosity.shape
    packet = (fields * viscosity.shape[0] + 2, viscosity.shape[2])
    table = jnp.transpose(block_table.astype(jnp.float32), (1, 2, 0)).reshape(-1)
    f32 = jnp.float32
    anywhere = pl.BlockSpec(memory_space=pl.ANY)
    in_vmem = pl.BlockSpec(memory_space=pltpu.VMEM)
    return pl.pallas_call(
        prologue_kernel,
        out_shape=(
            jax.ShapeDtypeStruct(stack_shape, f32),
            jax.ShapeDtypeStruct((9,) + hang_index.shape, f32),
            jax.ShapeDtypeStruct(packet, f32),
            jax.ShapeDtypeStruct(packet, f32),
            jax.ShapeDtypeStruct((fields, 1) + viscosity.shape[1:], f32),
            jax.ShapeDtypeStruct(stack_shape[:3] + (1,), f32),
            jax.ShapeDtypeStruct(stack_shape[:3] + (1,), f32),
        ),
        in_specs=[anywhere] * 6,
        out_specs=(in_vmem,) * 7,
        scratch_shapes=[
            pltpu.VMEM(velocity.shape, f32),
            pltpu.VMEM(viscosity.shape, f32),
            pltpu.VMEM(hang_flags.shape, jnp.int32),
            pltpu.VMEM(hang_index.shape, jnp.int32),
            pltpu.SMEM(table.shape, f32),
            pltpu.VMEM(direction.shape, f32),
            pltpu.SemaphoreType.DMA((6,)),
        ],
        cost_estimate=pl.CostEstimate(
            flops=200000, transcendentals=0, bytes_accessed=300000
        ),
    )(velocity, viscosity, hang_flags, hang_index, table, direction)


def block_matrices(hang_flags, hang_index, block_table):
    count = block_table.shape[0]
    numbers = lax.broadcasted_iota(jnp.int32, (count,) + hang_index.shape, 0)
    one_hot = (hang_index[None] == numbers).astype(jnp.float32)
    table = block_table.astype(jnp.float32).reshape(count, 9)
    chosen = lax.dot_general(
        table, one_hot, (((0,), (0,)), ((), ())), precision=lax.Precision.HIGHEST
    )
    identity = jnp.eye(3, dtype=jnp.float32).reshape(9)[:, None, None]
    blocks = jnp.where(hang_flags[None] != 0, chosen, identity)
    return [[blocks[m * 3 + k] for k in range(3)] for m in range(3)]


def apply_blocks(blocks, field, transpose):
    groups = field.shape[-1] // 3
    slots = [field[..., k * groups:(k + 1) * groups] for k in range(3)]
    mixed = []
    for m in range(3):
        total = None
        for k in range(3):
            weight = blocks[k][m] if transpose else blocks[m][k]
            term = weight * slots[k]
            total = term if total is None else total + term
        mixed.append(total)
    return jnp.concatenate(mixed, axis=-1)


def shifted(padded, spatial, offset):
    lead = padded.ndim - 3
    index = [slice(None)] * lead + [slice(1, -1)] * 3
    if offset == 1:
        index[lead + spatial] = slice(2, None)
    elif offset == -1:
        index[lead + spatial] = slice(None, -2)
    return padded[tuple(index)]


def stencil(padded_vel, padded_visc):
    centre_vel = shifted(padded_vel, 0, 0)
    centre_visc = shifted(padded_visc, 0, 0)
    total = jnp.zeros(centre_vel.shape, jnp.float32)
    for spatial in range(3):
        for offset in (1, -1):
            face = 0.5 * (centre_visc + shifted(padded_visc, spatial, offset))
            total = total + face[None] * (centre_vel - shifted(padded_vel, spatial, offset))
    return total


def laplace(padded):
    return (
        4.0 * padded[1:-1, 1:-1]
        - padded[2:, 1:-1]
        - padded[:-2, 1:-1]
        - padded[1:-1, 2:]
        - padded[1:-1, :-2]
    )


def local(
    velocity,
    adjoint,
    viscosity,
    hang_flags,
    hang_index,
    block_table,
    friction,
    basal_mask,
    direction,
):
    n_x = lax.axis_size("gx")
    n_y = lax.axis_size("gy")
    n_z = lax.axis_size("gz")
    i_x = lax.axis_index("gx")
    i_z = lax.axis_index("gz")
    n_col = n_y * n_z
    i_col = lax.axis_index("gy") * n_z + i_z

    stacked, table9, low_packet, high_packet, z_sent, y_low_edge, y_high_edge = prologue(
        velocity, viscosity, hang_flags, hang_index, block_table, direction
    )
    blocks = [[table9[m * 3 + k] for k in range(3)] for m in range(3)]
    fields, levels, rows, cols = stacked.shape
    d_rows, d_cols = direction.shape

    from_left = lax.ppermute(high_packet, "gx", shift_pairs(n_x, 1))
    from_right = lax.ppermute(low_packet, "gx", shift_pairs(n_x, -1))
    y_left = lax.ppermute(y_high_edge, "gy", shift_pairs(n_y, 1))
    y_right = lax.ppermute(y_low_edge, "gy", shift_pairs(n_y, -1))
    if n_z == 2:
        got = lax.ppermute(z_sent, "gz", [(0, 1), (1, 0)])
        zero = jnp.zeros_like(got)
        z_low = jnp.where(i_z == 1, got, zero)
        z_high = jnp.where(i_z == 0, got, zero)
    else:
        z_low = lax.ppermute(stacked[:, levels - 1:], "gz", shift_pairs(n_z, 1))
        z_high = lax.ppermute(stacked[:, :1], "gz", shift_pairs(n_z, -1))

    x_low = from_left[: fields * levels].reshape(fields, levels, 1, cols)
    x_high = from_right[: fields * levels].reshape(fields, levels, 1, cols)
    d_low = from_left[fields * levels:, :d_cols]
    d_high = from_right[fields * levels:, :d_cols]

    d_ext = jnp.concatenate([d_low, direction, d_high], axis=0)
    padded = jnp.concatenate([y_left, stacked, y_right], axis=3)
    pad_y = ((0, 0), (0, 0), (0, 0), (1, 1))
    padded = jnp.concatenate(
        [jnp.pad(x_low, pad_y), padded, jnp.pad(x_high, pad_y)], axis=2
    )
    pad_xy = ((0, 0), (0, 0), (1, 1), (1, 1))
    padded = jnp.concatenate(
        [jnp.pad(z_low, pad_xy), padded, jnp.pad(z_high, pad_xy)], axis=1
    )
    applied = stencil(padded[:3], padded[3])
    stokes_image = apply_blocks(blocks, applied, True)
    partial_value = jnp.sum(stokes_image * adjoint, axis=(0, 1))

    own_width = cols // n_z
    if n_z == 2:
        sent = lax.dynamic_slice_in_dim(partial_value, (1 - i_z) * own_width, own_width, axis=1)
        mine = lax.dynamic_slice_in_dim(partial_value, i_z * own_width, own_width, axis=1)
        d_partner = lax.dynamic_slice_in_dim(d_ext, (1 - i_z) * (d_cols - 2), 2, axis=1)
        d_across = lax.dynamic_slice_in_dim(d_ext, i_z * (d_cols - 2), 2, axis=1)
        flat = d_partner.reshape(1, -1)
        packet = jnp.concatenate(
            [sent, jnp.pad(flat, ((0, 0), (0, own_width - flat.shape[1])))], axis=0
        )
        packet, d_across = lax.optimization_barrier((packet, d_across))
        got = lax.ppermute(packet, "gz", [(0, 1), (1, 0)])
        across_pairs = []
        for block in range(n_y - 1):
            across_pairs += [(2 * block + 1, 2 * block + 2), (2 * block + 2, 2 * block + 1)]
        got_across = lax.ppermute(d_across, ("gy", "gz"), across_pairs)
        column = mine + got[: sent.shape[0]]
        got_partner = got[sent.shape[0], : flat.shape[1]].reshape(d_partner.shape)
        d_left = jnp.where(i_z == 0, got_across, got_partner)
        d_right = jnp.where(i_z == 0, got_partner, got_across)
    else:
        column = lax.psum_scatter(partial_value, "gz", scatter_dimension=1, tiled=True)
        d_left = lax.ppermute(d_ext[:, d_cols - 2:], ("gy", "gz"), shift_pairs(n_col, 1))
        d_right = lax.ppermute(d_ext[:, :2], ("gy", "gz"), shift_pairs(n_col, -1))

    d_full = jnp.concatenate([d_left, d_ext, d_right], axis=1)
    inner = laplace(d_full)
    row_ids = lax.broadcasted_iota(jnp.int32, inner.shape, 0)
    col_ids = lax.broadcasted_iota(jnp.int32, inner.shape, 1)
    outside = (
        ((row_ids == 0) & (i_x == 0))
        | ((row_ids == inner.shape[0] - 1) & (i_x == n_x - 1))
        | ((col_ids == 0) & (i_col == 0))
        | ((col_ids == inner.shape[1] - 1) & (i_col == n_col - 1))
    )
    inner = jnp.where(outside, 0.0, inner)
    bilaplace = laplace(inner)
    hessian_dir = reg_weight * bilaplace + basal_mask.astype(jnp.float32) * (
        jnp.exp(friction) * column
    )
    return (stokes_image, hessian_dir)


def solution(mesh):
    return jax.shard_map(
        local,
        mesh=mesh,
        in_specs=(
            P(None, "gz", "gx", "gy"),
            P(None, "gz", "gx", "gy"),
            P("gz", "gx", "gy"),
            P("gx", "gy"),
            P("gx", "gy"),
            P(),
            P("gx", ("gy", "gz")),
            P("gx", ("gy", "gz")),
            P("gx", ("gy", "gz")),
        ),
        out_specs=(P(None, "gz", "gx", "gy"), P("gx", ("gy", "gz"))),
        check_vma=False,
    )
```

```python
import jax
import jax.numpy as jnp
from jax import lax
from jax.sharding import PartitionSpec as P
from jax.experimental import pallas as pl
from jax.experimental.pallas import tpu as pltpu


reg_weight = 0.05


def shift_pairs(count, step):
    if step > 0:
        return [(i, i + 1) for i in range(count - 1)]
    return [(i + 1, i) for i in range(count - 1)]


def prologue_kernel(
    vel_hbm, visc_hbm, flags_hbm, index_hbm, table_hbm, dir_hbm,
    stacked_ref, blocks_ref, low_ref, high_ref,
    vel_v, visc_v, flags_v, index_v, table_s, dir_v, sems,
):
    pairs = [
        (vel_hbm, vel_v), (visc_hbm, visc_v), (flags_hbm, flags_v),
        (index_hbm, index_v), (table_hbm, table_s), (dir_hbm, dir_v),
    ]
    copies = [pltpu.make_async_copy(s, d, sems.at[i]) for i, (s, d) in enumerate(pairs)]
    for copy in copies:
        copy.start()
    for copy in copies:
        copy.wait()
    index = index_v[...]
    hanging = flags_v[...] != 0
    count = table_s.shape[0] // 9
    blocks = []
    for j in range(9):
        entry = jnp.full(index.shape, table_s[j], jnp.float32)
        for number in range(1, count):
            entry = jnp.where(index == number, table_s[number * 9 + j], entry)
        entry = jnp.where(hanging, entry, 1.0 if j % 4 == 0 else 0.0)
        blocks_ref[j] = entry
        blocks.append(entry)
    groups = index.shape[1]
    fields, levels, rows, cols = stacked_ref.shape
    for c in range(fields - 1):
        for z in range(levels):
            slots = [vel_v[c, z, :, k * groups:(k + 1) * groups] for k in range(3)]
            for m in range(3):
                total = blocks[m * 3] * slots[0]
                total = total + blocks[m * 3 + 1] * slots[1]
                total = total + blocks[m * 3 + 2] * slots[2]
                stacked_ref[c, z, :, m * groups:(m + 1) * groups] = total
    stacked_ref[fields - 1] = visc_v[...]
    for f in range(fields):
        for z in range(levels):
            row = f * levels + z
            low_ref[row:row + 1, :] = stacked_ref[f, z, 0:1, :]
            high_ref[row:row + 1, :] = stacked_ref[f, z, rows - 1:rows, :]
    d_rows, d_cols = dir_v.shape
    edge = fields * levels
    low_ref[edge:, :] = jnp.zeros((2, cols), jnp.float32)
    high_ref[edge:, :] = jnp.zeros((2, cols), jnp.float32)
    low_ref[edge:, 0:d_cols] = dir_v[0:2, :]
    high_ref[edge:, 0:d_cols] = dir_v[d_rows - 2:, :]


def prologue(velocity, viscosity, hang_flags, hang_index, block_table, direction):
    fields = velocity.shape[0] + 1
    stack_shape = (fields,) + viscosity.shape
    packet = (fields * viscosity.shape[0] + 2, viscosity.shape[2])
    table = block_table.astype(jnp.float32).reshape(-1)
    f32 = jnp.float32
    anywhere = pl.BlockSpec(memory_space=pl.ANY)
    in_vmem = pl.BlockSpec(memory_space=pltpu.VMEM)
    return pl.pallas_call(
        prologue_kernel,
        out_shape=(
            jax.ShapeDtypeStruct(stack_shape, f32),
            jax.ShapeDtypeStruct((9,) + hang_index.shape, f32),
            jax.ShapeDtypeStruct(packet, f32),
            jax.ShapeDtypeStruct(packet, f32),
        ),
        in_specs=[anywhere] * 6,
        out_specs=(in_vmem,) * 4,
        scratch_shapes=[
            pltpu.VMEM(velocity.shape, f32),
            pltpu.VMEM(viscosity.shape, f32),
            pltpu.VMEM(hang_flags.shape, jnp.int32),
            pltpu.VMEM(hang_index.shape, jnp.int32),
            pltpu.SMEM(table.shape, f32),
            pltpu.VMEM(direction.shape, f32),
            pltpu.SemaphoreType.DMA((6,)),
        ],
        cost_estimate=pl.CostEstimate(
            flops=200000, transcendentals=0, bytes_accessed=300000
        ),
    )(velocity, viscosity, hang_flags, hang_index, table, direction)


def block_matrices(hang_flags, hang_index, block_table):
    count = block_table.shape[0]
    numbers = lax.broadcasted_iota(jnp.int32, (count,) + hang_index.shape, 0)
    one_hot = (hang_index[None] == numbers).astype(jnp.float32)
    table = block_table.astype(jnp.float32).reshape(count, 9)
    chosen = lax.dot_general(
        table, one_hot, (((0,), (0,)), ((), ())), precision=lax.Precision.HIGHEST
    )
    identity = jnp.eye(3, dtype=jnp.float32).reshape(9)[:, None, None]
    blocks = jnp.where(hang_flags[None] != 0, chosen, identity)
    return [[blocks[m * 3 + k] for k in range(3)] for m in range(3)]


def apply_blocks(blocks, field, transpose):
    groups = field.shape[-1] // 3
    slots = [field[..., k * groups:(k + 1) * groups] for k in range(3)]
    mixed = []
    for m in range(3):
        total = None
        for k in range(3):
            weight = blocks[k][m] if transpose else blocks[m][k]
            term = weight * slots[k]
            total = term if total is None else total + term
        mixed.append(total)
    return jnp.concatenate(mixed, axis=-1)


def shifted(padded, spatial, offset):
    lead = padded.ndim - 3
    index = [slice(None)] * lead + [slice(1, -1)] * 3
    if offset == 1:
        index[lead + spatial] = slice(2, None)
    elif offset == -1:
        index[lead + spatial] = slice(None, -2)
    return padded[tuple(index)]


def stencil(padded_vel, padded_visc):
    centre_vel = shifted(padded_vel, 0, 0)
    centre_visc = shifted(padded_visc, 0, 0)
    total = jnp.zeros(centre_vel.shape, jnp.float32)
    for spatial in range(3):
        for offset in (1, -1):
            face = 0.5 * (centre_visc + shifted(padded_visc, spatial, offset))
            total = total + face[None] * (centre_vel - shifted(padded_vel, spatial, offset))
    return total


def laplace(padded):
    return (
        4.0 * padded[1:-1, 1:-1]
        - padded[2:, 1:-1]
        - padded[:-2, 1:-1]
        - padded[1:-1, 2:]
        - padded[1:-1, :-2]
    )


def local(
    velocity,
    adjoint,
    viscosity,
    hang_flags,
    hang_index,
    block_table,
    friction,
    basal_mask,
    direction,
):
    n_x = lax.axis_size("gx")
    n_y = lax.axis_size("gy")
    n_z = lax.axis_size("gz")
    i_x = lax.axis_index("gx")
    i_z = lax.axis_index("gz")
    n_col = n_y * n_z
    i_col = lax.axis_index("gy") * n_z + i_z

    stacked, table9, low_packet, high_packet = prologue(
        velocity, viscosity, hang_flags, hang_index, block_table, direction
    )
    blocks = [[table9[m * 3 + k] for k in range(3)] for m in range(3)]
    fields, levels, rows, cols = stacked.shape
    d_rows, d_cols = direction.shape

    from_left = lax.ppermute(high_packet, "gx", shift_pairs(n_x, 1))
    from_right = lax.ppermute(low_packet, "gx", shift_pairs(n_x, -1))
    y_left = lax.ppermute(stacked[:, :, :, cols - 1:], "gy", shift_pairs(n_y, 1))
    y_right = lax.ppermute(stacked[:, :, :, :1], "gy", shift_pairs(n_y, -1))
    if n_z == 2:
        sent = lax.dynamic_slice_in_dim(stacked, (1 - i_z) * (levels - 1), 1, axis=1)
        both = lax.all_to_all(jnp.stack([sent, sent]), "gz", 0, 0)
        got = lax.dynamic_index_in_dim(both, 1 - i_z, axis=0, keepdims=False)
        zero = jnp.zeros_like(got)
        z_low = jnp.where(i_z == 1, got, zero)
        z_high = jnp.where(i_z == 0, got, zero)
    else:
        z_low = lax.ppermute(stacked[:, levels - 1:], "gz", shift_pairs(n_z, 1))
        z_high = lax.ppermute(stacked[:, :1], "gz", shift_pairs(n_z, -1))

    x_low = from_left[: fields * levels].reshape(fields, levels, 1, cols)
    x_high = from_right[: fields * levels].reshape(fields, levels, 1, cols)
    d_low = from_left[fields * levels:, :d_cols]
    d_high = from_right[fields * levels:, :d_cols]

    d_ext = jnp.concatenate([d_low, direction, d_high], axis=0)
    padded = jnp.concatenate([y_left, stacked, y_right], axis=3)
    pad_y = ((0, 0), (0, 0), (0, 0), (1, 1))
    padded = jnp.concatenate(
        [jnp.pad(x_low, pad_y), padded, jnp.pad(x_high, pad_y)], axis=2
    )
    pad_xy = ((0, 0), (0, 0), (1, 1), (1, 1))
    padded = jnp.concatenate(
        [jnp.pad(z_low, pad_xy), padded, jnp.pad(z_high, pad_xy)], axis=1
    )
    applied = stencil(padded[:3], padded[3])
    stokes_image = apply_blocks(blocks, applied, True)
    partial_value = jnp.sum(stokes_image * adjoint, axis=(0, 1))

    own_width = cols // n_z
    if n_z == 2:
        sent = lax.dynamic_slice_in_dim(partial_value, (1 - i_z) * own_width, own_width, axis=1)
        mine = lax.dynamic_slice_in_dim(partial_value, i_z * own_width, own_width, axis=1)
        d_partner = lax.dynamic_slice_in_dim(d_ext, (1 - i_z) * (d_cols - 2), 2, axis=1)
        d_across = lax.dynamic_slice_in_dim(d_ext, i_z * (d_cols - 2), 2, axis=1)
        flat = d_partner.reshape(1, -1)
        packet = jnp.concatenate(
            [sent, jnp.pad(flat, ((0, 0), (0, own_width - flat.shape[1])))], axis=0
        )
        halves = jnp.stack([partial_value[:, :own_width], partial_value[:, own_width:]])
        extra = jnp.broadcast_to(
            jnp.pad(flat, ((0, 0), (0, own_width - flat.shape[1])))[None], (2, 1, own_width)
        )
        packets = jnp.concatenate([halves, extra], axis=1)
        packets, d_across = lax.optimization_barrier((packets, d_across))
        came = lax.all_to_all(packets, "gz", 0, 0)
        got = lax.dynamic_index_in_dim(came, 1 - i_z, axis=0, keepdims=False)
        across_pairs = []
        for block in range(n_y - 1):
            across_pairs += [(2 * block + 1, 2 * block + 2), (2 * block + 2, 2 * block + 1)]
        got_across = lax.ppermute(d_across, ("gy", "gz"), across_pairs)
        column = came[0, : sent.shape[0]] + came[1, : sent.shape[0]]
        got_partner = got[sent.shape[0], : flat.shape[1]].reshape(d_partner.shape)
        d_left = jnp.where(i_z == 0, got_across, got_partner)
        d_right = jnp.where(i_z == 0, got_partner, got_across)
    else:
        column = lax.psum_scatter(partial_value, "gz", scatter_dimension=1, tiled=True)
        d_left = lax.ppermute(d_ext[:, d_cols - 2:], ("gy", "gz"), shift_pairs(n_col, 1))
        d_right = lax.ppermute(d_ext[:, :2], ("gy", "gz"), shift_pairs(n_col, -1))

    d_full = jnp.concatenate([d_left, d_ext, d_right], axis=1)
    inner = laplace(d_full)
    row_ids = lax.broadcasted_iota(jnp.int32, inner.shape, 0)
    col_ids = lax.broadcasted_iota(jnp.int32, inner.shape, 1)
    outside = (
        ((row_ids == 0) & (i_x == 0))
        | ((row_ids == inner.shape[0] - 1) & (i_x == n_x - 1))
        | ((col_ids == 0) & (i_col == 0))
        | ((col_ids == inner.shape[1] - 1) & (i_col == n_col - 1))
    )
    inner = jnp.where(outside, 0.0, inner)
    bilaplace = laplace(inner)
    hessian_dir = reg_weight * bilaplace + basal_mask.astype(jnp.float32) * (
        jnp.exp(friction) * column
    )
    return (stokes_image, hessian_dir)


def solution(mesh):
    return jax.shard_map(
        local,
        mesh=mesh,
        in_specs=(
            P(None, "gz", "gx", "gy"),
            P(None, "gz", "gx", "gy"),
            P("gz", "gx", "gy"),
            P("gx", "gy"),
            P("gx", "gy"),
            P(),
            P("gx", ("gy", "gz")),
            P("gx", ("gy", "gz")),
            P("gx", ("gy", "gz")),
        ),
        out_specs=(P(None, "gz", "gx", "gy"), P("gx", ("gy", "gz"))),
        check_vma=False,
    )
```

```python
import jax
import jax.numpy as jnp
from jax import lax
from jax.sharding import PartitionSpec as P
from jax.experimental import pallas as pl
from jax.experimental.pallas import tpu as pltpu


reg_weight = 0.05


def shift_pairs(count, step):
    if step > 0:
        return [(i, i + 1) for i in range(count - 1)]
    return [(i + 1, i) for i in range(count - 1)]


def prologue_kernel(
    vel_hbm, visc_hbm, flags_hbm, index_hbm, table_hbm, dir_hbm,
    stacked_ref, blocks_ref, low_ref, high_ref,
    vel_v, visc_v, flags_v, index_v, table_s, dir_v, sems,
):
    pairs = [
        (vel_hbm, vel_v), (visc_hbm, visc_v), (flags_hbm, flags_v),
        (index_hbm, index_v), (table_hbm, table_s), (dir_hbm, dir_v),
    ]
    copies = [pltpu.make_async_copy(s, d, sems.at[i]) for i, (s, d) in enumerate(pairs)]
    for copy in copies:
        copy.start()
    for copy in copies:
        copy.wait()
    index = index_v[...]
    hanging = flags_v[...] != 0
    count = table_s.shape[0] // 9
    blocks = []
    for j in range(9):
        entry = jnp.full(index.shape, table_s[j], jnp.float32)
        for number in range(1, count):
            entry = jnp.where(index == number, table_s[number * 9 + j], entry)
        entry = jnp.where(hanging, entry, 1.0 if j % 4 == 0 else 0.0)
        blocks_ref[j] = entry
        blocks.append(entry)
    groups = index.shape[1]
    fields, levels, rows, cols = stacked_ref.shape
    for c in range(fields - 1):
        for z in range(levels):
            slots = [vel_v[c, z, :, k * groups:(k + 1) * groups] for k in range(3)]
            for m in range(3):
                total = blocks[m * 3] * slots[0]
                total = total + blocks[m * 3 + 1] * slots[1]
                total = total + blocks[m * 3 + 2] * slots[2]
                stacked_ref[c, z, :, m * groups:(m + 1) * groups] = total
    stacked_ref[fields - 1] = visc_v[...]
    for f in range(fields):
        for z in range(levels):
            row = f * levels + z
            low_ref[row:row + 1, :] = stacked_ref[f, z, 0:1, :]
            high_ref[row:row + 1, :] = stacked_ref[f, z, rows - 1:rows, :]
    d_rows, d_cols = dir_v.shape
    edge = fields * levels
    low_ref[edge:, :] = jnp.zeros((2, cols), jnp.float32)
    high_ref[edge:, :] = jnp.zeros((2, cols), jnp.float32)
    low_ref[edge:, 0:d_cols] = dir_v[0:2, :]
    high_ref[edge:, 0:d_cols] = dir_v[d_rows - 2:, :]


def prologue(velocity, viscosity, hang_flags, hang_index, block_table, direction):
    fields = velocity.shape[0] + 1
    stack_shape = (fields,) + viscosity.shape
    packet = (fields * viscosity.shape[0] + 2, viscosity.shape[2])
    table = block_table.astype(jnp.float32).reshape(-1)
    f32 = jnp.float32
    anywhere = pl.BlockSpec(memory_space=pl.ANY)
    in_vmem = pl.BlockSpec(memory_space=pltpu.VMEM)
    return pl.pallas_call(
        prologue_kernel,
        out_shape=(
            jax.ShapeDtypeStruct(stack_shape, f32),
            jax.ShapeDtypeStruct((9,) + hang_index.shape, f32),
            jax.ShapeDtypeStruct(packet, f32),
            jax.ShapeDtypeStruct(packet, f32),
        ),
        in_specs=[anywhere] * 6,
        out_specs=(in_vmem,) * 4,
        scratch_shapes=[
            pltpu.VMEM(velocity.shape, f32),
            pltpu.VMEM(viscosity.shape, f32),
            pltpu.VMEM(hang_flags.shape, jnp.int32),
            pltpu.VMEM(hang_index.shape, jnp.int32),
            pltpu.SMEM(table.shape, f32),
            pltpu.VMEM(direction.shape, f32),
            pltpu.SemaphoreType.DMA((6,)),
        ],
        cost_estimate=pl.CostEstimate(
            flops=200000, transcendentals=0, bytes_accessed=300000
        ),
    )(velocity, viscosity, hang_flags, hang_index, table, direction)


def block_matrices(hang_flags, hang_index, block_table):
    count = block_table.shape[0]
    numbers = lax.broadcasted_iota(jnp.int32, (count,) + hang_index.shape, 0)
    one_hot = (hang_index[None] == numbers).astype(jnp.float32)
    table = block_table.astype(jnp.float32).reshape(count, 9)
    chosen = lax.dot_general(
        table, one_hot, (((0,), (0,)), ((), ())), precision=lax.Precision.HIGHEST
    )
    identity = jnp.eye(3, dtype=jnp.float32).reshape(9)[:, None, None]
    blocks = jnp.where(hang_flags[None] != 0, chosen, identity)
    return [[blocks[m * 3 + k] for k in range(3)] for m in range(3)]


def apply_blocks(blocks, field, transpose):
    groups = field.shape[-1] // 3
    slots = [field[..., k * groups:(k + 1) * groups] for k in range(3)]
    mixed = []
    for m in range(3):
        total = None
        for k in range(3):
            weight = blocks[k][m] if transpose else blocks[m][k]
            term = weight * slots[k]
            total = term if total is None else total + term
        mixed.append(total)
    return jnp.concatenate(mixed, axis=-1)


def shifted(padded, spatial, offset):
    lead = padded.ndim - 3
    index = [slice(None)] * lead + [slice(1, -1)] * 3
    if offset == 1:
        index[lead + spatial] = slice(2, None)
    elif offset == -1:
        index[lead + spatial] = slice(None, -2)
    return padded[tuple(index)]


def stencil(padded_vel, padded_visc):
    centre_vel = shifted(padded_vel, 0, 0)
    centre_visc = shifted(padded_visc, 0, 0)
    total = jnp.zeros(centre_vel.shape, jnp.float32)
    for spatial in range(3):
        for offset in (1, -1):
            face = 0.5 * (centre_visc + shifted(padded_visc, spatial, offset))
            total = total + face[None] * (centre_vel - shifted(padded_vel, spatial, offset))
    return total


def laplace(padded):
    return (
        4.0 * padded[1:-1, 1:-1]
        - padded[2:, 1:-1]
        - padded[:-2, 1:-1]
        - padded[1:-1, 2:]
        - padded[1:-1, :-2]
    )


def local(
    velocity,
    adjoint,
    viscosity,
    hang_flags,
    hang_index,
    block_table,
    friction,
    basal_mask,
    direction,
):
    n_x = lax.axis_size("gx")
    n_y = lax.axis_size("gy")
    n_z = lax.axis_size("gz")
    i_x = lax.axis_index("gx")
    i_z = lax.axis_index("gz")
    n_col = n_y * n_z
    i_col = lax.axis_index("gy") * n_z + i_z

    stacked, table9, low_packet, high_packet = prologue(
        velocity, viscosity, hang_flags, hang_index, block_table, direction
    )
    blocks = [[table9[m * 3 + k] for k in range(3)] for m in range(3)]
    fields, levels, rows, cols = stacked.shape
    d_rows, d_cols = direction.shape

    from_left = lax.ppermute(high_packet, "gx", shift_pairs(n_x, 1))
    from_right = lax.ppermute(low_packet, "gx", shift_pairs(n_x, -1))
    scale = basal_mask.astype(jnp.float32) * jnp.exp(friction)
    d_mid = jnp.pad(direction, ((2, 2), (0, 0)))
    y_high_edge, y_low_edge, scale, d_mid = lax.optimization_barrier(
        (stacked[:, :, :, cols - 1:], stacked[:, :, :, :1], scale, d_mid)
    )
    y_left = lax.ppermute(y_high_edge, "gy", shift_pairs(n_y, 1))
    y_right = lax.ppermute(y_low_edge, "gy", shift_pairs(n_y, -1))
    if n_z == 2:
        sent = lax.dynamic_slice_in_dim(stacked, (1 - i_z) * (levels - 1), 1, axis=1)
        got = lax.ppermute(sent, "gz", [(0, 1), (1, 0)])
        zero = jnp.zeros_like(got)
        z_low = jnp.where(i_z == 1, got, zero)
        z_high = jnp.where(i_z == 0, got, zero)
    else:
        z_low = lax.ppermute(stacked[:, levels - 1:], "gz", shift_pairs(n_z, 1))
        z_high = lax.ppermute(stacked[:, :1], "gz", shift_pairs(n_z, -1))

    x_low = from_left[: fields * levels].reshape(fields, levels, 1, cols)
    x_high = from_right[: fields * levels].reshape(fields, levels, 1, cols)
    d_low = from_left[fields * levels:, :d_cols]
    d_high = from_right[fields * levels:, :d_cols]

    d_ext = jnp.concatenate([d_low, d_mid[2:2 + d_rows], d_high], axis=0)
    padded = jnp.concatenate([y_left, stacked, y_right], axis=3)
    pad_y = ((0, 0), (0, 0), (0, 0), (1, 1))
    padded = jnp.concatenate(
        [jnp.pad(x_low, pad_y), padded, jnp.pad(x_high, pad_y)], axis=2
    )
    pad_xy = ((0, 0), (0, 0), (1, 1), (1, 1))
    padded = jnp.concatenate(
        [jnp.pad(z_low, pad_xy), padded, jnp.pad(z_high, pad_xy)], axis=1
    )
    applied = stencil(padded[:3], padded[3])
    stokes_image = apply_blocks(blocks, applied, True)
    partial_value = jnp.sum(stokes_image * adjoint, axis=(0, 1))

    own_width = cols // n_z
    if n_z == 2:
        sent = lax.dynamic_slice_in_dim(partial_value, (1 - i_z) * own_width, own_width, axis=1)
        mine = lax.dynamic_slice_in_dim(partial_value, i_z * own_width, own_width, axis=1)
        d_partner = lax.dynamic_slice_in_dim(d_ext, (1 - i_z) * (d_cols - 2), 2, axis=1)
        d_across = lax.dynamic_slice_in_dim(d_ext, i_z * (d_cols - 2), 2, axis=1)
        flat = d_partner.reshape(1, -1)
        packet = jnp.concatenate(
            [sent, jnp.pad(flat, ((0, 0), (0, own_width - flat.shape[1])))], axis=0
        )
        packet, d_across = lax.optimization_barrier((packet, d_across))
        got = lax.ppermute(packet, "gz", [(0, 1), (1, 0)])
        across_pairs = []
        for block in range(n_y - 1):
            across_pairs += [(2 * block + 1, 2 * block + 2), (2 * block + 2, 2 * block + 1)]
        got_across = lax.ppermute(d_across, ("gy", "gz"), across_pairs)
        column = mine + got[: sent.shape[0]]
        got_partner = got[sent.shape[0], : flat.shape[1]].reshape(d_partner.shape)
        d_left = jnp.where(i_z == 0, got_across, got_partner)
        d_right = jnp.where(i_z == 0, got_partner, got_across)
    else:
        column = lax.psum_scatter(partial_value, "gz", scatter_dimension=1, tiled=True)
        d_left = lax.ppermute(d_ext[:, d_cols - 2:], ("gy", "gz"), shift_pairs(n_col, 1))
        d_right = lax.ppermute(d_ext[:, :2], ("gy", "gz"), shift_pairs(n_col, -1))

    d_full = jnp.concatenate([d_left, d_ext, d_right], axis=1)
    inner = laplace(d_full)
    row_ids = lax.broadcasted_iota(jnp.int32, inner.shape, 0)
    col_ids = lax.broadcasted_iota(jnp.int32, inner.shape, 1)
    outside = (
        ((row_ids == 0) & (i_x == 0))
        | ((row_ids == inner.shape[0] - 1) & (i_x == n_x - 1))
        | ((col_ids == 0) & (i_col == 0))
        | ((col_ids == inner.shape[1] - 1) & (i_col == n_col - 1))
    )
    inner = jnp.where(outside, 0.0, inner)
    bilaplace = laplace(inner)
    hessian_dir = reg_weight * bilaplace + scale * column
    return (stokes_image, hessian_dir)


def solution(mesh):
    return jax.shard_map(
        local,
        mesh=mesh,
        in_specs=(
            P(None, "gz", "gx", "gy"),
            P(None, "gz", "gx", "gy"),
            P("gz", "gx", "gy"),
            P("gx", "gy"),
            P("gx", "gy"),
            P(),
            P("gx", ("gy", "gz")),
            P("gx", ("gy", "gz")),
            P("gx", ("gy", "gz")),
        ),
        out_specs=(P(None, "gz", "gx", "gy"), P("gx", ("gy", "gz"))),
        check_vma=False,
    )
```

```python
import jax
import jax.numpy as jnp
from jax import lax
from jax.sharding import PartitionSpec as P
from jax.experimental import pallas as pl
from jax.experimental.pallas import tpu as pltpu


reg_weight = 0.05


def shift_pairs(count, step):
    if step > 0:
        return [(i, i + 1) for i in range(count - 1)]
    return [(i + 1, i) for i in range(count - 1)]


def prologue_kernel(
    vel_hbm, visc_hbm, flags_hbm, index_hbm, table_hbm, dir_hbm,
    stacked_ref, blocks_ref, low_ref, high_ref,
    vel_v, visc_v, flags_v, index_v, table_s, dir_v, sems,
):
    pairs = [
        (vel_hbm, vel_v), (visc_hbm, visc_v), (flags_hbm, flags_v),
        (index_hbm, index_v), (table_hbm, table_s), (dir_hbm, dir_v),
    ]
    copies = [pltpu.make_async_copy(s, d, sems.at[i]) for i, (s, d) in enumerate(pairs)]
    for copy in copies:
        copy.start()
    for copy in copies:
        copy.wait()
    index = index_v[...]
    hanging = flags_v[...] != 0
    count = table_s.shape[0] // 9
    blocks = []
    for j in range(9):
        entry = jnp.full(index.shape, table_s[j], jnp.float32)
        for number in range(1, count):
            entry = jnp.where(index == number, table_s[number * 9 + j], entry)
        entry = jnp.where(hanging, entry, 1.0 if j % 4 == 0 else 0.0)
        blocks_ref[j] = entry
        blocks.append(entry)
    groups = index.shape[1]
    fields, levels, rows, cols = stacked_ref.shape
    for c in range(fields - 1):
        for z in range(levels):
            slots = [vel_v[c, z, :, k * groups:(k + 1) * groups] for k in range(3)]
            for m in range(3):
                total = blocks[m * 3] * slots[0]
                total = total + blocks[m * 3 + 1] * slots[1]
                total = total + blocks[m * 3 + 2] * slots[2]
                stacked_ref[c, z, :, m * groups:(m + 1) * groups] = total
    stacked_ref[fields - 1] = visc_v[...]
    for f in range(fields):
        for z in range(levels):
            row = f * levels + z
            low_ref[row:row + 1, :] = stacked_ref[f, z, 0:1, :]
            high_ref[row:row + 1, :] = stacked_ref[f, z, rows - 1:rows, :]
    d_rows, d_cols = dir_v.shape
    edge = fields * levels
    low_ref[edge:, :] = jnp.zeros((2, cols), jnp.float32)
    high_ref[edge:, :] = jnp.zeros((2, cols), jnp.float32)
    low_ref[edge:, 0:d_cols] = dir_v[0:2, :]
    high_ref[edge:, 0:d_cols] = dir_v[d_rows - 2:, :]


def prologue(velocity, viscosity, hang_flags, hang_index, block_table, direction):
    fields = velocity.shape[0] + 1
    stack_shape = (fields,) + viscosity.shape
    packet = (fields * viscosity.shape[0] + 2, viscosity.shape[2])
    table = block_table.astype(jnp.float32).reshape(-1)
    f32 = jnp.float32
    anywhere = pl.BlockSpec(memory_space=pl.ANY)
    in_vmem = pl.BlockSpec(memory_space=pltpu.VMEM)
    return pl.pallas_call(
        prologue_kernel,
        out_shape=(
            jax.ShapeDtypeStruct(stack_shape, f32),
            jax.ShapeDtypeStruct((9,) + hang_index.shape, f32),
            jax.ShapeDtypeStruct(packet, f32),
            jax.ShapeDtypeStruct(packet, f32),
        ),
        in_specs=[anywhere] * 6,
        out_specs=(in_vmem,) * 4,
        scratch_shapes=[
            pltpu.VMEM(velocity.shape, f32),
            pltpu.VMEM(viscosity.shape, f32),
            pltpu.VMEM(hang_flags.shape, jnp.int32),
            pltpu.VMEM(hang_index.shape, jnp.int32),
            pltpu.SMEM(table.shape, f32),
            pltpu.VMEM(direction.shape, f32),
            pltpu.SemaphoreType.DMA((6,)),
        ],
        cost_estimate=pl.CostEstimate(
            flops=200000, transcendentals=0, bytes_accessed=300000
        ),
    )(velocity, viscosity, hang_flags, hang_index, table, direction)


def block_matrices(hang_flags, hang_index, block_table):
    count = block_table.shape[0]
    numbers = lax.broadcasted_iota(jnp.int32, (count,) + hang_index.shape, 0)
    one_hot = (hang_index[None] == numbers).astype(jnp.float32)
    table = block_table.astype(jnp.float32).reshape(count, 9)
    chosen = lax.dot_general(
        table, one_hot, (((0,), (0,)), ((), ())), precision=lax.Precision.HIGHEST
    )
    identity = jnp.eye(3, dtype=jnp.float32).reshape(9)[:, None, None]
    blocks = jnp.where(hang_flags[None] != 0, chosen, identity)
    return [[blocks[m * 3 + k] for k in range(3)] for m in range(3)]


def apply_blocks(blocks, field, transpose):
    groups = field.shape[-1] // 3
    slots = [field[..., k * groups:(k + 1) * groups] for k in range(3)]
    mixed = []
    for m in range(3):
        total = None
        for k in range(3):
            weight = blocks[k][m] if transpose else blocks[m][k]
            term = weight * slots[k]
            total = term if total is None else total + term
        mixed.append(total)
    return jnp.concatenate(mixed, axis=-1)


def shifted(padded, spatial, offset):
    lead = padded.ndim - 3
    index = [slice(None)] * lead + [slice(1, -1)] * 3
    if offset == 1:
        index[lead + spatial] = slice(2, None)
    elif offset == -1:
        index[lead + spatial] = slice(None, -2)
    return padded[tuple(index)]


def stencil(padded_vel, padded_visc):
    centre_vel = shifted(padded_vel, 0, 0)
    centre_visc = shifted(padded_visc, 0, 0)
    total = jnp.zeros(centre_vel.shape, jnp.float32)
    for spatial in range(3):
        for offset in (1, -1):
            face = 0.5 * (centre_visc + shifted(padded_visc, spatial, offset))
            total = total + face[None] * (centre_vel - shifted(padded_vel, spatial, offset))
    return total


def laplace(padded):
    return (
        4.0 * padded[1:-1, 1:-1]
        - padded[2:, 1:-1]
        - padded[:-2, 1:-1]
        - padded[1:-1, 2:]
        - padded[1:-1, :-2]
    )


def local(
    velocity,
    adjoint,
    viscosity,
    hang_flags,
    hang_index,
    block_table,
    friction,
    basal_mask,
    direction,
):
    n_x = lax.axis_size("gx")
    n_y = lax.axis_size("gy")
    n_z = lax.axis_size("gz")
    i_x = lax.axis_index("gx")
    i_z = lax.axis_index("gz")
    n_col = n_y * n_z
    i_col = lax.axis_index("gy") * n_z + i_z

    stacked, table9, low_packet, high_packet = prologue(
        velocity, viscosity, hang_flags, hang_index, block_table, direction
    )
    blocks = [[table9[m * 3 + k] for k in range(3)] for m in range(3)]
    fields, levels, rows, cols = stacked.shape
    d_rows, d_cols = direction.shape

    from_left = lax.ppermute(high_packet, "gx", shift_pairs(n_x, 1))
    from_right = lax.ppermute(low_packet, "gx", shift_pairs(n_x, -1))
    y_left = lax.ppermute(stacked[:, :, :, cols - 1:], "gy", shift_pairs(n_y, 1))
    y_right = lax.ppermute(stacked[:, :, :, :1], "gy", shift_pairs(n_y, -1))
    if n_z == 2:
        sent = lax.dynamic_slice_in_dim(stacked, (1 - i_z) * (levels - 1), 1, axis=1)
        got = lax.ppermute(sent, "gz", [(0, 1), (1, 0)])
        zero = jnp.zeros_like(got)
        z_low = jnp.where(i_z == 1, got, zero)
        z_high = jnp.where(i_z == 0, got, zero)
    else:
        z_low = lax.ppermute(stacked[:, levels - 1:], "gz", shift_pairs(n_z, 1))
        z_high = lax.ppermute(stacked[:, :1], "gz", shift_pairs(n_z, -1))

    x_low = from_left[: fields * levels].reshape(fields, levels, 1, cols)
    x_high = from_right[: fields * levels].reshape(fields, levels, 1, cols)
    d_low = from_left[fields * levels:, :d_cols]
    d_high = from_right[fields * levels:, :d_cols]

    d_ext = jnp.concatenate([d_low, direction, d_high], axis=0)
    padded = jnp.concatenate([y_left, stacked, y_right], axis=3)
    pad_y = ((0, 0), (0, 0), (0, 0), (1, 1))
    padded = jnp.concatenate(
        [jnp.pad(x_low, pad_y), padded, jnp.pad(x_high, pad_y)], axis=2
    )
    pad_xy = ((0, 0), (0, 0), (1, 1), (1, 1))
    padded = jnp.concatenate(
        [jnp.pad(z_low, pad_xy), padded, jnp.pad(z_high, pad_xy)], axis=1
    )
    applied = stencil(padded[:3], padded[3])
    stokes_image = apply_blocks(blocks, applied, True)
    partial_value = jnp.sum(stokes_image * adjoint, axis=(0, 1))

    own_width = cols // n_z
    if n_z == 2:
        sent = lax.dynamic_slice_in_dim(partial_value, (1 - i_z) * own_width, own_width, axis=1)
        mine = lax.dynamic_slice_in_dim(partial_value, i_z * own_width, own_width, axis=1)
        d_partner = lax.dynamic_slice_in_dim(d_ext, (1 - i_z) * (d_cols - 2), 2, axis=1)
        d_across = lax.dynamic_slice_in_dim(d_ext, i_z * (d_cols - 2), 2, axis=1)
        flat = d_partner.reshape(1, -1)
        packet = jnp.concatenate(
            [sent, jnp.pad(flat, ((0, 0), (0, own_width - flat.shape[1])))], axis=0
        )
        scale = basal_mask.astype(jnp.float32) * jnp.exp(friction)
        packet, d_across, scale = lax.optimization_barrier((packet, d_across, scale))
        got = lax.ppermute(packet, "gz", [(0, 1), (1, 0)])
        across_pairs = []
        for block in range(n_y - 1):
            across_pairs += [(2 * block + 1, 2 * block + 2), (2 * block + 2, 2 * block + 1)]
        got_across = lax.ppermute(d_across, ("gy", "gz"), across_pairs)
        column = mine + got[: sent.shape[0]]
        got_partner = got[sent.shape[0], : flat.shape[1]].reshape(d_partner.shape)
        d_left = jnp.where(i_z == 0, got_across, got_partner)
        d_right = jnp.where(i_z == 0, got_partner, got_across)
    else:
        column = lax.psum_scatter(partial_value, "gz", scatter_dimension=1, tiled=True)
        d_left = lax.ppermute(d_ext[:, d_cols - 2:], ("gy", "gz"), shift_pairs(n_col, 1))
        d_right = lax.ppermute(d_ext[:, :2], ("gy", "gz"), shift_pairs(n_col, -1))

    d_full = jnp.concatenate([d_left, d_ext, d_right], axis=1)
    inner = laplace(d_full)
    row_ids = lax.broadcasted_iota(jnp.int32, inner.shape, 0)
    col_ids = lax.broadcasted_iota(jnp.int32, inner.shape, 1)
    outside = (
        ((row_ids == 0) & (i_x == 0))
        | ((row_ids == inner.shape[0] - 1) & (i_x == n_x - 1))
        | ((col_ids == 0) & (i_col == 0))
        | ((col_ids == inner.shape[1] - 1) & (i_col == n_col - 1))
    )
    inner = jnp.where(outside, 0.0, inner)
    bilaplace = laplace(inner)
    if n_z != 2:
        scale = basal_mask.astype(jnp.float32) * jnp.exp(friction)
    hessian_dir = reg_weight * bilaplace + scale * column
    return (stokes_image, hessian_dir)


def solution(mesh):
    return jax.shard_map(
        local,
        mesh=mesh,
        in_specs=(
            P(None, "gz", "gx", "gy"),
            P(None, "gz", "gx", "gy"),
            P("gz", "gx", "gy"),
            P("gx", "gy"),
            P("gx", "gy"),
            P(),
            P("gx", ("gy", "gz")),
            P("gx", ("gy", "gz")),
            P("gx", ("gy", "gz")),
        ),
        out_specs=(P(None, "gz", "gx", "gy"), P("gx", ("gy", "gz"))),
        check_vma=False,
    )
```

```python
import jax
import jax.numpy as jnp
from jax import lax
from jax.sharding import PartitionSpec as P
from jax.experimental import pallas as pl
from jax.experimental.pallas import tpu as pltpu


reg_weight = 0.05


def shift_pairs(count, step):
    if step > 0:
        return [(i, i + 1) for i in range(count - 1)]
    return [(i + 1, i) for i in range(count - 1)]


def prologue_kernel(
    vel_hbm, visc_hbm, flags_hbm, index_hbm, table_hbm, dir_hbm,
    stacked_ref, blocks_ref, low_ref, high_ref, y_low_ref, y_high_ref,
    vel_v, visc_v, flags_v, index_v, table_s, dir_v, sems,
):
    pairs = [
        (vel_hbm, vel_v), (visc_hbm, visc_v), (flags_hbm, flags_v),
        (index_hbm, index_v), (table_hbm, table_s), (dir_hbm, dir_v),
    ]
    copies = [pltpu.make_async_copy(s, d, sems.at[i]) for i, (s, d) in enumerate(pairs)]
    for copy in copies:
        copy.start()
    for copy in copies:
        copy.wait()
    index = index_v[...]
    hanging = flags_v[...] != 0
    count = table_s.shape[0] // 9
    blocks = []
    for j in range(9):
        entry = jnp.full(index.shape, table_s[j], jnp.float32)
        for number in range(1, count):
            entry = jnp.where(index == number, table_s[number * 9 + j], entry)
        entry = jnp.where(hanging, entry, 1.0 if j % 4 == 0 else 0.0)
        blocks_ref[j] = entry
        blocks.append(entry)
    groups = index.shape[1]
    fields, levels, rows, cols = stacked_ref.shape
    for c in range(fields - 1):
        for z in range(levels):
            slots = [vel_v[c, z, :, k * groups:(k + 1) * groups] for k in range(3)]
            for m in range(3):
                total = blocks[m * 3] * slots[0]
                total = total + blocks[m * 3 + 1] * slots[1]
                total = total + blocks[m * 3 + 2] * slots[2]
                stacked_ref[c, z, :, m * groups:(m + 1) * groups] = total
    stacked_ref[fields - 1] = visc_v[...]
    for f in range(fields):
        for z in range(levels):
            row = f * levels + z
            low_ref[row:row + 1, :] = stacked_ref[f, z, 0:1, :]
            high_ref[row:row + 1, :] = stacked_ref[f, z, rows - 1:rows, :]
    y_low_ref[...] = jnp.zeros(y_low_ref.shape, jnp.float32)
    y_high_ref[...] = jnp.zeros(y_high_ref.shape, jnp.float32)
    for f in range(fields):
        for z in range(levels):
            row = f * levels + z
            first = jnp.transpose(stacked_ref[f, z, :, 0:128])
            last = jnp.transpose(stacked_ref[f, z, :, cols - 128:cols])
            y_low_ref[row:row + 1, 0:rows] = first[0:1, :]
            y_high_ref[row:row + 1, 0:rows] = last[127:128, :]
    d_rows, d_cols = dir_v.shape
    edge = fields * levels
    low_ref[edge:, :] = jnp.zeros((2, cols), jnp.float32)
    high_ref[edge:, :] = jnp.zeros((2, cols), jnp.float32)
    low_ref[edge:, 0:d_cols] = dir_v[0:2, :]
    high_ref[edge:, 0:d_cols] = dir_v[d_rows - 2:, :]


def prologue(velocity, viscosity, hang_flags, hang_index, block_table, direction):
    fields = velocity.shape[0] + 1
    stack_shape = (fields,) + viscosity.shape
    packet = (fields * viscosity.shape[0] + 2, viscosity.shape[2])
    table = block_table.astype(jnp.float32).reshape(-1)
    f32 = jnp.float32
    anywhere = pl.BlockSpec(memory_space=pl.ANY)
    in_vmem = pl.BlockSpec(memory_space=pltpu.VMEM)
    return pl.pallas_call(
        prologue_kernel,
        out_shape=(
            jax.ShapeDtypeStruct(stack_shape, f32),
            jax.ShapeDtypeStruct((9,) + hang_index.shape, f32),
            jax.ShapeDtypeStruct(packet, f32),
            jax.ShapeDtypeStruct(packet, f32),
            jax.ShapeDtypeStruct((fields * viscosity.shape[0], 128), f32),
            jax.ShapeDtypeStruct((fields * viscosity.shape[0], 128), f32),
        ),
        in_specs=[anywhere] * 6,
        out_specs=(in_vmem,) * 6,
        scratch_shapes=[
            pltpu.VMEM(velocity.shape, f32),
            pltpu.VMEM(viscosity.shape, f32),
            pltpu.VMEM(hang_flags.shape, jnp.int32),
            pltpu.VMEM(hang_index.shape, jnp.int32),
            pltpu.SMEM(table.shape, f32),
            pltpu.VMEM(direction.shape, f32),
            pltpu.SemaphoreType.DMA((6,)),
        ],
        cost_estimate=pl.CostEstimate(
            flops=200000, transcendentals=0, bytes_accessed=300000
        ),
    )(velocity, viscosity, hang_flags, hang_index, table, direction)


def block_matrices(hang_flags, hang_index, block_table):
    count = block_table.shape[0]
    numbers = lax.broadcasted_iota(jnp.int32, (count,) + hang_index.shape, 0)
    one_hot = (hang_index[None] == numbers).astype(jnp.float32)
    table = block_table.astype(jnp.float32).reshape(count, 9)
    chosen = lax.dot_general(
        table, one_hot, (((0,), (0,)), ((), ())), precision=lax.Precision.HIGHEST
    )
    identity = jnp.eye(3, dtype=jnp.float32).reshape(9)[:, None, None]
    blocks = jnp.where(hang_flags[None] != 0, chosen, identity)
    return [[blocks[m * 3 + k] for k in range(3)] for m in range(3)]


def apply_blocks(blocks, field, transpose):
    groups = field.shape[-1] // 3
    slots = [field[..., k * groups:(k + 1) * groups] for k in range(3)]
    mixed = []
    for m in range(3):
        total = None
        for k in range(3):
            weight = blocks[k][m] if transpose else blocks[m][k]
            term = weight * slots[k]
            total = term if total is None else total + term
        mixed.append(total)
    return jnp.concatenate(mixed, axis=-1)


def shifted(padded, spatial, offset):
    lead = padded.ndim - 3
    index = [slice(None)] * lead + [slice(1, -1)] * 3
    if offset == 1:
        index[lead + spatial] = slice(2, None)
    elif offset == -1:
        index[lead + spatial] = slice(None, -2)
    return padded[tuple(index)]


def stencil(padded_vel, padded_visc):
    centre_vel = shifted(padded_vel, 0, 0)
    centre_visc = shifted(padded_visc, 0, 0)
    total = jnp.zeros(centre_vel.shape, jnp.float32)
    for spatial in range(3):
        for offset in (1, -1):
            face = 0.5 * (centre_visc + shifted(padded_visc, spatial, offset))
            total = total + face[None] * (centre_vel - shifted(padded_vel, spatial, offset))
    return total


def laplace(padded):
    return (
        4.0 * padded[1:-1, 1:-1]
        - padded[2:, 1:-1]
        - padded[:-2, 1:-1]
        - padded[1:-1, 2:]
        - padded[1:-1, :-2]
    )


def local(
    velocity,
    adjoint,
    viscosity,
    hang_flags,
    hang_index,
    block_table,
    friction,
    basal_mask,
    direction,
):
    n_x = lax.axis_size("gx")
    n_y = lax.axis_size("gy")
    n_z = lax.axis_size("gz")
    i_x = lax.axis_index("gx")
    i_z = lax.axis_index("gz")
    n_col = n_y * n_z
    i_col = lax.axis_index("gy") * n_z + i_z

    stacked, table9, low_packet, high_packet, y_low_edge, y_high_edge = prologue(
        velocity, viscosity, hang_flags, hang_index, block_table, direction
    )
    blocks = [[table9[m * 3 + k] for k in range(3)] for m in range(3)]
    fields, levels, rows, cols = stacked.shape
    d_rows, d_cols = direction.shape

    from_left = lax.ppermute(high_packet, "gx", shift_pairs(n_x, 1))
    from_right = lax.ppermute(low_packet, "gx", shift_pairs(n_x, -1))
    y_left = lax.ppermute(y_high_edge, "gy", shift_pairs(n_y, 1))
    y_right = lax.ppermute(y_low_edge, "gy", shift_pairs(n_y, -1))
    y_left = y_left[:, :rows].reshape(fields, levels, rows, 1)
    y_right = y_right[:, :rows].reshape(fields, levels, rows, 1)
    if n_z == 2:
        sent = lax.dynamic_slice_in_dim(stacked, (1 - i_z) * (levels - 1), 1, axis=1)
        got = lax.ppermute(sent, "gz", [(0, 1), (1, 0)])
        zero = jnp.zeros_like(got)
        z_low = jnp.where(i_z == 1, got, zero)
        z_high = jnp.where(i_z == 0, got, zero)
    else:
        z_low = lax.ppermute(stacked[:, levels - 1:], "gz", shift_pairs(n_z, 1))
        z_high = lax.ppermute(stacked[:, :1], "gz", shift_pairs(n_z, -1))

    x_low = from_left[: fields * levels].reshape(fields, levels, 1, cols)
    x_high = from_right[: fields * levels].reshape(fields, levels, 1, cols)
    d_low = from_left[fields * levels:, :d_cols]
    d_high = from_right[fields * levels:, :d_cols]

    d_ext = jnp.concatenate([d_low, direction, d_high], axis=0)
    padded = jnp.concatenate([y_left, stacked, y_right], axis=3)
    pad_y = ((0, 0), (0, 0), (0, 0), (1, 1))
    padded = jnp.concatenate(
        [jnp.pad(x_low, pad_y), padded, jnp.pad(x_high, pad_y)], axis=2
    )
    pad_xy = ((0, 0), (0, 0), (1, 1), (1, 1))
    padded = jnp.concatenate(
        [jnp.pad(z_low, pad_xy), padded, jnp.pad(z_high, pad_xy)], axis=1
    )
    applied = stencil(padded[:3], padded[3])
    stokes_image = apply_blocks(blocks, applied, True)
    partial_value = jnp.sum(stokes_image * adjoint, axis=(0, 1))

    own_width = cols // n_z
    if n_z == 2:
        sent = lax.dynamic_slice_in_dim(partial_value, (1 - i_z) * own_width, own_width, axis=1)
        mine = lax.dynamic_slice_in_dim(partial_value, i_z * own_width, own_width, axis=1)
        d_partner = lax.dynamic_slice_in_dim(d_ext, (1 - i_z) * (d_cols - 2), 2, axis=1)
        d_across = lax.dynamic_slice_in_dim(d_ext, i_z * (d_cols - 2), 2, axis=1)
        flat = d_partner.reshape(1, -1)
        packet = jnp.concatenate(
            [sent, jnp.pad(flat, ((0, 0), (0, own_width - flat.shape[1])))], axis=0
        )
        packet, d_across = lax.optimization_barrier((packet, d_across))
        got = lax.ppermute(packet, "gz", [(0, 1), (1, 0)])
        across_pairs = []
        for block in range(n_y - 1):
            across_pairs += [(2 * block + 1, 2 * block + 2), (2 * block + 2, 2 * block + 1)]
        got_across = lax.ppermute(d_across, ("gy", "gz"), across_pairs)
        column = mine + got[: sent.shape[0]]
        got_partner = got[sent.shape[0], : flat.shape[1]].reshape(d_partner.shape)
        d_left = jnp.where(i_z == 0, got_across, got_partner)
        d_right = jnp.where(i_z == 0, got_partner, got_across)
    else:
        column = lax.psum_scatter(partial_value, "gz", scatter_dimension=1, tiled=True)
        d_left = lax.ppermute(d_ext[:, d_cols - 2:], ("gy", "gz"), shift_pairs(n_col, 1))
        d_right = lax.ppermute(d_ext[:, :2], ("gy", "gz"), shift_pairs(n_col, -1))

    d_full = jnp.concatenate([d_left, d_ext, d_right], axis=1)
    inner = laplace(d_full)
    row_ids = lax.broadcasted_iota(jnp.int32, inner.shape, 0)
    col_ids = lax.broadcasted_iota(jnp.int32, inner.shape, 1)
    outside = (
        ((row_ids == 0) & (i_x == 0))
        | ((row_ids == inner.shape[0] - 1) & (i_x == n_x - 1))
        | ((col_ids == 0) & (i_col == 0))
        | ((col_ids == inner.shape[1] - 1) & (i_col == n_col - 1))
    )
    inner = jnp.where(outside, 0.0, inner)
    bilaplace = laplace(inner)
    hessian_dir = reg_weight * bilaplace + basal_mask.astype(jnp.float32) * (
        jnp.exp(friction) * column
    )
    return (stokes_image, hessian_dir)


def solution(mesh):
    return jax.shard_map(
        local,
        mesh=mesh,
        in_specs=(
            P(None, "gz", "gx", "gy"),
            P(None, "gz", "gx", "gy"),
            P("gz", "gx", "gy"),
            P("gx", "gy"),
            P("gx", "gy"),
            P(),
            P("gx", ("gy", "gz")),
            P("gx", ("gy", "gz")),
            P("gx", ("gy", "gz")),
        ),
        out_specs=(P(None, "gz", "gx", "gy"), P("gx", ("gy", "gz"))),
        check_vma=False,
    )
```

```python
import jax
import jax.numpy as jnp
from jax import lax
from jax.sharding import PartitionSpec as P
from jax.experimental import pallas as pl
from jax.experimental.pallas import tpu as pltpu


reg_weight = 0.05


def shift_pairs(count, step):
    if step > 0:
        return [(i, i + 1) for i in range(count - 1)]
    return [(i + 1, i) for i in range(count - 1)]


def prologue_kernel(
    vel_hbm, visc_hbm, flags_hbm, index_hbm, table_hbm, dir_hbm,
    stacked_ref, blocks_ref, low_ref, high_ref,
    vel_v, visc_v, flags_v, index_v, table_v, dir_v, sems,
):
    pairs = [
        (vel_hbm, vel_v), (visc_hbm, visc_v), (flags_hbm, flags_v),
        (index_hbm, index_v), (table_hbm, table_v), (dir_hbm, dir_v),
    ]
    copies = [pltpu.make_async_copy(s, d, sems.at[i]) for i, (s, d) in enumerate(pairs)]
    for copy in copies:
        copy.start()
    for copy in copies:
        copy.wait()
    index = index_v[...]
    hanging = flags_v[...] != 0
    count = table_v.shape[0]
    blocks = []
    for j in range(9):
        m, k = j // 3, j % 3
        entry = jnp.broadcast_to(table_v[0, m:m + 1, k:k + 1], index.shape)
        for number in range(1, count):
            value = jnp.broadcast_to(table_v[number, m:m + 1, k:k + 1], index.shape)
            entry = jnp.where(index == number, value, entry)
        entry = jnp.where(hanging, entry, 1.0 if j % 4 == 0 else 0.0)
        blocks_ref[j] = entry
        blocks.append(entry)
    groups = index.shape[1]
    fields, levels, rows, cols = stacked_ref.shape
    for c in range(fields - 1):
        for z in range(levels):
            slots = [vel_v[c, z, :, k * groups:(k + 1) * groups] for k in range(3)]
            for m in range(3):
                total = blocks[m * 3] * slots[0]
                total = total + blocks[m * 3 + 1] * slots[1]
                total = total + blocks[m * 3 + 2] * slots[2]
                stacked_ref[c, z, :, m * groups:(m + 1) * groups] = total
    stacked_ref[fields - 1] = visc_v[...]
    for f in range(fields):
        for z in range(levels):
            row = f * levels + z
            low_ref[row:row + 1, :] = stacked_ref[f, z, 0:1, :]
            high_ref[row:row + 1, :] = stacked_ref[f, z, rows - 1:rows, :]
    d_rows, d_cols = dir_v.shape
    edge = fields * levels
    low_ref[edge:, :] = jnp.zeros((2, cols), jnp.float32)
    high_ref[edge:, :] = jnp.zeros((2, cols), jnp.float32)
    low_ref[edge:, 0:d_cols] = dir_v[0:2, :]
    high_ref[edge:, 0:d_cols] = dir_v[d_rows - 2:, :]


def prologue(velocity, viscosity, hang_flags, hang_index, block_table, direction):
    fields = velocity.shape[0] + 1
    stack_shape = (fields,) + viscosity.shape
    packet = (fields * viscosity.shape[0] + 2, viscosity.shape[2])
    table = block_table.astype(jnp.float32)
    f32 = jnp.float32
    anywhere = pl.BlockSpec(memory_space=pl.ANY)
    in_vmem = pl.BlockSpec(memory_space=pltpu.VMEM)
    return pl.pallas_call(
        prologue_kernel,
        out_shape=(
            jax.ShapeDtypeStruct(stack_shape, f32),
            jax.ShapeDtypeStruct((9,) + hang_index.shape, f32),
            jax.ShapeDtypeStruct(packet, f32),
            jax.ShapeDtypeStruct(packet, f32),
        ),
        in_specs=[anywhere] * 6,
        out_specs=(in_vmem,) * 4,
        scratch_shapes=[
            pltpu.VMEM(velocity.shape, f32),
            pltpu.VMEM(viscosity.shape, f32),
            pltpu.VMEM(hang_flags.shape, jnp.int32),
            pltpu.VMEM(hang_index.shape, jnp.int32),
            pltpu.VMEM(table.shape, f32),
            pltpu.VMEM(direction.shape, f32),
            pltpu.SemaphoreType.DMA((6,)),
        ],
        cost_estimate=pl.CostEstimate(
            flops=200000, transcendentals=0, bytes_accessed=300000
        ),
    )(velocity, viscosity, hang_flags, hang_index, table, direction)


def block_matrices(hang_flags, hang_index, block_table):
    count = block_table.shape[0]
    numbers = lax.broadcasted_iota(jnp.int32, (count,) + hang_index.shape, 0)
    one_hot = (hang_index[None] == numbers).astype(jnp.float32)
    table = block_table.astype(jnp.float32).reshape(count, 9)
    chosen = lax.dot_general(
        table, one_hot, (((0,), (0,)), ((), ())), precision=lax.Precision.HIGHEST
    )
    identity = jnp.eye(3, dtype=jnp.float32).reshape(9)[:, None, None]
    blocks = jnp.where(hang_flags[None] != 0, chosen, identity)
    return [[blocks[m * 3 + k] for k in range(3)] for m in range(3)]


def apply_blocks(blocks, field, transpose):
    groups = field.shape[-1] // 3
    slots = [field[..., k * groups:(k + 1) * groups] for k in range(3)]
    mixed = []
    for m in range(3):
        total = None
        for k in range(3):
            weight = blocks[k][m] if transpose else blocks[m][k]
            term = weight * slots[k]
            total = term if total is None else total + term
        mixed.append(total)
    return jnp.concatenate(mixed, axis=-1)


def shifted(padded, spatial, offset):
    lead = padded.ndim - 3
    index = [slice(None)] * lead + [slice(1, -1)] * 3
    if offset == 1:
        index[lead + spatial] = slice(2, None)
    elif offset == -1:
        index[lead + spatial] = slice(None, -2)
    return padded[tuple(index)]


def stencil(padded_vel, padded_visc):
    centre_vel = shifted(padded_vel, 0, 0)
    centre_visc = shifted(padded_visc, 0, 0)
    total = jnp.zeros(centre_vel.shape, jnp.float32)
    for spatial in range(3):
        for offset in (1, -1):
            face = 0.5 * (centre_visc + shifted(padded_visc, spatial, offset))
            total = total + face[None] * (centre_vel - shifted(padded_vel, spatial, offset))
    return total


def laplace(padded):
    return (
        4.0 * padded[1:-1, 1:-1]
        - padded[2:, 1:-1]
        - padded[:-2, 1:-1]
        - padded[1:-1, 2:]
        - padded[1:-1, :-2]
    )


def local(
    velocity,
    adjoint,
    viscosity,
    hang_flags,
    hang_index,
    block_table,
    friction,
    basal_mask,
    direction,
):
    n_x = lax.axis_size("gx")
    n_y = lax.axis_size("gy")
    n_z = lax.axis_size("gz")
    i_x = lax.axis_index("gx")
    i_z = lax.axis_index("gz")
    n_col = n_y * n_z
    i_col = lax.axis_index("gy") * n_z + i_z

    stacked, table9, low_packet, high_packet = prologue(
        velocity, viscosity, hang_flags, hang_index, block_table, direction
    )
    blocks = [[table9[m * 3 + k] for k in range(3)] for m in range(3)]
    fields, levels, rows, cols = stacked.shape
    d_rows, d_cols = direction.shape

    from_left = lax.ppermute(high_packet, "gx", shift_pairs(n_x, 1))
    from_right = lax.ppermute(low_packet, "gx", shift_pairs(n_x, -1))
    y_left = lax.ppermute(stacked[:, :, :, cols - 1:], "gy", shift_pairs(n_y, 1))
    y_right = lax.ppermute(stacked[:, :, :, :1], "gy", shift_pairs(n_y, -1))
    if n_z == 2:
        sent = lax.dynamic_slice_in_dim(stacked, (1 - i_z) * (levels - 1), 1, axis=1)
        got = lax.ppermute(sent, "gz", [(0, 1), (1, 0)])
        zero = jnp.zeros_like(got)
        z_low = jnp.where(i_z == 1, got, zero)
        z_high = jnp.where(i_z == 0, got, zero)
    else:
        z_low = lax.ppermute(stacked[:, levels - 1:], "gz", shift_pairs(n_z, 1))
        z_high = lax.ppermute(stacked[:, :1], "gz", shift_pairs(n_z, -1))

    x_low = from_left[: fields * levels].reshape(fields, levels, 1, cols)
    x_high = from_right[: fields * levels].reshape(fields, levels, 1, cols)
    d_low = from_left[fields * levels:, :d_cols]
    d_high = from_right[fields * levels:, :d_cols]

    d_ext = jnp.concatenate([d_low, direction, d_high], axis=0)
    padded = jnp.concatenate([y_left, stacked, y_right], axis=3)
    pad_y = ((0, 0), (0, 0), (0, 0), (1, 1))
    padded = jnp.concatenate(
        [jnp.pad(x_low, pad_y), padded, jnp.pad(x_high, pad_y)], axis=2
    )
    pad_xy = ((0, 0), (0, 0), (1, 1), (1, 1))
    padded = jnp.concatenate(
        [jnp.pad(z_low, pad_xy), padded, jnp.pad(z_high, pad_xy)], axis=1
    )
    applied = stencil(padded[:3], padded[3])
    stokes_image = apply_blocks(blocks, applied, True)
    partial_value = jnp.sum(stokes_image * adjoint, axis=(0, 1))

    own_width = cols // n_z
    if n_z == 2:
        sent = lax.dynamic_slice_in_dim(partial_value, (1 - i_z) * own_width, own_width, axis=1)
        mine = lax.dynamic_slice_in_dim(partial_value, i_z * own_width, own_width, axis=1)
        d_partner = lax.dynamic_slice_in_dim(d_ext, (1 - i_z) * (d_cols - 2), 2, axis=1)
        d_across = lax.dynamic_slice_in_dim(d_ext, i_z * (d_cols - 2), 2, axis=1)
        flat = d_partner.reshape(1, -1)
        packet = jnp.concatenate(
            [sent, jnp.pad(flat, ((0, 0), (0, own_width - flat.shape[1])))], axis=0
        )
        packet, d_across = lax.optimization_barrier((packet, d_across))
        got = lax.ppermute(packet, "gz", [(0, 1), (1, 0)])
        across_pairs = []
        for block in range(n_y - 1):
            across_pairs += [(2 * block + 1, 2 * block + 2), (2 * block + 2, 2 * block + 1)]
        got_across = lax.ppermute(d_across, ("gy", "gz"), across_pairs)
        column = mine + got[: sent.shape[0]]
        got_partner = got[sent.shape[0], : flat.shape[1]].reshape(d_partner.shape)
        d_left = jnp.where(i_z == 0, got_across, got_partner)
        d_right = jnp.where(i_z == 0, got_partner, got_across)
    else:
        column = lax.psum_scatter(partial_value, "gz", scatter_dimension=1, tiled=True)
        d_left = lax.ppermute(d_ext[:, d_cols - 2:], ("gy", "gz"), shift_pairs(n_col, 1))
        d_right = lax.ppermute(d_ext[:, :2], ("gy", "gz"), shift_pairs(n_col, -1))

    d_full = jnp.concatenate([d_left, d_ext, d_right], axis=1)
    inner = laplace(d_full)
    row_ids = lax.broadcasted_iota(jnp.int32, inner.shape, 0)
    col_ids = lax.broadcasted_iota(jnp.int32, inner.shape, 1)
    outside = (
        ((row_ids == 0) & (i_x == 0))
        | ((row_ids == inner.shape[0] - 1) & (i_x == n_x - 1))
        | ((col_ids == 0) & (i_col == 0))
        | ((col_ids == inner.shape[1] - 1) & (i_col == n_col - 1))
    )
    inner = jnp.where(outside, 0.0, inner)
    bilaplace = laplace(inner)
    hessian_dir = reg_weight * bilaplace + basal_mask.astype(jnp.float32) * (
        jnp.exp(friction) * column
    )
    return (stokes_image, hessian_dir)


def solution(mesh):
    return jax.shard_map(
        local,
        mesh=mesh,
        in_specs=(
            P(None, "gz", "gx", "gy"),
            P(None, "gz", "gx", "gy"),
            P("gz", "gx", "gy"),
            P("gx", "gy"),
            P("gx", "gy"),
            P(),
            P("gx", ("gy", "gz")),
            P("gx", ("gy", "gz")),
            P("gx", ("gy", "gz")),
        ),
        out_specs=(P(None, "gz", "gx", "gy"), P("gx", ("gy", "gz"))),
        check_vma=False,
    )
```

```python
import jax
import jax.numpy as jnp
from jax import lax
from jax.sharding import PartitionSpec as P
from jax.experimental import pallas as pl
from jax.experimental.pallas import tpu as pltpu


reg_weight = 0.05


def shift_pairs(count, step):
    if step > 0:
        return [(i, i + 1) for i in range(count - 1)]
    return [(i + 1, i) for i in range(count - 1)]


def prologue_kernel(
    vel_hbm, visc_hbm, flags_hbm, index_hbm, table_hbm, dir_hbm,
    stacked_ref, blocks_ref, low_ref, high_ref,
    vel_v, visc_v, flags_v, index_v, table_s, dir_v, sems,
):
    pairs = [
        (vel_hbm, vel_v), (visc_hbm, visc_v), (flags_hbm, flags_v),
        (index_hbm, index_v), (table_hbm, table_s), (dir_hbm, dir_v),
    ]
    copies = [pltpu.make_async_copy(s, d, sems.at[i]) for i, (s, d) in enumerate(pairs)]
    for copy in copies:
        copy.start()
    for copy in copies:
        copy.wait()
    index = index_v[...]
    hanging = flags_v[...] != 0
    count = table_s.shape[0] // 9
    blocks = []
    for j in range(9):
        entry = jnp.full(index.shape, table_s[j], jnp.float32)
        for number in range(1, count):
            entry = jnp.where(index == number, table_s[number * 9 + j], entry)
        entry = jnp.where(hanging, entry, 1.0 if j % 4 == 0 else 0.0)
        blocks_ref[j] = entry
        blocks.append(entry)
    groups = index.shape[1]
    fields, levels, rows, cols = stacked_ref.shape
    for c in range(fields - 1):
        for z in range(levels):
            slots = [vel_v[c, z, :, k * groups:(k + 1) * groups] for k in range(3)]
            for m in range(3):
                total = blocks[m * 3] * slots[0]
                total = total + blocks[m * 3 + 1] * slots[1]
                total = total + blocks[m * 3 + 2] * slots[2]
                stacked_ref[c, z, :, m * groups:(m + 1) * groups] = total
    stacked_ref[fields - 1] = visc_v[...]
    for f in range(fields):
        for z in range(levels):
            row = f * levels + z
            low_ref[row:row + 1, :] = stacked_ref[f, z, 0:1, :]
            high_ref[row:row + 1, :] = stacked_ref[f, z, rows - 1:rows, :]
    d_rows, d_cols = dir_v.shape
    edge = fields * levels
    low_ref[edge:, :] = jnp.zeros((2, cols), jnp.float32)
    high_ref[edge:, :] = jnp.zeros((2, cols), jnp.float32)
    low_ref[edge:, 0:d_cols] = dir_v[0:2, :]
    high_ref[edge:, 0:d_cols] = dir_v[d_rows - 2:, :]
    low = low_ref[...]
    high = high_ref[...]
    even = lax.axis_index("gx") % 2 == 0
    low_ref[...] = jnp.where(even, high, low)
    high_ref[...] = jnp.where(even, low, high)


def prologue(velocity, viscosity, hang_flags, hang_index, block_table, direction):
    fields = velocity.shape[0] + 1
    stack_shape = (fields,) + viscosity.shape
    packet = (fields * viscosity.shape[0] + 2, viscosity.shape[2])
    table = block_table.astype(jnp.float32).reshape(-1)
    f32 = jnp.float32
    anywhere = pl.BlockSpec(memory_space=pl.ANY)
    in_vmem = pl.BlockSpec(memory_space=pltpu.VMEM)
    return pl.pallas_call(
        prologue_kernel,
        out_shape=(
            jax.ShapeDtypeStruct(stack_shape, f32),
            jax.ShapeDtypeStruct((9,) + hang_index.shape, f32),
            jax.ShapeDtypeStruct(packet, f32),
            jax.ShapeDtypeStruct(packet, f32),
        ),
        in_specs=[anywhere] * 6,
        out_specs=(in_vmem,) * 4,
        scratch_shapes=[
            pltpu.VMEM(velocity.shape, f32),
            pltpu.VMEM(viscosity.shape, f32),
            pltpu.VMEM(hang_flags.shape, jnp.int32),
            pltpu.VMEM(hang_index.shape, jnp.int32),
            pltpu.SMEM(table.shape, f32),
            pltpu.VMEM(direction.shape, f32),
            pltpu.SemaphoreType.DMA((6,)),
        ],
        cost_estimate=pl.CostEstimate(
            flops=200000, transcendentals=0, bytes_accessed=300000
        ),
    )(velocity, viscosity, hang_flags, hang_index, table, direction)


def block_matrices(hang_flags, hang_index, block_table):
    count = block_table.shape[0]
    numbers = lax.broadcasted_iota(jnp.int32, (count,) + hang_index.shape, 0)
    one_hot = (hang_index[None] == numbers).astype(jnp.float32)
    table = block_table.astype(jnp.float32).reshape(count, 9)
    chosen = lax.dot_general(
        table, one_hot, (((0,), (0,)), ((), ())), precision=lax.Precision.HIGHEST
    )
    identity = jnp.eye(3, dtype=jnp.float32).reshape(9)[:, None, None]
    blocks = jnp.where(hang_flags[None] != 0, chosen, identity)
    return [[blocks[m * 3 + k] for k in range(3)] for m in range(3)]


def apply_blocks(blocks, field, transpose):
    groups = field.shape[-1] // 3
    slots = [field[..., k * groups:(k + 1) * groups] for k in range(3)]
    mixed = []
    for m in range(3):
        total = None
        for k in range(3):
            weight = blocks[k][m] if transpose else blocks[m][k]
            term = weight * slots[k]
            total = term if total is None else total + term
        mixed.append(total)
    return jnp.concatenate(mixed, axis=-1)


def shifted(padded, spatial, offset):
    lead = padded.ndim - 3
    index = [slice(None)] * lead + [slice(1, -1)] * 3
    if offset == 1:
        index[lead + spatial] = slice(2, None)
    elif offset == -1:
        index[lead + spatial] = slice(None, -2)
    return padded[tuple(index)]


def stencil(padded_vel, padded_visc):
    centre_vel = shifted(padded_vel, 0, 0)
    centre_visc = shifted(padded_visc, 0, 0)
    total = jnp.zeros(centre_vel.shape, jnp.float32)
    for spatial in range(3):
        for offset in (1, -1):
            face = 0.5 * (centre_visc + shifted(padded_visc, spatial, offset))
            total = total + face[None] * (centre_vel - shifted(padded_vel, spatial, offset))
    return total


def laplace(padded):
    return (
        4.0 * padded[1:-1, 1:-1]
        - padded[2:, 1:-1]
        - padded[:-2, 1:-1]
        - padded[1:-1, 2:]
        - padded[1:-1, :-2]
    )


def local(
    velocity,
    adjoint,
    viscosity,
    hang_flags,
    hang_index,
    block_table,
    friction,
    basal_mask,
    direction,
):
    n_x = lax.axis_size("gx")
    n_y = lax.axis_size("gy")
    n_z = lax.axis_size("gz")
    i_x = lax.axis_index("gx")
    i_z = lax.axis_index("gz")
    n_col = n_y * n_z
    i_col = lax.axis_index("gy") * n_z + i_z

    stacked, table9, low_packet, high_packet = prologue(
        velocity, viscosity, hang_flags, hang_index, block_table, direction
    )
    blocks = [[table9[m * 3 + k] for k in range(3)] for m in range(3)]
    fields, levels, rows, cols = stacked.shape
    d_rows, d_cols = direction.shape

    even = i_x % 2 == 0
    pairs_a = [(i, i ^ 1) for i in range(n_x - n_x % 2)]
    pairs_b = []
    for k in range(1, n_x - 1, 2):
        pairs_b += [(k, k + 1), (k + 1, k)]
    got_a = lax.ppermute(low_packet, "gx", pairs_a)
    got_b = lax.ppermute(high_packet, "gx", pairs_b)
    from_left = jnp.where(even, got_b, got_a)
    from_right = jnp.where(even, got_a, got_b)
    y_left = lax.ppermute(stacked[:, :, :, cols - 1:], "gy", shift_pairs(n_y, 1))
    y_right = lax.ppermute(stacked[:, :, :, :1], "gy", shift_pairs(n_y, -1))
    if n_z == 2:
        sent = lax.dynamic_slice_in_dim(stacked, (1 - i_z) * (levels - 1), 1, axis=1)
        got = lax.ppermute(sent, "gz", [(0, 1), (1, 0)])
        zero = jnp.zeros_like(got)
        z_low = jnp.where(i_z == 1, got, zero)
        z_high = jnp.where(i_z == 0, got, zero)
    else:
        z_low = lax.ppermute(stacked[:, levels - 1:], "gz", shift_pairs(n_z, 1))
        z_high = lax.ppermute(stacked[:, :1], "gz", shift_pairs(n_z, -1))

    x_low = from_left[: fields * levels].reshape(fields, levels, 1, cols)
    x_high = from_right[: fields * levels].reshape(fields, levels, 1, cols)
    d_low = from_left[fields * levels:, :d_cols]
    d_high = from_right[fields * levels:, :d_cols]

    d_ext = jnp.concatenate([d_low, direction, d_high], axis=0)
    padded = jnp.concatenate([y_left, stacked, y_right], axis=3)
    pad_y = ((0, 0), (0, 0), (0, 0), (1, 1))
    padded = jnp.concatenate(
        [jnp.pad(x_low, pad_y), padded, jnp.pad(x_high, pad_y)], axis=2
    )
    pad_xy = ((0, 0), (0, 0), (1, 1), (1, 1))
    padded = jnp.concatenate(
        [jnp.pad(z_low, pad_xy), padded, jnp.pad(z_high, pad_xy)], axis=1
    )
    applied = stencil(padded[:3], padded[3])
    stokes_image = apply_blocks(blocks, applied, True)
    partial_value = jnp.sum(stokes_image * adjoint, axis=(0, 1))

    own_width = cols // n_z
    if n_z == 2:
        sent = lax.dynamic_slice_in_dim(partial_value, (1 - i_z) * own_width, own_width, axis=1)
        mine = lax.dynamic_slice_in_dim(partial_value, i_z * own_width, own_width, axis=1)
        d_partner = lax.dynamic_slice_in_dim(d_ext, (1 - i_z) * (d_cols - 2), 2, axis=1)
        d_across = lax.dynamic_slice_in_dim(d_ext, i_z * (d_cols - 2), 2, axis=1)
        flat = d_partner.reshape(1, -1)
        packet = jnp.concatenate(
            [sent, jnp.pad(flat, ((0, 0), (0, own_width - flat.shape[1])))], axis=0
        )
        packet, d_across = lax.optimization_barrier((packet, d_across))
        got = lax.ppermute(packet, "gz", [(0, 1), (1, 0)])
        across_pairs = []
        for block in range(n_y - 1):
            across_pairs += [(2 * block + 1, 2 * block + 2), (2 * block + 2, 2 * block + 1)]
        got_across = lax.ppermute(d_across, ("gy", "gz"), across_pairs)
        column = mine + got[: sent.shape[0]]
        got_partner = got[sent.shape[0], : flat.shape[1]].reshape(d_partner.shape)
        d_left = jnp.where(i_z == 0, got_across, got_partner)
        d_right = jnp.where(i_z == 0, got_partner, got_across)
    else:
        column = lax.psum_scatter(partial_value, "gz", scatter_dimension=1, tiled=True)
        d_left = lax.ppermute(d_ext[:, d_cols - 2:], ("gy", "gz"), shift_pairs(n_col, 1))
        d_right = lax.ppermute(d_ext[:, :2], ("gy", "gz"), shift_pairs(n_col, -1))

    d_full = jnp.concatenate([d_left, d_ext, d_right], axis=1)
    inner = laplace(d_full)
    row_ids = lax.broadcasted_iota(jnp.int32, inner.shape, 0)
    col_ids = lax.broadcasted_iota(jnp.int32, inner.shape, 1)
    outside = (
        ((row_ids == 0) & (i_x == 0))
        | ((row_ids == inner.shape[0] - 1) & (i_x == n_x - 1))
        | ((col_ids == 0) & (i_col == 0))
        | ((col_ids == inner.shape[1] - 1) & (i_col == n_col - 1))
    )
    inner = jnp.where(outside, 0.0, inner)
    bilaplace = laplace(inner)
    hessian_dir = reg_weight * bilaplace + basal_mask.astype(jnp.float32) * (
        jnp.exp(friction) * column
    )
    return (stokes_image, hessian_dir)


def solution(mesh):
    return jax.shard_map(
        local,
        mesh=mesh,
        in_specs=(
            P(None, "gz", "gx", "gy"),
            P(None, "gz", "gx", "gy"),
            P("gz", "gx", "gy"),
            P("gx", "gy"),
            P("gx", "gy"),
            P(),
            P("gx", ("gy", "gz")),
            P("gx", ("gy", "gz")),
            P("gx", ("gy", "gz")),
        ),
        out_specs=(P(None, "gz", "gx", "gy"), P("gx", ("gy", "gz"))),
        check_vma=False,
    )
```

```python
import jax
import jax.numpy as jnp
from jax import lax
from jax.sharding import PartitionSpec as P
from jax.experimental import pallas as pl
from jax.experimental.pallas import tpu as pltpu


reg_weight = 0.05


def shift_pairs(count, step):
    if step > 0:
        return [(i, i + 1) for i in range(count - 1)]
    return [(i + 1, i) for i in range(count - 1)]


def prologue_kernel(
    vel_hbm, visc_hbm, flags_hbm, index_hbm, table_hbm, dir_hbm,
    stacked_ref, blocks_ref, low_ref, high_ref, y_a_ref, y_b_ref,
    vel_v, visc_v, flags_v, index_v, table_s, dir_v, sems,
):
    pairs = [
        (vel_hbm, vel_v), (visc_hbm, visc_v), (flags_hbm, flags_v),
        (index_hbm, index_v), (table_hbm, table_s), (dir_hbm, dir_v),
    ]
    copies = [pltpu.make_async_copy(s, d, sems.at[i]) for i, (s, d) in enumerate(pairs)]
    for copy in copies:
        copy.start()
    for copy in copies:
        copy.wait()
    index = index_v[...]
    hanging = flags_v[...] != 0
    count = table_s.shape[0] // 9
    blocks = []
    for j in range(9):
        entry = jnp.full(index.shape, table_s[j], jnp.float32)
        for number in range(1, count):
            entry = jnp.where(index == number, table_s[number * 9 + j], entry)
        entry = jnp.where(hanging, entry, 1.0 if j % 4 == 0 else 0.0)
        blocks_ref[j] = entry
        blocks.append(entry)
    groups = index.shape[1]
    fields, levels, rows, cols = stacked_ref.shape
    for c in range(fields - 1):
        for z in range(levels):
            slots = [vel_v[c, z, :, k * groups:(k + 1) * groups] for k in range(3)]
            for m in range(3):
                total = blocks[m * 3] * slots[0]
                total = total + blocks[m * 3 + 1] * slots[1]
                total = total + blocks[m * 3 + 2] * slots[2]
                stacked_ref[c, z, :, m * groups:(m + 1) * groups] = total
    stacked_ref[fields - 1] = visc_v[...]
    for f in range(fields):
        for z in range(levels):
            row = f * levels + z
            low_ref[row:row + 1, :] = stacked_ref[f, z, 0:1, :]
            high_ref[row:row + 1, :] = stacked_ref[f, z, rows - 1:rows, :]
    d_rows, d_cols = dir_v.shape
    edge = fields * levels
    low_ref[edge:, :] = jnp.zeros((2, cols), jnp.float32)
    high_ref[edge:, :] = jnp.zeros((2, cols), jnp.float32)
    low_ref[edge:, 0:d_cols] = dir_v[0:2, :]
    high_ref[edge:, 0:d_cols] = dir_v[d_rows - 2:, :]
    y_even = lax.axis_index("gy") % 2 == 0
    for f in range(fields):
        for z in range(levels):
            first = stacked_ref[f, z, :, 0:1]
            last = stacked_ref[f, z, :, cols - 1:cols]
            y_a_ref[f, z] = jnp.where(y_even, last, first)
            y_b_ref[f, z] = jnp.where(y_even, first, last)
    low = low_ref[...]
    high = high_ref[...]
    even = lax.axis_index("gx") % 2 == 0
    low_ref[...] = jnp.where(even, high, low)
    high_ref[...] = jnp.where(even, low, high)


def prologue(velocity, viscosity, hang_flags, hang_index, block_table, direction):
    fields = velocity.shape[0] + 1
    stack_shape = (fields,) + viscosity.shape
    packet = (fields * viscosity.shape[0] + 2, viscosity.shape[2])
    table = block_table.astype(jnp.float32).reshape(-1)
    f32 = jnp.float32
    anywhere = pl.BlockSpec(memory_space=pl.ANY)
    in_vmem = pl.BlockSpec(memory_space=pltpu.VMEM)
    return pl.pallas_call(
        prologue_kernel,
        out_shape=(
            jax.ShapeDtypeStruct(stack_shape, f32),
            jax.ShapeDtypeStruct((9,) + hang_index.shape, f32),
            jax.ShapeDtypeStruct(packet, f32),
            jax.ShapeDtypeStruct(packet, f32),
            jax.ShapeDtypeStruct(stack_shape[:3] + (1,), f32),
            jax.ShapeDtypeStruct(stack_shape[:3] + (1,), f32),
        ),
        in_specs=[anywhere] * 6,
        out_specs=(in_vmem,) * 6,
        scratch_shapes=[
            pltpu.VMEM(velocity.shape, f32),
            pltpu.VMEM(viscosity.shape, f32),
            pltpu.VMEM(hang_flags.shape, jnp.int32),
            pltpu.VMEM(hang_index.shape, jnp.int32),
            pltpu.SMEM(table.shape, f32),
            pltpu.VMEM(direction.shape, f32),
            pltpu.SemaphoreType.DMA((6,)),
        ],
        cost_estimate=pl.CostEstimate(
            flops=200000, transcendentals=0, bytes_accessed=300000
        ),
    )(velocity, viscosity, hang_flags, hang_index, table, direction)


def block_matrices(hang_flags, hang_index, block_table):
    count = block_table.shape[0]
    numbers = lax.broadcasted_iota(jnp.int32, (count,) + hang_index.shape, 0)
    one_hot = (hang_index[None] == numbers).astype(jnp.float32)
    table = block_table.astype(jnp.float32).reshape(count, 9)
    chosen = lax.dot_general(
        table, one_hot, (((0,), (0,)), ((), ())), precision=lax.Precision.HIGHEST
    )
    identity = jnp.eye(3, dtype=jnp.float32).reshape(9)[:, None, None]
    blocks = jnp.where(hang_flags[None] != 0, chosen, identity)
    return [[blocks[m * 3 + k] for k in range(3)] for m in range(3)]


def apply_blocks(blocks, field, transpose):
    groups = field.shape[-1] // 3
    slots = [field[..., k * groups:(k + 1) * groups] for k in range(3)]
    mixed = []
    for m in range(3):
        total = None
        for k in range(3):
            weight = blocks[k][m] if transpose else blocks[m][k]
            term = weight * slots[k]
            total = term if total is None else total + term
        mixed.append(total)
    return jnp.concatenate(mixed, axis=-1)


def shifted(padded, spatial, offset):
    lead = padded.ndim - 3
    index = [slice(None)] * lead + [slice(1, -1)] * 3
    if offset == 1:
        index[lead + spatial] = slice(2, None)
    elif offset == -1:
        index[lead + spatial] = slice(None, -2)
    return padded[tuple(index)]


def stencil(padded_vel, padded_visc):
    centre_vel = shifted(padded_vel, 0, 0)
    centre_visc = shifted(padded_visc, 0, 0)
    total = jnp.zeros(centre_vel.shape, jnp.float32)
    for spatial in range(3):
        for offset in (1, -1):
            face = 0.5 * (centre_visc + shifted(padded_visc, spatial, offset))
            total = total + face[None] * (centre_vel - shifted(padded_vel, spatial, offset))
    return total


def laplace(padded):
    return (
        4.0 * padded[1:-1, 1:-1]
        - padded[2:, 1:-1]
        - padded[:-2, 1:-1]
        - padded[1:-1, 2:]
        - padded[1:-1, :-2]
    )


def local(
    velocity,
    adjoint,
    viscosity,
    hang_flags,
    hang_index,
    block_table,
    friction,
    basal_mask,
    direction,
):
    n_x = lax.axis_size("gx")
    n_y = lax.axis_size("gy")
    n_z = lax.axis_size("gz")
    i_x = lax.axis_index("gx")
    i_z = lax.axis_index("gz")
    n_col = n_y * n_z
    i_col = lax.axis_index("gy") * n_z + i_z

    stacked, table9, low_packet, high_packet, y_a, y_b = prologue(
        velocity, viscosity, hang_flags, hang_index, block_table, direction
    )
    blocks = [[table9[m * 3 + k] for k in range(3)] for m in range(3)]
    fields, levels, rows, cols = stacked.shape
    d_rows, d_cols = direction.shape

    even = i_x % 2 == 0
    pairs_a = [(i, i ^ 1) for i in range(n_x - n_x % 2)]
    pairs_b = []
    for k in range(1, n_x - 1, 2):
        pairs_b += [(k, k + 1), (k + 1, k)]
    got_a = lax.ppermute(low_packet, "gx", pairs_a)
    got_b = lax.ppermute(high_packet, "gx", pairs_b)
    from_left = jnp.where(even, got_b, got_a)
    from_right = jnp.where(even, got_a, got_b)
    y_even = lax.axis_index("gy") % 2 == 0
    y_pairs_a = [(i, i ^ 1) for i in range(n_y - n_y % 2)]
    y_pairs_b = []
    for k in range(1, n_y - 1, 2):
        y_pairs_b += [(k, k + 1), (k + 1, k)]
    y_got_a = lax.ppermute(y_a, "gy", y_pairs_a)
    y_got_b = lax.ppermute(y_b, "gy", y_pairs_b)
    y_left = jnp.where(y_even, y_got_b, y_got_a)
    y_right = jnp.where(y_even, y_got_a, y_got_b)
    if n_z == 2:
        sent = lax.dynamic_slice_in_dim(stacked, (1 - i_z) * (levels - 1), 1, axis=1)
        got = lax.ppermute(sent, "gz", [(0, 1), (1, 0)])
        zero = jnp.zeros_like(got)
        z_low = jnp.where(i_z == 1, got, zero)
        z_high = jnp.where(i_z == 0, got, zero)
    else:
        z_low = lax.ppermute(stacked[:, levels - 1:], "gz", shift_pairs(n_z, 1))
        z_high = lax.ppermute(stacked[:, :1], "gz", shift_pairs(n_z, -1))

    x_low = from_left[: fields * levels].reshape(fields, levels, 1, cols)
    x_high = from_right[: fields * levels].reshape(fields, levels, 1, cols)
    d_low = from_left[fields * levels:, :d_cols]
    d_high = from_right[fields * levels:, :d_cols]

    d_ext = jnp.concatenate([d_low, direction, d_high], axis=0)
    padded = jnp.concatenate([y_left, stacked, y_right], axis=3)
    pad_y = ((0, 0), (0, 0), (0, 0), (1, 1))
    padded = jnp.concatenate(
        [jnp.pad(x_low, pad_y), padded, jnp.pad(x_high, pad_y)], axis=2
    )
    pad_xy = ((0, 0), (0, 0), (1, 1), (1, 1))
    padded = jnp.concatenate(
        [jnp.pad(z_low, pad_xy), padded, jnp.pad(z_high, pad_xy)], axis=1
    )
    applied = stencil(padded[:3], padded[3])
    stokes_image = apply_blocks(blocks, applied, True)
    partial_value = jnp.sum(stokes_image * adjoint, axis=(0, 1))

    own_width = cols // n_z
    if n_z == 2:
        sent = lax.dynamic_slice_in_dim(partial_value, (1 - i_z) * own_width, own_width, axis=1)
        mine = lax.dynamic_slice_in_dim(partial_value, i_z * own_width, own_width, axis=1)
        d_partner = lax.dynamic_slice_in_dim(d_ext, (1 - i_z) * (d_cols - 2), 2, axis=1)
        d_across = lax.dynamic_slice_in_dim(d_ext, i_z * (d_cols - 2), 2, axis=1)
        flat = d_partner.reshape(1, -1)
        packet = jnp.concatenate(
            [sent, jnp.pad(flat, ((0, 0), (0, own_width - flat.shape[1])))], axis=0
        )
        packet, d_across = lax.optimization_barrier((packet, d_across))
        got = lax.ppermute(packet, "gz", [(0, 1), (1, 0)])
        across_pairs = []
        for block in range(n_y - 1):
            across_pairs += [(2 * block + 1, 2 * block + 2), (2 * block + 2, 2 * block + 1)]
        got_across = lax.ppermute(d_across, ("gy", "gz"), across_pairs)
        column = mine + got[: sent.shape[0]]
        got_partner = got[sent.shape[0], : flat.shape[1]].reshape(d_partner.shape)
        d_left = jnp.where(i_z == 0, got_across, got_partner)
        d_right = jnp.where(i_z == 0, got_partner, got_across)
    else:
        column = lax.psum_scatter(partial_value, "gz", scatter_dimension=1, tiled=True)
        d_left = lax.ppermute(d_ext[:, d_cols - 2:], ("gy", "gz"), shift_pairs(n_col, 1))
        d_right = lax.ppermute(d_ext[:, :2], ("gy", "gz"), shift_pairs(n_col, -1))

    d_full = jnp.concatenate([d_left, d_ext, d_right], axis=1)
    inner = laplace(d_full)
    row_ids = lax.broadcasted_iota(jnp.int32, inner.shape, 0)
    col_ids = lax.broadcasted_iota(jnp.int32, inner.shape, 1)
    outside = (
        ((row_ids == 0) & (i_x == 0))
        | ((row_ids == inner.shape[0] - 1) & (i_x == n_x - 1))
        | ((col_ids == 0) & (i_col == 0))
        | ((col_ids == inner.shape[1] - 1) & (i_col == n_col - 1))
    )
    inner = jnp.where(outside, 0.0, inner)
    bilaplace = laplace(inner)
    hessian_dir = reg_weight * bilaplace + basal_mask.astype(jnp.float32) * (
        jnp.exp(friction) * column
    )
    return (stokes_image, hessian_dir)


def solution(mesh):
    return jax.shard_map(
        local,
        mesh=mesh,
        in_specs=(
            P(None, "gz", "gx", "gy"),
            P(None, "gz", "gx", "gy"),
            P("gz", "gx", "gy"),
            P("gx", "gy"),
            P("gx", "gy"),
            P(),
            P("gx", ("gy", "gz")),
            P("gx", ("gy", "gz")),
            P("gx", ("gy", "gz")),
        ),
        out_specs=(P(None, "gz", "gx", "gy"), P("gx", ("gy", "gz"))),
        check_vma=False,
    )
```

```python
import jax
import jax.numpy as jnp
from jax import lax
from jax.sharding import PartitionSpec as P
from jax.experimental import pallas as pl
from jax.experimental.pallas import tpu as pltpu


reg_weight = 0.05


def shift_pairs(count, step):
    if step > 0:
        return [(i, i + 1) for i in range(count - 1)]
    return [(i + 1, i) for i in range(count - 1)]


def prologue_kernel(
    vel_hbm, visc_hbm, flags_hbm, index_hbm, table_hbm, dir_hbm,
    stacked_ref, blocks_ref, low_ref, high_ref, level_ref,
    vel_v, visc_v, flags_v, index_v, table_s, dir_v, sems,
):
    pairs = [
        (vel_hbm, vel_v), (visc_hbm, visc_v), (flags_hbm, flags_v),
        (index_hbm, index_v), (table_hbm, table_s), (dir_hbm, dir_v),
    ]
    copies = [pltpu.make_async_copy(s, d, sems.at[i]) for i, (s, d) in enumerate(pairs)]
    for copy in copies:
        copy.start()
    for copy in copies:
        copy.wait()
    index = index_v[...]
    hanging = flags_v[...] != 0
    count = table_s.shape[0] // 9
    blocks = []
    for j in range(9):
        entry = jnp.full(index.shape, table_s[j], jnp.float32)
        for number in range(1, count):
            entry = jnp.where(index == number, table_s[number * 9 + j], entry)
        entry = jnp.where(hanging, entry, 1.0 if j % 4 == 0 else 0.0)
        blocks_ref[j] = entry
        blocks.append(entry)
    groups = index.shape[1]
    fields, levels, rows, cols = stacked_ref.shape
    for c in range(fields - 1):
        for z in range(levels):
            slots = [vel_v[c, z, :, k * groups:(k + 1) * groups] for k in range(3)]
            for m in range(3):
                total = blocks[m * 3] * slots[0]
                total = total + blocks[m * 3 + 1] * slots[1]
                total = total + blocks[m * 3 + 2] * slots[2]
                stacked_ref[c, z, :, m * groups:(m + 1) * groups] = total
    stacked_ref[fields - 1] = visc_v[...]
    for f in range(fields):
        for z in range(levels):
            row = f * levels + z
            low_ref[row:row + 1, :] = stacked_ref[f, z, 0:1, :]
            high_ref[row:row + 1, :] = stacked_ref[f, z, rows - 1:rows, :]
    d_rows, d_cols = dir_v.shape
    edge = fields * levels
    low_ref[edge:, :] = jnp.zeros((2, cols), jnp.float32)
    high_ref[edge:, :] = jnp.zeros((2, cols), jnp.float32)
    low_ref[edge:, 0:d_cols] = dir_v[0:2, :]
    high_ref[edge:, 0:d_cols] = dir_v[d_rows - 2:, :]
    if lax.axis_size("gz") == 2:
        level = (1 - lax.axis_index("gz")) * (levels - 1)
        level_ref[...] = stacked_ref[:, pl.ds(level, 1)]
    else:
        level_ref[...] = stacked_ref[:, 0:1]
    low = low_ref[...]
    high = high_ref[...]
    even = lax.axis_index("gx") % 2 == 0
    low_ref[...] = jnp.where(even, high, low)
    high_ref[...] = jnp.where(even, low, high)


def prologue(velocity, viscosity, hang_flags, hang_index, block_table, direction):
    fields = velocity.shape[0] + 1
    stack_shape = (fields,) + viscosity.shape
    packet = (fields * viscosity.shape[0] + 2, viscosity.shape[2])
    table = block_table.astype(jnp.float32).reshape(-1)
    f32 = jnp.float32
    anywhere = pl.BlockSpec(memory_space=pl.ANY)
    in_vmem = pl.BlockSpec(memory_space=pltpu.VMEM)
    return pl.pallas_call(
        prologue_kernel,
        out_shape=(
            jax.ShapeDtypeStruct(stack_shape, f32),
            jax.ShapeDtypeStruct((9,) + hang_index.shape, f32),
            jax.ShapeDtypeStruct(packet, f32),
            jax.ShapeDtypeStruct(packet, f32),
            jax.ShapeDtypeStruct((fields, 1) + viscosity.shape[1:], f32),
        ),
        in_specs=[anywhere] * 6,
        out_specs=(in_vmem,) * 5,
        scratch_shapes=[
            pltpu.VMEM(velocity.shape, f32),
            pltpu.VMEM(viscosity.shape, f32),
            pltpu.VMEM(hang_flags.shape, jnp.int32),
            pltpu.VMEM(hang_index.shape, jnp.int32),
            pltpu.SMEM(table.shape, f32),
            pltpu.VMEM(direction.shape, f32),
            pltpu.SemaphoreType.DMA((6,)),
        ],
        cost_estimate=pl.CostEstimate(
            flops=200000, transcendentals=0, bytes_accessed=300000
        ),
    )(velocity, viscosity, hang_flags, hang_index, table, direction)


def block_matrices(hang_flags, hang_index, block_table):
    count = block_table.shape[0]
    numbers = lax.broadcasted_iota(jnp.int32, (count,) + hang_index.shape, 0)
    one_hot = (hang_index[None] == numbers).astype(jnp.float32)
    table = block_table.astype(jnp.float32).reshape(count, 9)
    chosen = lax.dot_general(
        table, one_hot, (((0,), (0,)), ((), ())), precision=lax.Precision.HIGHEST
    )
    identity = jnp.eye(3, dtype=jnp.float32).reshape(9)[:, None, None]
    blocks = jnp.where(hang_flags[None] != 0, chosen, identity)
    return [[blocks[m * 3 + k] for k in range(3)] for m in range(3)]


def apply_blocks(blocks, field, transpose):
    groups = field.shape[-1] // 3
    slots = [field[..., k * groups:(k + 1) * groups] for k in range(3)]
    mixed = []
    for m in range(3):
        total = None
        for k in range(3):
            weight = blocks[k][m] if transpose else blocks[m][k]
            term = weight * slots[k]
            total = term if total is None else total + term
        mixed.append(total)
    return jnp.concatenate(mixed, axis=-1)


def shifted(padded, spatial, offset):
    lead = padded.ndim - 3
    index = [slice(None)] * lead + [slice(1, -1)] * 3
    if offset == 1:
        index[lead + spatial] = slice(2, None)
    elif offset == -1:
        index[lead + spatial] = slice(None, -2)
    return padded[tuple(index)]


def stencil(padded_vel, padded_visc):
    centre_vel = shifted(padded_vel, 0, 0)
    centre_visc = shifted(padded_visc, 0, 0)
    total = jnp.zeros(centre_vel.shape, jnp.float32)
    for spatial in range(3):
        for offset in (1, -1):
            face = 0.5 * (centre_visc + shifted(padded_visc, spatial, offset))
            total = total + face[None] * (centre_vel - shifted(padded_vel, spatial, offset))
    return total


def laplace(padded):
    return (
        4.0 * padded[1:-1, 1:-1]
        - padded[2:, 1:-1]
        - padded[:-2, 1:-1]
        - padded[1:-1, 2:]
        - padded[1:-1, :-2]
    )


def local(
    velocity,
    adjoint,
    viscosity,
    hang_flags,
    hang_index,
    block_table,
    friction,
    basal_mask,
    direction,
):
    n_x = lax.axis_size("gx")
    n_y = lax.axis_size("gy")
    n_z = lax.axis_size("gz")
    i_x = lax.axis_index("gx")
    i_z = lax.axis_index("gz")
    n_col = n_y * n_z
    i_col = lax.axis_index("gy") * n_z + i_z

    stacked, table9, low_packet, high_packet, z_sent = prologue(
        velocity, viscosity, hang_flags, hang_index, block_table, direction
    )
    blocks = [[table9[m * 3 + k] for k in range(3)] for m in range(3)]
    fields, levels, rows, cols = stacked.shape
    d_rows, d_cols = direction.shape

    even = i_x % 2 == 0
    pairs_a = [(i, i ^ 1) for i in range(n_x - n_x % 2)]
    pairs_b = []
    for k in range(1, n_x - 1, 2):
        pairs_b += [(k, k + 1), (k + 1, k)]
    got_a = lax.ppermute(low_packet, "gx", pairs_a)
    got_b = lax.ppermute(high_packet, "gx", pairs_b)
    from_left = jnp.where(even, got_b, got_a)
    from_right = jnp.where(even, got_a, got_b)
    y_left = lax.ppermute(stacked[:, :, :, cols - 1:], "gy", shift_pairs(n_y, 1))
    y_right = lax.ppermute(stacked[:, :, :, :1], "gy", shift_pairs(n_y, -1))
    if n_z == 2:
        got = lax.ppermute(z_sent, "gz", [(0, 1), (1, 0)])
        zero = jnp.zeros_like(got)
        z_low = jnp.where(i_z == 1, got, zero)
        z_high = jnp.where(i_z == 0, got, zero)
    else:
        z_low = lax.ppermute(stacked[:, levels - 1:], "gz", shift_pairs(n_z, 1))
        z_high = lax.ppermute(stacked[:, :1], "gz", shift_pairs(n_z, -1))

    x_low = from_left[: fields * levels].reshape(fields, levels, 1, cols)
    x_high = from_right[: fields * levels].reshape(fields, levels, 1, cols)
    d_low = from_left[fields * levels:, :d_cols]
    d_high = from_right[fields * levels:, :d_cols]

    d_ext = jnp.concatenate([d_low, direction, d_high], axis=0)
    padded = jnp.concatenate([y_left, stacked, y_right], axis=3)
    pad_y = ((0, 0), (0, 0), (0, 0), (1, 1))
    padded = jnp.concatenate(
        [jnp.pad(x_low, pad_y), padded, jnp.pad(x_high, pad_y)], axis=2
    )
    pad_xy = ((0, 0), (0, 0), (1, 1), (1, 1))
    padded = jnp.concatenate(
        [jnp.pad(z_low, pad_xy), padded, jnp.pad(z_high, pad_xy)], axis=1
    )
    applied = stencil(padded[:3], padded[3])
    stokes_image = apply_blocks(blocks, applied, True)
    partial_value = jnp.sum(stokes_image * adjoint, axis=(0, 1))

    own_width = cols // n_z
    if n_z == 2:
        sent = lax.dynamic_slice_in_dim(partial_value, (1 - i_z) * own_width, own_width, axis=1)
        mine = lax.dynamic_slice_in_dim(partial_value, i_z * own_width, own_width, axis=1)
        d_partner = lax.dynamic_slice_in_dim(d_ext, (1 - i_z) * (d_cols - 2), 2, axis=1)
        d_across = lax.dynamic_slice_in_dim(d_ext, i_z * (d_cols - 2), 2, axis=1)
        flat = d_partner.reshape(1, -1)
        packet = jnp.concatenate(
            [sent, jnp.pad(flat, ((0, 0), (0, own_width - flat.shape[1])))], axis=0
        )
        packet, d_across = lax.optimization_barrier((packet, d_across))
        got = lax.ppermute(packet, "gz", [(0, 1), (1, 0)])
        across_pairs = []
        for block in range(n_y - 1):
            across_pairs += [(2 * block + 1, 2 * block + 2), (2 * block + 2, 2 * block + 1)]
        got_across = lax.ppermute(d_across, ("gy", "gz"), across_pairs)
        column = mine + got[: sent.shape[0]]
        got_partner = got[sent.shape[0], : flat.shape[1]].reshape(d_partner.shape)
        d_left = jnp.where(i_z == 0, got_across, got_partner)
        d_right = jnp.where(i_z == 0, got_partner, got_across)
    else:
        column = lax.psum_scatter(partial_value, "gz", scatter_dimension=1, tiled=True)
        d_left = lax.ppermute(d_ext[:, d_cols - 2:], ("gy", "gz"), shift_pairs(n_col, 1))
        d_right = lax.ppermute(d_ext[:, :2], ("gy", "gz"), shift_pairs(n_col, -1))

    d_full = jnp.concatenate([d_left, d_ext, d_right], axis=1)
    inner = laplace(d_full)
    row_ids = lax.broadcasted_iota(jnp.int32, inner.shape, 0)
    col_ids = lax.broadcasted_iota(jnp.int32, inner.shape, 1)
    outside = (
        ((row_ids == 0) & (i_x == 0))
        | ((row_ids == inner.shape[0] - 1) & (i_x == n_x - 1))
        | ((col_ids == 0) & (i_col == 0))
        | ((col_ids == inner.shape[1] - 1) & (i_col == n_col - 1))
    )
    inner = jnp.where(outside, 0.0, inner)
    bilaplace = laplace(inner)
    hessian_dir = reg_weight * bilaplace + basal_mask.astype(jnp.float32) * (
        jnp.exp(friction) * column
    )
    return (stokes_image, hessian_dir)


def solution(mesh):
    return jax.shard_map(
        local,
        mesh=mesh,
        in_specs=(
            P(None, "gz", "gx", "gy"),
            P(None, "gz", "gx", "gy"),
            P("gz", "gx", "gy"),
            P("gx", "gy"),
            P("gx", "gy"),
            P(),
            P("gx", ("gy", "gz")),
            P("gx", ("gy", "gz")),
            P("gx", ("gy", "gz")),
        ),
        out_specs=(P(None, "gz", "gx", "gy"), P("gx", ("gy", "gz"))),
        check_vma=False,
    )
```
